32 devices in a mesh: beam: 2 (over y), band: 16 (over z, x, core).
Axes of the slice: x: 2, y: 2, z: 4, core: 2. Of those that a mesh axis runs over, the one named last changes fastest.
Arguments:
- filterbank: float32 [1024, 6144], P(('beam', 'band')), parts along dimension 0, may hold values from -40 to 40
- offsets: int32 [9, 512], P(None, 'band'), may hold values from 0 to 255, as said below
- widths: int32 [8], replicated, may hold values from 1 to 128, as said below
Outputs:
- detection: float32 [1024, 2048], P(('beam', 'band')), parts along dimension 0
- peak_series: float32 [4096], P('beam'), parts along dimension 0
The draws below stay inside these ranges and needn't reach their ends.
There are 2 independent parts, one for each index of `beam`. The reference program is written for one: setup_inputs(seed, part) draws one part's arguments, and reference() takes and returns one part's arrays. A program takes and returns all parts, laid end to end along the dimension named above; an argument that names none is the same for every part. Nothing has to cross between parts.
Inputs may be any that keep to these rules, and one draw needn't show every extreme that they name: `offsets`: in every section some offset equals 255. Among the 8 widths are 1 and 128.
All inputs are finite; a program needn't handle non-finite values.
Results may differ from the reference program's by a relative error of at most 0.0002.
Values sent between devices are 32-bit elements; how exact they have to be, the bound alone decides.
No kernel may reach another device: no remote copies, remote signals or barrier semaphores. Data moves between devices by JAX's collectives and lax.ppermute only.
A program may use at most 64 MiB of HBM per device.

```python
import math
import jax
import jax.numpy as jnp
from jax import lax

LEVELS = 9
CHANNELS = 512
TS = 2048
TIN = 6144
SHIFT = 256
TAPS = 128
TEMPLATES = 8


def draw_filterbank(key, part):
    noise_key, channel_key, time_key = jax.random.split(key, 3)
    channel_pos = jnp.arange(CHANNELS, dtype=jnp.float32) / CHANNELS
    channel_gain = (1.0 + 2.0 * channel_pos) * jnp.exp(jax.random.uniform(channel_key, (CHANNELS,), jnp.float32, -math.log(3.3), 0.0))
    time_gain = jnp.exp(jax.random.uniform(time_key, (TIN,), jnp.float32, -math.log(3.0), math.log(3.0)))
    scales = channel_gain[:, None] * time_gain[None, :]
    noise_part = jnp.clip(jax.random.normal(noise_key, (CHANNELS, TIN), jnp.float32), -4.0, 4.0)
    return noise_part * scales


def draw_offsets(key, part):
    value_key, column_key = jax.random.split(key)
    delay_table = jax.random.randint(value_key, (LEVELS, CHANNELS), 0, SHIFT, jnp.int32)
    columns = jax.random.randint(column_key, (LEVELS,), 0, CHANNELS, jnp.int32)
    return delay_table.at[jnp.arange(LEVELS), columns].set(SHIFT - 1)


def draw_widths(key, part):
    value_key, placing_key = jax.random.split(key)
    chosen = jax.random.randint(value_key, (TEMPLATES,), 2, TAPS, jnp.int32)
    placing = jax.random.permutation(placing_key, TEMPLATES)
    return chosen.at[placing[0]].set(TAPS).at[placing[1]].set(1)


def setup_inputs(seed: int = 0, part: int = 0) -> dict:
    key_list = jax.random.split(jax.random.key(seed), 4)
    own_keys = jax.random.split(jax.random.fold_in(key_list[3], part), 4)
    filterbank = draw_filterbank(jax.random.fold_in(jax.random.fold_in(key_list[3], part), 71), part)
    offsets = draw_offsets(jax.random.fold_in(key_list[3], 71), part)
    widths = draw_widths(jax.random.fold_in(key_list[3], 71), part)
    return dict(filterbank=filterbank, offsets=offsets, widths=widths)


def shift_rows(trial_rows, amounts, length):
    padded = jnp.pad(trial_rows, ((0, 0), (0, SHIFT)))

    def take_one(single_row, amount):
        return lax.dynamic_slice_in_dim(single_row, amount, length)
    return jax.vmap(take_one)(padded, amounts)

def merge_section(current, offsets_now, section_index, new_length):
    group_trials = 2 ** section_index
    total_rows = current.shape[0]
    groups = total_rows // (2 * group_trials)
    blocks = current.reshape(groups, 2, group_trials, current.shape[1])
    lower_part = blocks[:, 0, :, :new_length]
    upper_flat = blocks[:, 1].reshape(groups * group_trials, current.shape[1])
    amounts = offsets_now.reshape(groups, 2, group_trials)
    first_half = lower_part + shift_rows(upper_flat, amounts[:, 0].reshape(-1), new_length).reshape(groups, group_trials, new_length)
    second_half = lower_part + shift_rows(upper_flat, amounts[:, 1].reshape(-1), new_length).reshape(groups, group_trials, new_length)
    return jnp.stack([first_half, second_half], axis=1).reshape(total_rows, new_length)

def template_tables(widths):
    source = lax.broadcasted_iota(jnp.int32, (2 * TAPS, TAPS), 0)
    target = lax.broadcasted_iota(jnp.int32, (2 * TAPS, TAPS), 1)
    tap_offset = source - target
    inside = (tap_offset[None] >= 0) & (tap_offset[None] < widths[:, None, None])
    tap_scale = 1.0 / jnp.sqrt(widths.astype(jnp.float32))
    return jnp.where(inside, tap_scale[:, None, None], jnp.zeros((), jnp.float32))

def boxcar_max(dedispersed, widths):
    total_rows = dedispersed.shape[0]
    blocks_time = TS // TAPS
    window = dedispersed[:, :TS + TAPS].reshape(total_rows, blocks_time + 1, TAPS)
    paired = jnp.concatenate([window[:, :-1], window[:, 1:]], axis=2).reshape(total_rows * blocks_time, 2 * TAPS)
    tables = template_tables(widths)
    best_value = None
    for template_index in range(TEMPLATES):
        result = jnp.dot(paired, tables[template_index], precision=lax.Precision.HIGHEST, preferred_element_type=jnp.float32)
        if template_index == 0:
            best_value = result
        else:
            best_value = jnp.maximum(best_value, result)
    return best_value.reshape(total_rows, TS)

def reference(filterbank, offsets, widths):
    channel_mean = lax.optimization_barrier(jnp.sum(filterbank, axis=0)) / CHANNELS
    current = filterbank - channel_mean[None, :]
    for section_index in range(LEVELS):
        current = merge_section(current, offsets[section_index], section_index, TIN)
    dedispersed = current * (1.0 / math.sqrt(CHANNELS))
    detection = boxcar_max(dedispersed, widths)
    peak_series = lax.optimization_barrier(jnp.max(detection, axis=0))
    return (detection, peak_series)
```

```python
import math

import jax
import jax.numpy as jnp
from jax import lax
from jax.sharding import PartitionSpec as P

TS = 2048
TIN = 6144
SHIFT = 256
TAPS = 128
TEMPLATES = 8


def from_partner(value, axis, distance):
    mask = 2**distance
    pairs = [(source, source ^ mask) for source in range(lax.axis_size(axis))]
    return lax.ppermute(value, axis, pairs)


def butterfly(value, axis, combine):
    for bit_index in range(lax.axis_size(axis).bit_length() - 1):
        value = combine(value, from_partner(value, axis, bit_index))
    return value


def shift_rows(trial_rows, amounts, length):
    current = jnp.pad(trial_rows, ((0, 0), (0, 2 * SHIFT)))
    top_bit = (SHIFT - 1).bit_length()
    for bit_index in reversed(range(top_bit)):
        span = 2**bit_index
        keep_len = length + span - 1
        chosen = (amounts >> bit_index & 1)[:, None] == 1
        current = jnp.where(chosen, current[:, span : span + keep_len], current[:, :keep_len])
    return current


def merge_section(current, offsets_now, section_index, new_length):
    group_trials = 2**section_index
    total_rows = current.shape[0]
    groups = total_rows // (2 * group_trials)
    blocks = current.reshape(groups, 2, group_trials, current.shape[1])
    lower_part = blocks[:, 0, :, :new_length]
    upper_flat = blocks[:, 1].reshape(groups * group_trials, current.shape[1])
    amounts = offsets_now.reshape(groups, 2, group_trials)
    first_half = lower_part + shift_rows(upper_flat, amounts[:, 0].reshape(-1), new_length).reshape(
        groups, group_trials, new_length
    )
    second_half = lower_part + shift_rows(
        upper_flat, amounts[:, 1].reshape(-1), new_length
    ).reshape(groups, group_trials, new_length)
    return jnp.stack([first_half, second_half], axis=1).reshape(total_rows, new_length)


def template_tables(widths):
    source = lax.broadcasted_iota(jnp.int32, (2 * TAPS, TAPS), 0)
    target = lax.broadcasted_iota(jnp.int32, (2 * TAPS, TAPS), 1)
    tap_offset = source - target
    inside = (tap_offset[None] >= 0) & (tap_offset[None] < widths[:, None, None])
    tap_scale = 1.0 / jnp.sqrt(widths.astype(jnp.float32))
    return jnp.where(inside, tap_scale[:, None, None], jnp.zeros((), jnp.float32))


def boxcar_max(dedispersed, widths):
    total_rows = dedispersed.shape[0]
    blocks_time = TS // TAPS
    window = dedispersed.reshape(total_rows, blocks_time + 1, TAPS)
    paired = jnp.concatenate([window[:, :-1], window[:, 1:]], axis=2).reshape(
        total_rows * blocks_time, 2 * TAPS
    )
    tables = template_tables(widths)
    best_value = None
    for template_index in range(TEMPLATES):
        result = jnp.dot(
            paired,
            tables[template_index],
            precision=lax.Precision.HIGHEST,
            preferred_element_type=jnp.float32,
        )
        if template_index == 0:
            best_value = result
        else:
            best_value = jnp.maximum(best_value, result)
    return best_value.reshape(total_rows, TS)


def per_device(filterbank, offsets, widths):
    levels = offsets.shape[0]
    local_count = filterbank.shape[0].bit_length() - 1
    band_count = lax.axis_size("band")
    channels_all = filterbank.shape[0] * band_count

    def length_after(sections_done):
        needed = TS + TAPS + (levels - sections_done) * (SHIFT - 1)
        needed = -(-needed // 128) * 128
        return min(TIN, needed)

    partial_value = jnp.sum(filterbank, axis=0)
    channel_mean = butterfly(partial_value, "band", jnp.add) / channels_all
    current = filterbank - channel_mean[None, :]
    for local_section_index in range(local_count):
        current = merge_section(
            current,
            offsets[local_section_index],
            local_section_index,
            length_after(local_section_index + 1),
        )
    band_index = lax.axis_index("band")
    for bit_index in range(band_count.bit_length() - 1):
        section_index = local_count + bit_index
        new_length = length_after(section_index + 1)
        partner = from_partner(current, "band", bit_index)
        upper_half = band_index // 2**bit_index % 2 == 1
        lower_part = jnp.where(upper_half, partner, current)
        upper_part = jnp.where(upper_half, current, partner)
        current = lower_part[:, :new_length] + shift_rows(
            upper_part, offsets[section_index], new_length
        )
    dedispersed = current * (1.0 / math.sqrt(channels_all))
    detection = boxcar_max(dedispersed, widths)
    peak_series = butterfly(jnp.max(detection, axis=0), "band", jnp.maximum)
    return (detection, peak_series)


def solution(mesh):
    placed = (P(("beam", "band"), None), P(None, "band"), P())
    return jax.shard_map(
        per_device,
        mesh=mesh,
        in_specs=placed,
        out_specs=(P(("beam", "band"), None), P("beam")),
        check_vma=False,
    )
```

```python
import math

import jax
import jax.numpy as jnp
from jax import lax
from jax.sharding import PartitionSpec as P

TS = 2048
TIN = 6144
SHIFT = 256
TAPS = 128
TEMPLATES = 8


def from_partner(value, axis, distance):
    mask = 2**distance
    pairs = [(source, source ^ mask) for source in range(lax.axis_size(axis))]
    return lax.ppermute(value, axis, pairs)


def from_xor(value, axis, mask):
    pairs = [(source, source ^ mask) for source in range(lax.axis_size(axis))]
    return lax.ppermute(value, axis, pairs)


def butterfly(value, axis, combine):
    bit_count = lax.axis_size(axis).bit_length() - 1
    position = lax.axis_index(axis)
    low_bit = 0
    while low_bit < bit_count:
        width = min(2, bit_count - low_bit)
        group = 2**width
        received = [value] + [from_xor(value, axis, k << low_bit) for k in range(1, group)]
        mine = position >> low_bit & (group - 1)
        ordered = []
        for slot in range(group):
            chosen = received[0]
            for k in range(1, group):
                chosen = jnp.where((mine ^ slot) == k, received[k], chosen)
            ordered.append(chosen)
        while len(ordered) > 1:
            ordered = [combine(ordered[i], ordered[i + 1]) for i in range(0, len(ordered), 2)]
        value = ordered[0]
        low_bit += width
    return value


def shift_rows(trial_rows, amounts, length):
    current = jnp.pad(trial_rows, ((0, 0), (0, 2 * SHIFT)))
    top_bit = (SHIFT - 1).bit_length()
    for bit_index in reversed(range(top_bit)):
        span = 2**bit_index
        keep_len = length + span - 1
        chosen = (amounts >> bit_index & 1)[:, None] == 1
        current = jnp.where(chosen, current[:, span : span + keep_len], current[:, :keep_len])
    return current


def merge_section(current, offsets_now, section_index, new_length):
    group_trials = 2**section_index
    total_rows = current.shape[0]
    groups = total_rows // (2 * group_trials)
    blocks = current.reshape(groups, 2, group_trials, current.shape[1])
    lower_part = blocks[:, 0, :, :new_length]
    upper_flat = blocks[:, 1].reshape(groups * group_trials, current.shape[1])
    amounts = offsets_now.reshape(groups, 2, group_trials)
    first_half = lower_part + shift_rows(upper_flat, amounts[:, 0].reshape(-1), new_length).reshape(
        groups, group_trials, new_length
    )
    second_half = lower_part + shift_rows(
        upper_flat, amounts[:, 1].reshape(-1), new_length
    ).reshape(groups, group_trials, new_length)
    return jnp.stack([first_half, second_half], axis=1).reshape(total_rows, new_length)


def template_tables(widths):
    source = lax.broadcasted_iota(jnp.int32, (2 * TAPS, TAPS), 0)
    target = lax.broadcasted_iota(jnp.int32, (2 * TAPS, TAPS), 1)
    tap_offset = source - target
    inside = (tap_offset[None] >= 0) & (tap_offset[None] < widths[:, None, None])
    tap_scale = 1.0 / jnp.sqrt(widths.astype(jnp.float32))
    return jnp.where(inside, tap_scale[:, None, None], jnp.zeros((), jnp.float32))


def boxcar_max(dedispersed, widths):
    total_rows = dedispersed.shape[0]
    blocks_time = TS // TAPS
    window = dedispersed.reshape(total_rows, blocks_time + 1, TAPS)
    paired = jnp.concatenate([window[:, :-1], window[:, 1:]], axis=2).reshape(
        total_rows * blocks_time, 2 * TAPS
    )
    tables = template_tables(widths)
    best_value = None
    for template_index in range(TEMPLATES):
        result = jnp.dot(
            paired,
            tables[template_index],
            precision=lax.Precision.HIGHEST,
            preferred_element_type=jnp.float32,
        )
        if template_index == 0:
            best_value = result
        else:
            best_value = jnp.maximum(best_value, result)
    return best_value.reshape(total_rows, TS)


def per_device(filterbank, offsets, widths):
    levels = offsets.shape[0]
    local_count = filterbank.shape[0].bit_length() - 1
    band_count = lax.axis_size("band")
    channels_all = filterbank.shape[0] * band_count

    def length_after(sections_done):
        needed = TS + TAPS + (levels - sections_done) * (SHIFT - 1)
        needed = -(-needed // 128) * 128
        return min(TIN, needed)

    partial_value = jnp.sum(filterbank, axis=0)
    channel_mean = butterfly(partial_value, "band", jnp.add) / channels_all
    current = filterbank - channel_mean[None, :]
    for local_section_index in range(local_count):
        current = merge_section(
            current,
            offsets[local_section_index],
            local_section_index,
            length_after(local_section_index + 1),
        )
    band_index = lax.axis_index("band")
    for bit_index in range(band_count.bit_length() - 1):
        section_index = local_count + bit_index
        new_length = length_after(section_index + 1)
        partner = from_partner(current, "band", bit_index)
        upper_half = band_index // 2**bit_index % 2 == 1
        lower_part = jnp.where(upper_half, partner, current)
        upper_part = jnp.where(upper_half, current, partner)
        current = lower_part[:, :new_length] + shift_rows(
            upper_part, offsets[section_index], new_length
        )
    dedispersed = current * (1.0 / math.sqrt(channels_all))
    detection = boxcar_max(dedispersed, widths)
    peak_series = butterfly(jnp.max(detection, axis=0), "band", jnp.maximum)
    return (detection, peak_series)


def solution(mesh):
    placed = (P(("beam", "band"), None), P(None, "band"), P())
    return jax.shard_map(
        per_device,
        mesh=mesh,
        in_specs=placed,
        out_specs=(P(("beam", "band"), None), P("beam")),
        check_vma=False,
    )
```

```python
import math

import jax
import jax.numpy as jnp
from jax import lax
from jax.sharding import PartitionSpec as P

TS = 2048
TIN = 6144
SHIFT = 256
TAPS = 128
TEMPLATES = 8


def from_partner(value, axis, distance):
    mask = 2**distance
    pairs = [(source, source ^ mask) for source in range(lax.axis_size(axis))]
    return lax.ppermute(value, axis, pairs)


def from_xor(value, axis, mask):
    pairs = [(source, source ^ mask) for source in range(lax.axis_size(axis))]
    return lax.ppermute(value, axis, pairs)


def butterfly(value, axis, combine):
    bit_count = lax.axis_size(axis).bit_length() - 1
    position = lax.axis_index(axis)
    low_bit = 0
    while low_bit < bit_count:
        width = min(2, bit_count - low_bit)
        group = 2**width
        received = [value] + [from_xor(value, axis, k << low_bit) for k in range(1, group)]
        mine = position >> low_bit & (group - 1)
        ordered = []
        for slot in range(group):
            chosen = received[0]
            for k in range(1, group):
                chosen = jnp.where((mine ^ slot) == k, received[k], chosen)
            ordered.append(chosen)
        while len(ordered) > 1:
            ordered = [combine(ordered[i], ordered[i + 1]) for i in range(0, len(ordered), 2)]
        value = ordered[0]
        low_bit += width
    return value


def shift_rows(trial_rows, amounts, length):
    current = jnp.pad(trial_rows, ((0, 0), (0, 2 * SHIFT)))
    top_bit = (SHIFT - 1).bit_length()
    for bit_index in reversed(range(top_bit)):
        span = 2**bit_index
        keep_len = length + span - 1
        chosen = (amounts >> bit_index & 1)[:, None] == 1
        current = jnp.where(chosen, current[:, span : span + keep_len], current[:, :keep_len])
    return current


def merge_section(current, offsets_now, section_index, new_length):
    group_trials = 2**section_index
    total_rows = current.shape[0]
    groups = total_rows // (2 * group_trials)
    blocks = current.reshape(groups, 2, group_trials, current.shape[1])
    lower_part = blocks[:, 0, :, :new_length]
    upper_flat = blocks[:, 1].reshape(groups * group_trials, current.shape[1])
    amounts = offsets_now.reshape(groups, 2, group_trials)
    first_half = lower_part + shift_rows(upper_flat, amounts[:, 0].reshape(-1), new_length).reshape(
        groups, group_trials, new_length
    )
    second_half = lower_part + shift_rows(
        upper_flat, amounts[:, 1].reshape(-1), new_length
    ).reshape(groups, group_trials, new_length)
    return jnp.stack([first_half, second_half], axis=1).reshape(total_rows, new_length)


def template_tables(widths):
    source = lax.broadcasted_iota(jnp.int32, (2 * TAPS, TAPS), 0)
    target = lax.broadcasted_iota(jnp.int32, (2 * TAPS, TAPS), 1)
    tap_offset = source - target
    inside = (tap_offset[None] >= 0) & (tap_offset[None] < widths[:, None, None])
    tap_scale = 1.0 / jnp.sqrt(widths.astype(jnp.float32))
    return jnp.where(inside, tap_scale[:, None, None], jnp.zeros((), jnp.float32))


def boxcar_max(dedispersed, widths):
    total_rows = dedispersed.shape[0]
    blocks_time = TS // TAPS
    window = dedispersed.reshape(total_rows, blocks_time + 1, TAPS)
    paired = jnp.concatenate([window[:, :-1], window[:, 1:]], axis=2).reshape(
        total_rows * blocks_time, 2 * TAPS
    )
    tables = template_tables(widths)
    joined = jnp.transpose(tables, (1, 0, 2)).reshape(2 * TAPS, TEMPLATES * TAPS)
    result = jnp.dot(
        paired,
        joined,
        precision=lax.Precision.HIGHEST,
        preferred_element_type=jnp.float32,
    )
    best_value = jnp.max(result.reshape(total_rows * blocks_time, TEMPLATES, TAPS), axis=1)
    return best_value.reshape(total_rows, TS)


def per_device(filterbank, offsets, widths):
    levels = offsets.shape[0]
    local_count = filterbank.shape[0].bit_length() - 1
    band_count = lax.axis_size("band")
    channels_all = filterbank.shape[0] * band_count

    def length_after(sections_done):
        needed = TS + TAPS + (levels - sections_done) * (SHIFT - 1)
        needed = -(-needed // 128) * 128
        return min(TIN, needed)

    partial_value = jnp.sum(filterbank, axis=0)
    channel_mean = butterfly(partial_value, "band", jnp.add) / channels_all
    current = filterbank - channel_mean[None, :]
    for local_section_index in range(local_count):
        current = merge_section(
            current,
            offsets[local_section_index],
            local_section_index,
            length_after(local_section_index + 1),
        )
    band_index = lax.axis_index("band")
    for bit_index in range(band_count.bit_length() - 1):
        section_index = local_count + bit_index
        new_length = length_after(section_index + 1)
        partner = from_partner(current, "band", bit_index)
        upper_half = band_index // 2**bit_index % 2 == 1
        lower_part = jnp.where(upper_half, partner, current)
        upper_part = jnp.where(upper_half, current, partner)
        current = lower_part[:, :new_length] + shift_rows(
            upper_part, offsets[section_index], new_length
        )
    dedispersed = current * (1.0 / math.sqrt(channels_all))
    detection = boxcar_max(dedispersed, widths)
    peak_series = butterfly(jnp.max(detection, axis=0), "band", jnp.maximum)
    return (detection, peak_series)


def solution(mesh):
    placed = (P(("beam", "band"), None), P(None, "band"), P())
    return jax.shard_map(
        per_device,
        mesh=mesh,
        in_specs=placed,
        out_specs=(P(("beam", "band"), None), P("beam")),
        check_vma=False,
    )
```

```python
import functools
import math

import jax
import jax.numpy as jnp
from jax import lax
from jax.experimental import pallas as pl
from jax.experimental.pallas import tpu as pltpu
from jax.sharding import PartitionSpec as P

TS = 2048
TIN = 6144
SHIFT = 256
TAPS = 128
TEMPLATES = 8


def from_partner(value, axis, distance):
    mask = 2**distance
    pairs = [(source, source ^ mask) for source in range(lax.axis_size(axis))]
    return lax.ppermute(value, axis, pairs)


def from_xor(value, axis, mask):
    pairs = [(source, source ^ mask) for source in range(lax.axis_size(axis))]
    return lax.ppermute(value, axis, pairs)


def butterfly(value, axis, combine):
    bit_count = lax.axis_size(axis).bit_length() - 1
    position = lax.axis_index(axis)
    low_bit = 0
    while low_bit < bit_count:
        width = min(2, bit_count - low_bit)
        group = 2**width
        received = [value] + [from_xor(value, axis, k << low_bit) for k in range(1, group)]
        mine = position >> low_bit & (group - 1)
        ordered = []
        for slot in range(group):
            chosen = received[0]
            for k in range(1, group):
                chosen = jnp.where((mine ^ slot) == k, received[k], chosen)
            ordered.append(chosen)
        while len(ordered) > 1:
            ordered = [combine(ordered[i], ordered[i + 1]) for i in range(0, len(ordered), 2)]
        value = ordered[0]
        low_bit += width
    return value


def shift_rows(trial_rows, amounts, length):
    current = jnp.pad(trial_rows, ((0, 0), (0, 2 * SHIFT)))
    top_bit = (SHIFT - 1).bit_length()
    for bit_index in reversed(range(top_bit)):
        span = 2**bit_index
        keep_len = length + span - 1
        chosen = (amounts >> bit_index & 1)[:, None] == 1
        current = jnp.where(chosen, current[:, span : span + keep_len], current[:, :keep_len])
    return current


def local_tree_kernel(widths_seq, x_ref, mean_ref, amount_ref, out_ref):
    rows = x_ref.shape[0]
    cur = x_ref[:, : widths_seq[0]] - mean_ref[:, : widths_seq[0]]
    row_id = lax.broadcasted_iota(jnp.int32, (rows, 1), 0)
    for section_index in range(len(widths_seq) - 1):
        mask = 2**section_index
        width = widths_seq[section_index]
        new_width = widths_seq[section_index + 1]
        is_upper = (row_id & mask) != 0
        from_below = pltpu.roll(cur, rows - mask, axis=0)
        from_above = pltpu.roll(cur, mask, axis=0)
        partner = jnp.where(is_upper, from_above, from_below)
        lower = jnp.where(is_upper, partner, cur)
        shifted = jnp.where(is_upper, cur, partner)
        amount = amount_ref[section_index][:, 0:1]
        for bit_index in range((SHIFT - 1).bit_length()):
            span = 2**bit_index
            chosen = (amount >> bit_index & 1) == 1
            shifted = jnp.where(chosen, pltpu.roll(shifted, width - span, axis=1), shifted)
        cur = lower[:, :new_width] + shifted[:, :new_width]
    out_ref[...] = cur


def local_tree(filterbank, channel_mean, amounts, widths_seq):
    rows = filterbank.shape[0]
    vmem = pl.BlockSpec(memory_space=pltpu.VMEM)
    lane_amounts = jnp.broadcast_to(amounts[:, :, None], amounts.shape + (128,))
    levels = len(widths_seq) - 1
    work = rows * sum(widths_seq[:-1])
    return pl.pallas_call(
        functools.partial(local_tree_kernel, tuple(widths_seq)),
        out_shape=jax.ShapeDtypeStruct((rows, widths_seq[-1]), jnp.float32),
        in_specs=[vmem, vmem, vmem],
        out_specs=vmem,
        cost_estimate=pl.CostEstimate(
            flops=40 * work, transcendentals=0, bytes_accessed=4 * (rows * widths_seq[0] + rows * widths_seq[-1])
        ),
    )(filterbank, channel_mean[None, :], lane_amounts[:levels])


def merge_section(current, offsets_now, section_index, new_length):
    group_trials = 2**section_index
    total_rows = current.shape[0]
    groups = total_rows // (2 * group_trials)
    blocks = current.reshape(groups, 2, group_trials, current.shape[1])
    lower_part = blocks[:, 0, :, :new_length]
    upper_flat = blocks[:, 1].reshape(groups * group_trials, current.shape[1])
    amounts = offsets_now.reshape(groups, 2, group_trials)
    first_half = lower_part + shift_rows(upper_flat, amounts[:, 0].reshape(-1), new_length).reshape(
        groups, group_trials, new_length
    )
    second_half = lower_part + shift_rows(
        upper_flat, amounts[:, 1].reshape(-1), new_length
    ).reshape(groups, group_trials, new_length)
    return jnp.stack([first_half, second_half], axis=1).reshape(total_rows, new_length)


def template_tables(widths):
    source = lax.broadcasted_iota(jnp.int32, (2 * TAPS, TAPS), 0)
    target = lax.broadcasted_iota(jnp.int32, (2 * TAPS, TAPS), 1)
    tap_offset = source - target
    inside = (tap_offset[None] >= 0) & (tap_offset[None] < widths[:, None, None])
    tap_scale = 1.0 / jnp.sqrt(widths.astype(jnp.float32))
    return jnp.where(inside, tap_scale[:, None, None], jnp.zeros((), jnp.float32))


def boxcar_max(dedispersed, widths):
    total_rows = dedispersed.shape[0]
    blocks_time = TS // TAPS
    window = dedispersed.reshape(total_rows, blocks_time + 1, TAPS)
    paired = jnp.concatenate([window[:, :-1], window[:, 1:]], axis=2).reshape(
        total_rows * blocks_time, 2 * TAPS
    )
    tables = template_tables(widths)
    joined = jnp.transpose(tables, (1, 0, 2)).reshape(2 * TAPS, TEMPLATES * TAPS)
    result = jnp.dot(
        paired,
        joined,
        precision=lax.Precision.HIGHEST,
        preferred_element_type=jnp.float32,
    )
    best_value = jnp.max(result.reshape(total_rows * blocks_time, TEMPLATES, TAPS), axis=1)
    return best_value.reshape(total_rows, TS)


def per_device(filterbank, offsets, widths):
    levels = offsets.shape[0]
    local_count = filterbank.shape[0].bit_length() - 1
    band_count = lax.axis_size("band")
    channels_all = filterbank.shape[0] * band_count

    def length_after(sections_done):
        needed = TS + TAPS + (levels - sections_done) * (SHIFT - 1)
        needed = -(-needed // 128) * 128
        return min(TIN, needed)

    partial_value = jnp.sum(filterbank, axis=0)
    channel_mean = butterfly(partial_value, "band", jnp.add) / channels_all
    widths_seq = [length_after(section) for section in range(local_count + 1)]
    current = local_tree(filterbank, channel_mean, offsets[:local_count], widths_seq)
    band_index = lax.axis_index("band")
    for bit_index in range(band_count.bit_length() - 1):
        section_index = local_count + bit_index
        new_length = length_after(section_index + 1)
        partner = from_partner(current, "band", bit_index)
        upper_half = band_index // 2**bit_index % 2 == 1
        lower_part = jnp.where(upper_half, partner, current)
        upper_part = jnp.where(upper_half, current, partner)
        current = lower_part[:, :new_length] + shift_rows(
            upper_part, offsets[section_index], new_length
        )
    dedispersed = current * (1.0 / math.sqrt(channels_all))
    detection = boxcar_max(dedispersed, widths)
    peak_series = butterfly(jnp.max(detection, axis=0), "band", jnp.maximum)
    return (detection, peak_series)


def solution(mesh):
    placed = (P(("beam", "band"), None), P(None, "band"), P())
    return jax.shard_map(
        per_device,
        mesh=mesh,
        in_specs=placed,
        out_specs=(P(("beam", "band"), None), P("beam")),
        check_vma=False,
    )
```

```python
import functools
import math

import jax
import jax.numpy as jnp
from jax import lax
from jax.experimental import pallas as pl
from jax.experimental.pallas import tpu as pltpu
from jax.sharding import PartitionSpec as P

TS = 2048
TIN = 6144
SHIFT = 256
TAPS = 128
TEMPLATES = 8
TAIL_WIDTH = 1152


def from_partner(value, axis, distance):
    mask = 2**distance
    pairs = [(source, source ^ mask) for source in range(lax.axis_size(axis))]
    return lax.ppermute(value, axis, pairs)


def from_xor(value, axis, mask):
    pairs = [(source, source ^ mask) for source in range(lax.axis_size(axis))]
    return lax.ppermute(value, axis, pairs)


def butterfly(value, axis, combine):
    bit_count = lax.axis_size(axis).bit_length() - 1
    position = lax.axis_index(axis)
    low_bit = 0
    while low_bit < bit_count:
        width = min(2, bit_count - low_bit)
        group = 2**width
        received = [value] + [from_xor(value, axis, k << low_bit) for k in range(1, group)]
        mine = position >> low_bit & (group - 1)
        ordered = []
        for slot in range(group):
            chosen = received[0]
            for k in range(1, group):
                chosen = jnp.where((mine ^ slot) == k, received[k], chosen)
            ordered.append(chosen)
        while len(ordered) > 1:
            ordered = [combine(ordered[i], ordered[i + 1]) for i in range(0, len(ordered), 2)]
        value = ordered[0]
        low_bit += width
    return value


def shift_rows(trial_rows, amounts, length):
    current = jnp.pad(trial_rows, ((0, 0), (0, 2 * SHIFT)))
    top_bit = (SHIFT - 1).bit_length()
    for bit_index in reversed(range(top_bit)):
        span = 2**bit_index
        keep_len = length + span - 1
        chosen = (amounts >> bit_index & 1)[:, None] == 1
        current = jnp.where(chosen, current[:, span : span + keep_len], current[:, :keep_len])
    return current


def local_tree_kernel(widths_seq, x_ref, mean_ref, amount_ref, out_ref):
    rows = x_ref.shape[0]
    cur = x_ref[:, : widths_seq[0]] - mean_ref[:, : widths_seq[0]]
    row_id = lax.broadcasted_iota(jnp.int32, (rows, 1), 0)
    for section_index in range(len(widths_seq) - 1):
        mask = 2**section_index
        width = widths_seq[section_index]
        new_width = widths_seq[section_index + 1]
        is_upper = (row_id & mask) != 0
        from_below = pltpu.roll(cur, rows - mask, axis=0)
        from_above = pltpu.roll(cur, mask, axis=0)
        partner = jnp.where(is_upper, from_above, from_below)
        lower = jnp.where(is_upper, partner, cur)
        shifted = jnp.where(is_upper, cur, partner)
        amount = amount_ref[section_index][:, 0:1]
        for bit_index in range((SHIFT - 1).bit_length()):
            span = 2**bit_index
            chosen = (amount >> bit_index & 1) == 1
            shifted = jnp.where(chosen, pltpu.roll(shifted, width - span, axis=1), shifted)
        cur = lower[:, :new_width] + shifted[:, :new_width]
    out_ref[...] = cur


def local_tree(filterbank, channel_mean, amounts, widths_seq):
    rows = filterbank.shape[0]
    vmem = pl.BlockSpec(memory_space=pltpu.VMEM)
    lane_amounts = jnp.broadcast_to(amounts[:, :, None], amounts.shape + (128,))
    levels = len(widths_seq) - 1
    work = rows * sum(widths_seq[:-1])
    return pl.pallas_call(
        functools.partial(local_tree_kernel, tuple(widths_seq)),
        out_shape=jax.ShapeDtypeStruct((rows, widths_seq[-1]), jnp.float32),
        in_specs=[vmem, vmem, vmem],
        out_specs=vmem,
        cost_estimate=pl.CostEstimate(
            flops=40 * work, transcendentals=0, bytes_accessed=4 * (rows * widths_seq[0] + rows * widths_seq[-1])
        ),
    )(filterbank, channel_mean[None, :], lane_amounts[:levels])


def merge_section(current, offsets_now, section_index, new_length):
    group_trials = 2**section_index
    total_rows = current.shape[0]
    groups = total_rows // (2 * group_trials)
    blocks = current.reshape(groups, 2, group_trials, current.shape[1])
    lower_part = blocks[:, 0, :, :new_length]
    upper_flat = blocks[:, 1].reshape(groups * group_trials, current.shape[1])
    amounts = offsets_now.reshape(groups, 2, group_trials)
    first_half = lower_part + shift_rows(upper_flat, amounts[:, 0].reshape(-1), new_length).reshape(
        groups, group_trials, new_length
    )
    second_half = lower_part + shift_rows(
        upper_flat, amounts[:, 1].reshape(-1), new_length
    ).reshape(groups, group_trials, new_length)
    return jnp.stack([first_half, second_half], axis=1).reshape(total_rows, new_length)


def template_tables(widths):
    source = lax.broadcasted_iota(jnp.int32, (2 * TAPS, TAPS), 0)
    target = lax.broadcasted_iota(jnp.int32, (2 * TAPS, TAPS), 1)
    tap_offset = source - target
    inside = (tap_offset[None] >= 0) & (tap_offset[None] < widths[:, None, None])
    tap_scale = 1.0 / jnp.sqrt(widths.astype(jnp.float32))
    return jnp.where(inside, tap_scale[:, None, None], jnp.zeros((), jnp.float32))


def boxcar_max(dedispersed, widths):
    total_rows = dedispersed.shape[0]
    blocks_time = TS // TAPS
    window = dedispersed.reshape(total_rows, blocks_time + 1, TAPS)
    paired = jnp.concatenate([window[:, :-1], window[:, 1:]], axis=2).reshape(
        total_rows * blocks_time, 2 * TAPS
    )
    tables = template_tables(widths)
    joined = jnp.transpose(tables, (1, 0, 2)).reshape(2 * TAPS, TEMPLATES * TAPS)
    result = jnp.dot(
        paired,
        joined,
        precision=lax.Precision.HIGHEST,
        preferred_element_type=jnp.float32,
    )
    best_value = jnp.max(result.reshape(total_rows * blocks_time, TEMPLATES, TAPS), axis=1)
    return best_value.reshape(total_rows, TS)


def per_device(filterbank, offsets, widths):
    levels = offsets.shape[0]
    local_count = filterbank.shape[0].bit_length() - 1
    band_count = lax.axis_size("band")
    channels_all = filterbank.shape[0] * band_count

    def length_after(sections_done):
        needed = TS + TAPS + (levels - sections_done) * (SHIFT - 1)
        needed = -(-needed // 128) * 128
        return min(TIN, needed)

    partial_value = jnp.sum(filterbank, axis=0)
    channel_mean = butterfly(partial_value, "band", jnp.add) / channels_all
    widths_seq = [length_after(section) for section in range(local_count + 1)]
    current = local_tree(filterbank, channel_mean, offsets[:local_count], widths_seq)
    band_index = lax.axis_index("band")
    bit_count = band_count.bit_length() - 1
    tail_width = TAIL_WIDTH

    def halves(own, partner, bit_index):
        upper_half = band_index // 2**bit_index % 2 == 1
        return jnp.where(upper_half, partner, own), jnp.where(upper_half, own, partner)

    head = current[:, : current.shape[1] - tail_width]
    tail = current[:, current.shape[1] - tail_width :]
    partner_head = from_partner(head, "band", 0)
    for bit_index in range(bit_count):
        amounts = offsets[local_count + bit_index]
        tail, partner_head = lax.optimization_barrier((tail, partner_head))
        lower_head, upper_head = halves(head, partner_head, bit_index)
        head_width = head.shape[1] - SHIFT
        new_head = lower_head[:, :head_width] + shift_rows(upper_head, amounts, head_width)
        partner_tail = from_partner(tail, "band", bit_index)
        if bit_index + 1 < bit_count:
            next_partner_head = from_partner(new_head, "band", bit_index + 1)
            partner_tail, next_partner_head = lax.optimization_barrier((partner_tail, next_partner_head))
            partner_head = next_partner_head
        lower_tail, upper_tail = halves(tail, partner_tail, bit_index)
        lower_window = jnp.concatenate([lower_head[:, head_width:], lower_tail], axis=1)
        upper_window = jnp.concatenate([upper_head[:, head_width:], upper_tail], axis=1)
        tail = lower_window[:, :tail_width] + shift_rows(upper_window, amounts, tail_width)
        head = new_head
    current = jnp.concatenate([head, tail], axis=1)
    dedispersed = current * (1.0 / math.sqrt(channels_all))
    detection = boxcar_max(dedispersed, widths)
    peak_series = butterfly(jnp.max(detection, axis=0), "band", jnp.maximum)
    return (detection, peak_series)


def solution(mesh):
    placed = (P(("beam", "band"), None), P(None, "band"), P())
    return jax.shard_map(
        per_device,
        mesh=mesh,
        in_specs=placed,
        out_specs=(P(("beam", "band"), None), P("beam")),
        check_vma=False,
    )
```

```python
import functools
import math

import jax
import jax.numpy as jnp
from jax import lax
from jax.experimental import pallas as pl
from jax.experimental.pallas import tpu as pltpu
from jax.sharding import PartitionSpec as P

TS = 2048
TIN = 6144
SHIFT = 256
TAPS = 128
TEMPLATES = 8
TAIL_WIDTH = 1152


def from_partner(value, axis, distance):
    mask = 2**distance
    pairs = [(source, source ^ mask) for source in range(lax.axis_size(axis))]
    return lax.ppermute(value, axis, pairs)


def from_xor(value, axis, mask):
    pairs = [(source, source ^ mask) for source in range(lax.axis_size(axis))]
    return lax.ppermute(value, axis, pairs)


def butterfly(value, axis, combine):
    bit_count = lax.axis_size(axis).bit_length() - 1
    position = lax.axis_index(axis)
    low_bit = 0
    while low_bit < bit_count:
        width = min(2, bit_count - low_bit)
        group = 2**width
        received = [value] + [from_xor(value, axis, k << low_bit) for k in range(1, group)]
        mine = position >> low_bit & (group - 1)
        ordered = []
        for slot in range(group):
            chosen = received[0]
            for k in range(1, group):
                chosen = jnp.where((mine ^ slot) == k, received[k], chosen)
            ordered.append(chosen)
        while len(ordered) > 1:
            ordered = [combine(ordered[i], ordered[i + 1]) for i in range(0, len(ordered), 2)]
        value = ordered[0]
        low_bit += width
    return value


def shift_rows(trial_rows, amounts, length):
    current = jnp.pad(trial_rows, ((0, 0), (0, 2 * SHIFT)))
    top_bit = (SHIFT - 1).bit_length()
    for bit_index in reversed(range(top_bit)):
        span = 2**bit_index
        keep_len = length + span - 1
        chosen = (amounts >> bit_index & 1)[:, None] == 1
        current = jnp.where(chosen, current[:, span : span + keep_len], current[:, :keep_len])
    return current


def local_tree_kernel(widths_seq, channels_all, x_ref, total_ref, offsets_ref, head_ref, tail_ref):
    rows = x_ref.shape[0]
    cur = x_ref[:, : widths_seq[0]] - total_ref[:, : widths_seq[0]] / channels_all
    row_id = lax.broadcasted_iota(jnp.int32, (rows, 1), 0)
    diagonal = lax.broadcasted_iota(jnp.int32, (rows, rows), 0) == lax.broadcasted_iota(
        jnp.int32, (rows, rows), 1
    )
    for section_index in range(len(widths_seq) - 1):
        mask = 2**section_index
        width = widths_seq[section_index]
        new_width = widths_seq[section_index + 1]
        is_upper = (row_id & mask) != 0
        from_below = pltpu.roll(cur, rows - mask, axis=0)
        from_above = pltpu.roll(cur, mask, axis=0)
        partner = jnp.where(is_upper, from_above, from_below)
        lower = jnp.where(is_upper, partner, cur)
        shifted = jnp.where(is_upper, cur, partner)
        amount_row = jnp.broadcast_to(offsets_ref[section_index : section_index + 1, :], (rows, rows))
        amount = jnp.sum(jnp.where(diagonal, amount_row, 0), axis=1, keepdims=True)
        for bit_index in range((SHIFT - 1).bit_length()):
            span = 2**bit_index
            chosen = (amount >> bit_index & 1) == 1
            shifted = jnp.where(chosen, pltpu.roll(shifted, width - span, axis=1), shifted)
        cur = lower[:, :new_width] + shifted[:, :new_width]
    head_width = head_ref.shape[1]
    head_ref[...] = cur[:, :head_width]
    tail_ref[...] = cur[:, head_width:]


def local_tree(filterbank, channel_total, offsets, widths_seq, channels_all, tail_width):
    rows = filterbank.shape[0]
    vmem = pl.BlockSpec(memory_space=pltpu.VMEM)
    work = rows * sum(widths_seq[:-1])
    head_width = widths_seq[-1] - tail_width
    return pl.pallas_call(
        functools.partial(local_tree_kernel, tuple(widths_seq), float(channels_all)),
        out_shape=(
            jax.ShapeDtypeStruct((rows, head_width), jnp.float32),
            jax.ShapeDtypeStruct((rows, tail_width), jnp.float32),
        ),
        in_specs=[vmem, vmem, vmem],
        out_specs=(vmem, vmem),
        cost_estimate=pl.CostEstimate(
            flops=40 * work, transcendentals=0, bytes_accessed=4 * (rows * widths_seq[0] + rows * widths_seq[-1])
        ),
    )(filterbank, channel_total[None, :], offsets)


def merge_section(current, offsets_now, section_index, new_length):
    group_trials = 2**section_index
    total_rows = current.shape[0]
    groups = total_rows // (2 * group_trials)
    blocks = current.reshape(groups, 2, group_trials, current.shape[1])
    lower_part = blocks[:, 0, :, :new_length]
    upper_flat = blocks[:, 1].reshape(groups * group_trials, current.shape[1])
    amounts = offsets_now.reshape(groups, 2, group_trials)
    first_half = lower_part + shift_rows(upper_flat, amounts[:, 0].reshape(-1), new_length).reshape(
        groups, group_trials, new_length
    )
    second_half = lower_part + shift_rows(
        upper_flat, amounts[:, 1].reshape(-1), new_length
    ).reshape(groups, group_trials, new_length)
    return jnp.stack([first_half, second_half], axis=1).reshape(total_rows, new_length)


def template_tables(widths):
    source = lax.broadcasted_iota(jnp.int32, (2 * TAPS, TAPS), 0)
    target = lax.broadcasted_iota(jnp.int32, (2 * TAPS, TAPS), 1)
    tap_offset = source - target
    inside = (tap_offset[None] >= 0) & (tap_offset[None] < widths[:, None, None])
    tap_scale = 1.0 / jnp.sqrt(widths.astype(jnp.float32))
    return jnp.where(inside, tap_scale[:, None, None], jnp.zeros((), jnp.float32))


def boxcar_max(dedispersed, widths):
    total_rows = dedispersed.shape[0]
    blocks_time = TS // TAPS
    window = dedispersed.reshape(total_rows, blocks_time + 1, TAPS)
    paired = jnp.concatenate([window[:, :-1], window[:, 1:]], axis=2).reshape(
        total_rows * blocks_time, 2 * TAPS
    )
    tables = template_tables(widths)
    joined = jnp.transpose(tables, (1, 0, 2)).reshape(2 * TAPS, TEMPLATES * TAPS)
    result = jnp.dot(
        paired,
        joined,
        precision=lax.Precision.HIGHEST,
        preferred_element_type=jnp.float32,
    )
    best_value = jnp.max(result.reshape(total_rows * blocks_time, TEMPLATES, TAPS), axis=1)
    return best_value.reshape(total_rows, TS)


def per_device(filterbank, offsets, widths):
    levels = offsets.shape[0]
    local_count = filterbank.shape[0].bit_length() - 1
    band_count = lax.axis_size("band")
    channels_all = filterbank.shape[0] * band_count

    def length_after(sections_done):
        needed = TS + TAPS + (levels - sections_done) * (SHIFT - 1)
        needed = -(-needed // 128) * 128
        return min(TIN, needed)

    partial_value = jnp.sum(filterbank, axis=0)
    channel_total = butterfly(partial_value, "band", jnp.add)
    widths_seq = [length_after(section) for section in range(local_count + 1)]
    head, tail = local_tree(filterbank, channel_total, offsets, widths_seq, channels_all, TAIL_WIDTH)
    band_index = lax.axis_index("band")
    bit_count = band_count.bit_length() - 1
    tail_width = TAIL_WIDTH

    def halves(own, partner, bit_index):
        upper_half = band_index // 2**bit_index % 2 == 1
        return jnp.where(upper_half, partner, own), jnp.where(upper_half, own, partner)

    partner_head = from_partner(head, "band", 0)
    for bit_index in range(bit_count):
        amounts = offsets[local_count + bit_index]
        tail, partner_head = lax.optimization_barrier((tail, partner_head))
        lower_head, upper_head = halves(head, partner_head, bit_index)
        head_width = head.shape[1] - SHIFT
        new_head = lower_head[:, :head_width] + shift_rows(upper_head, amounts, head_width)
        partner_tail = from_partner(tail, "band", bit_index)
        if bit_index + 1 < bit_count:
            next_partner_head = from_partner(new_head, "band", bit_index + 1)
            partner_tail, next_partner_head = lax.optimization_barrier((partner_tail, next_partner_head))
            partner_head = next_partner_head
        lower_tail, upper_tail = halves(tail, partner_tail, bit_index)
        lower_window = jnp.concatenate([lower_head[:, head_width:], lower_tail], axis=1)
        upper_window = jnp.concatenate([upper_head[:, head_width:], upper_tail], axis=1)
        tail = lower_window[:, :tail_width] + shift_rows(upper_window, amounts, tail_width)
        head = new_head
    current = jnp.concatenate([head, tail], axis=1)
    dedispersed = current * (1.0 / math.sqrt(channels_all))
    detection = boxcar_max(dedispersed, widths)
    peak_series = butterfly(jnp.max(detection, axis=0), "band", jnp.maximum)
    return (detection, peak_series)


def solution(mesh):
    placed = (P(("beam", "band"), None), P(None, "band"), P())
    return jax.shard_map(
        per_device,
        mesh=mesh,
        in_specs=placed,
        out_specs=(P(("beam", "band"), None), P("beam")),
        check_vma=False,
    )
```

```python
import functools
import math

import jax
import jax.numpy as jnp
from jax import lax
from jax.experimental import pallas as pl
from jax.experimental.pallas import tpu as pltpu
from jax.sharding import PartitionSpec as P

TS = 2048
TIN = 6144
SHIFT = 256
TAPS = 128
TEMPLATES = 8
TAIL_WIDTH = 1152
RADIX_BITS = 4


def from_partner(value, axis, distance):
    mask = 2**distance
    pairs = [(source, source ^ mask) for source in range(lax.axis_size(axis))]
    return lax.ppermute(value, axis, pairs)


def from_xor(value, axis, mask):
    pairs = [(source, source ^ mask) for source in range(lax.axis_size(axis))]
    return lax.ppermute(value, axis, pairs)


def butterfly(value, axis, combine):
    bit_count = lax.axis_size(axis).bit_length() - 1
    position = lax.axis_index(axis)
    low_bit = 0
    while low_bit < bit_count:
        width = min(RADIX_BITS, bit_count - low_bit)
        group = 2**width
        received = [value] + [from_xor(value, axis, k << low_bit) for k in range(1, group)]
        mine = position >> low_bit & (group - 1)
        ordered = []
        for slot in range(group):
            chosen = received[0]
            for k in range(1, group):
                chosen = jnp.where((mine ^ slot) == k, received[k], chosen)
            ordered.append(chosen)
        while len(ordered) > 1:
            ordered = [combine(ordered[i], ordered[i + 1]) for i in range(0, len(ordered), 2)]
        value = ordered[0]
        low_bit += width
    return value


def shift_rows(trial_rows, amounts, length):
    current = jnp.pad(trial_rows, ((0, 0), (0, 2 * SHIFT)))
    top_bit = (SHIFT - 1).bit_length()
    for bit_index in reversed(range(top_bit)):
        span = 2**bit_index
        keep_len = length + span - 1
        chosen = (amounts >> bit_index & 1)[:, None] == 1
        current = jnp.where(chosen, current[:, span : span + keep_len], current[:, :keep_len])
    return current


def local_tree_kernel(widths_seq, channels_all, x_ref, total_ref, offsets_ref, head_ref, tail_ref):
    rows = x_ref.shape[0]
    cur = x_ref[:, : widths_seq[0]] - total_ref[:, : widths_seq[0]] / channels_all
    row_id = lax.broadcasted_iota(jnp.int32, (rows, 1), 0)
    diagonal = lax.broadcasted_iota(jnp.int32, (rows, rows), 0) == lax.broadcasted_iota(
        jnp.int32, (rows, rows), 1
    )
    for section_index in range(len(widths_seq) - 1):
        mask = 2**section_index
        width = widths_seq[section_index]
        new_width = widths_seq[section_index + 1]
        is_upper = (row_id & mask) != 0
        from_below = pltpu.roll(cur, rows - mask, axis=0)
        from_above = pltpu.roll(cur, mask, axis=0)
        partner = jnp.where(is_upper, from_above, from_below)
        lower = jnp.where(is_upper, partner, cur)
        shifted = jnp.where(is_upper, cur, partner)
        amount_row = jnp.broadcast_to(offsets_ref[section_index : section_index + 1, :], (rows, rows))
        amount = jnp.sum(jnp.where(diagonal, amount_row, 0), axis=1, keepdims=True)
        for bit_index in range((SHIFT - 1).bit_length()):
            span = 2**bit_index
            chosen = (amount >> bit_index & 1) == 1
            shifted = jnp.where(chosen, pltpu.roll(shifted, width - span, axis=1), shifted)
        cur = lower[:, :new_width] + shifted[:, :new_width]
    head_width = head_ref.shape[1]
    head_ref[...] = cur[:, :head_width]
    tail_ref[...] = cur[:, head_width:]


def local_tree(filterbank, channel_total, offsets, widths_seq, channels_all, tail_width):
    rows = filterbank.shape[0]
    vmem = pl.BlockSpec(memory_space=pltpu.VMEM)
    work = rows * sum(widths_seq[:-1])
    head_width = widths_seq[-1] - tail_width
    return pl.pallas_call(
        functools.partial(local_tree_kernel, tuple(widths_seq), float(channels_all)),
        out_shape=(
            jax.ShapeDtypeStruct((rows, head_width), jnp.float32),
            jax.ShapeDtypeStruct((rows, tail_width), jnp.float32),
        ),
        in_specs=[vmem, vmem, vmem],
        out_specs=(vmem, vmem),
        cost_estimate=pl.CostEstimate(
            flops=40 * work, transcendentals=0, bytes_accessed=4 * (rows * widths_seq[0] + rows * widths_seq[-1])
        ),
    )(filterbank, channel_total[None, :], offsets)


def merge_section(current, offsets_now, section_index, new_length):
    group_trials = 2**section_index
    total_rows = current.shape[0]
    groups = total_rows // (2 * group_trials)
    blocks = current.reshape(groups, 2, group_trials, current.shape[1])
    lower_part = blocks[:, 0, :, :new_length]
    upper_flat = blocks[:, 1].reshape(groups * group_trials, current.shape[1])
    amounts = offsets_now.reshape(groups, 2, group_trials)
    first_half = lower_part + shift_rows(upper_flat, amounts[:, 0].reshape(-1), new_length).reshape(
        groups, group_trials, new_length
    )
    second_half = lower_part + shift_rows(
        upper_flat, amounts[:, 1].reshape(-1), new_length
    ).reshape(groups, group_trials, new_length)
    return jnp.stack([first_half, second_half], axis=1).reshape(total_rows, new_length)


def template_tables(widths):
    source = lax.broadcasted_iota(jnp.int32, (2 * TAPS, TAPS), 0)
    target = lax.broadcasted_iota(jnp.int32, (2 * TAPS, TAPS), 1)
    tap_offset = source - target
    inside = (tap_offset[None] >= 0) & (tap_offset[None] < widths[:, None, None])
    tap_scale = 1.0 / jnp.sqrt(widths.astype(jnp.float32))
    return jnp.where(inside, tap_scale[:, None, None], jnp.zeros((), jnp.float32))


def boxcar_max(dedispersed, widths):
    total_rows = dedispersed.shape[0]
    blocks_time = TS // TAPS
    window = dedispersed.reshape(total_rows, blocks_time + 1, TAPS)
    paired = jnp.concatenate([window[:, :-1], window[:, 1:]], axis=2).reshape(
        total_rows * blocks_time, 2 * TAPS
    )
    tables = template_tables(widths)
    joined = jnp.transpose(tables, (1, 0, 2)).reshape(2 * TAPS, TEMPLATES * TAPS)
    result = jnp.dot(
        paired,
        joined,
        precision=lax.Precision.HIGHEST,
        preferred_element_type=jnp.float32,
    )
    best_value = jnp.max(result.reshape(total_rows * blocks_time, TEMPLATES, TAPS), axis=1)
    return best_value.reshape(total_rows, TS)


def per_device(filterbank, offsets, widths):
    levels = offsets.shape[0]
    local_count = filterbank.shape[0].bit_length() - 1
    band_count = lax.axis_size("band")
    channels_all = filterbank.shape[0] * band_count

    def length_after(sections_done):
        needed = TS + TAPS + (levels - sections_done) * (SHIFT - 1)
        needed = -(-needed // 128) * 128
        return min(TIN, needed)

    partial_value = jnp.sum(filterbank, axis=0)
    channel_total = butterfly(partial_value, "band", jnp.add)
    widths_seq = [length_after(section) for section in range(local_count + 1)]
    head, tail = local_tree(filterbank, channel_total, offsets, widths_seq, channels_all, TAIL_WIDTH)
    band_index = lax.axis_index("band")
    bit_count = band_count.bit_length() - 1
    tail_width = TAIL_WIDTH

    def halves(own, partner, bit_index):
        upper_half = band_index // 2**bit_index % 2 == 1
        return jnp.where(upper_half, partner, own), jnp.where(upper_half, own, partner)

    partner_head = from_partner(head, "band", 0)
    for bit_index in range(bit_count):
        amounts = offsets[local_count + bit_index]
        tail, partner_head = lax.optimization_barrier((tail, partner_head))
        lower_head, upper_head = halves(head, partner_head, bit_index)
        head_width = head.shape[1] - SHIFT
        new_head = lower_head[:, :head_width] + shift_rows(upper_head, amounts, head_width)
        partner_tail = from_partner(tail, "band", bit_index)
        if bit_index + 1 < bit_count:
            next_partner_head = from_partner(new_head, "band", bit_index + 1)
            partner_tail, next_partner_head = lax.optimization_barrier((partner_tail, next_partner_head))
            partner_head = next_partner_head
        lower_tail, upper_tail = halves(tail, partner_tail, bit_index)
        lower_window = jnp.concatenate([lower_head[:, head_width:], lower_tail], axis=1)
        upper_window = jnp.concatenate([upper_head[:, head_width:], upper_tail], axis=1)
        tail = lower_window[:, :tail_width] + shift_rows(upper_window, amounts, tail_width)
        head = new_head
    current = jnp.concatenate([head, tail], axis=1)
    dedispersed = current * (1.0 / math.sqrt(channels_all))
    detection = boxcar_max(dedispersed, widths)
    peak_series = butterfly(jnp.max(detection, axis=0), "band", jnp.maximum)
    return (detection, peak_series)


def solution(mesh):
    placed = (P(("beam", "band"), None), P(None, "band"), P())
    return jax.shard_map(
        per_device,
        mesh=mesh,
        in_specs=placed,
        out_specs=(P(("beam", "band"), None), P("beam")),
        check_vma=False,
    )
```

```python
import functools
import math

import jax
import jax.numpy as jnp
from jax import lax
from jax.experimental import pallas as pl
from jax.experimental.pallas import tpu as pltpu
from jax.sharding import PartitionSpec as P

TS = 2048
TIN = 6144
SHIFT = 256
TAPS = 128
TEMPLATES = 8
TAIL_WIDTH = 1152


def from_partner(value, axis, distance):
    mask = 2**distance
    pairs = [(source, source ^ mask) for source in range(lax.axis_size(axis))]
    return lax.ppermute(value, axis, pairs)


def from_xor(value, axis, mask):
    pairs = [(source, source ^ mask) for source in range(lax.axis_size(axis))]
    return lax.ppermute(value, axis, pairs)


def butterfly(value, axis, combine, side=None):
    bit_count = lax.axis_size(axis).bit_length() - 1
    position = lax.axis_index(axis)
    partners = {}
    low_bit = 0
    while low_bit < bit_count:
        width = min(2, bit_count - low_bit)
        group = 2**width
        payload = value if side is None else jnp.concatenate([value, side])
        received = [payload] + [from_xor(payload, axis, k << low_bit) for k in range(1, group)]
        if side is not None:
            for k in range(1, group):
                partners[k << low_bit] = received[k][value.shape[0] :]
            received = [item[: value.shape[0]] for item in received]
        mine = position >> low_bit & (group - 1)
        ordered = []
        for slot in range(group):
            chosen = received[0]
            for k in range(1, group):
                chosen = jnp.where((mine ^ slot) == k, received[k], chosen)
            ordered.append(chosen)
        while len(ordered) > 1:
            ordered = [combine(ordered[i], ordered[i + 1]) for i in range(0, len(ordered), 2)]
        value = ordered[0]
        low_bit += width
    return value, partners


def shift_rows(trial_rows, amounts, length):
    current = jnp.pad(trial_rows, ((0, 0), (0, 2 * SHIFT)))
    top_bit = (SHIFT - 1).bit_length()
    for bit_index in reversed(range(top_bit)):
        span = 2**bit_index
        keep_len = length + span - 1
        chosen = (amounts >> bit_index & 1)[:, None] == 1
        current = jnp.where(chosen, current[:, span : span + keep_len], current[:, :keep_len])
    return current


def local_tree_kernel(widths_seq, channels_all, x_ref, total_ref, offsets_ref, head_ref, tail_ref):
    rows = x_ref.shape[0]
    cur = x_ref[:, : widths_seq[0]] - total_ref[:, : widths_seq[0]] / channels_all
    row_id = lax.broadcasted_iota(jnp.int32, (rows, 1), 0)
    diagonal = lax.broadcasted_iota(jnp.int32, (rows, rows), 0) == lax.broadcasted_iota(
        jnp.int32, (rows, rows), 1
    )
    for section_index in range(len(widths_seq) - 1):
        mask = 2**section_index
        width = widths_seq[section_index]
        new_width = widths_seq[section_index + 1]
        is_upper = (row_id & mask) != 0
        from_below = pltpu.roll(cur, rows - mask, axis=0)
        from_above = pltpu.roll(cur, mask, axis=0)
        partner = jnp.where(is_upper, from_above, from_below)
        lower = jnp.where(is_upper, partner, cur)
        shifted = jnp.where(is_upper, cur, partner)
        amount_row = jnp.broadcast_to(offsets_ref[section_index : section_index + 1, :], (rows, rows))
        amount = jnp.sum(jnp.where(diagonal, amount_row, 0), axis=1, keepdims=True)
        for bit_index in range((SHIFT - 1).bit_length()):
            span = 2**bit_index
            chosen = (amount >> bit_index & 1) == 1
            shifted = jnp.where(chosen, pltpu.roll(shifted, width - span, axis=1), shifted)
        cur = lower[:, :new_width] + shifted[:, :new_width]
    head_width = head_ref.shape[1]
    head_ref[...] = cur[:, :head_width]
    tail_ref[...] = cur[:, head_width:]


def local_tree(filterbank, channel_total, offsets, widths_seq, channels_all, tail_width):
    rows = filterbank.shape[0]
    vmem = pl.BlockSpec(memory_space=pltpu.VMEM)
    work = rows * sum(widths_seq[:-1])
    head_width = widths_seq[-1] - tail_width
    return pl.pallas_call(
        functools.partial(local_tree_kernel, tuple(widths_seq), float(channels_all)),
        out_shape=(
            jax.ShapeDtypeStruct((rows, head_width), jnp.float32),
            jax.ShapeDtypeStruct((rows, tail_width), jnp.float32),
        ),
        in_specs=[vmem, vmem, vmem],
        out_specs=(vmem, vmem),
        cost_estimate=pl.CostEstimate(
            flops=40 * work, transcendentals=0, bytes_accessed=4 * (rows * widths_seq[0] + rows * widths_seq[-1])
        ),
    )(filterbank, channel_total[None, :], offsets)


def merge_section(current, offsets_now, section_index, new_length):
    group_trials = 2**section_index
    total_rows = current.shape[0]
    groups = total_rows // (2 * group_trials)
    blocks = current.reshape(groups, 2, group_trials, current.shape[1])
    lower_part = blocks[:, 0, :, :new_length]
    upper_flat = blocks[:, 1].reshape(groups * group_trials, current.shape[1])
    amounts = offsets_now.reshape(groups, 2, group_trials)
    first_half = lower_part + shift_rows(upper_flat, amounts[:, 0].reshape(-1), new_length).reshape(
        groups, group_trials, new_length
    )
    second_half = lower_part + shift_rows(
        upper_flat, amounts[:, 1].reshape(-1), new_length
    ).reshape(groups, group_trials, new_length)
    return jnp.stack([first_half, second_half], axis=1).reshape(total_rows, new_length)


def template_tables(widths):
    source = lax.broadcasted_iota(jnp.int32, (2 * TAPS, TAPS), 0)
    target = lax.broadcasted_iota(jnp.int32, (2 * TAPS, TAPS), 1)
    tap_offset = source - target
    inside = (tap_offset[None] >= 0) & (tap_offset[None] < widths[:, None, None])
    tap_scale = 1.0 / jnp.sqrt(widths.astype(jnp.float32))
    return jnp.where(inside, tap_scale[:, None, None], jnp.zeros((), jnp.float32))


def boxcar_max(dedispersed, widths):
    total_rows = dedispersed.shape[0]
    blocks_time = TS // TAPS
    window = dedispersed.reshape(total_rows, blocks_time + 1, TAPS)
    paired = jnp.concatenate([window[:, :-1], window[:, 1:]], axis=2).reshape(
        total_rows * blocks_time, 2 * TAPS
    )
    tables = template_tables(widths)
    joined = jnp.transpose(tables, (1, 0, 2)).reshape(2 * TAPS, TEMPLATES * TAPS)
    result = jnp.dot(
        paired,
        joined,
        precision=lax.Precision.HIGHEST,
        preferred_element_type=jnp.float32,
    )
    best_value = jnp.max(result.reshape(total_rows * blocks_time, TEMPLATES, TAPS), axis=1)
    return best_value.reshape(total_rows, TS)


def per_device(filterbank, offsets, widths):
    levels = offsets.shape[0]
    local_count = filterbank.shape[0].bit_length() - 1
    band_count = lax.axis_size("band")
    channels_all = filterbank.shape[0] * band_count

    def length_after(sections_done):
        needed = TS + TAPS + (levels - sections_done) * (SHIFT - 1)
        needed = -(-needed // 128) * 128
        return min(TIN, needed)

    partial_value = jnp.sum(filterbank, axis=0)
    own_side = offsets.astype(jnp.float32).reshape(-1)
    channel_total, partner_sides = butterfly(partial_value, "band", jnp.add, own_side)
    widths_seq = [length_after(section) for section in range(local_count + 1)]
    head, tail = local_tree(filterbank, channel_total, offsets, widths_seq, channels_all, TAIL_WIDTH)
    band_index = lax.axis_index("band")
    bit_count = band_count.bit_length() - 1
    tail_width = TAIL_WIDTH

    def amounts_for(bit_index, own):
        section_index = local_count + bit_index
        if own:
            values = offsets[section_index]
        else:
            side = partner_sides[2**bit_index].reshape(levels, -1)
            values = side[section_index].astype(jnp.int32)
        upper_half = band_index // 2**bit_index % 2 == 1
        return jnp.where(upper_half, values, 0)

    head_width = head.shape[1] - SHIFT
    partner_head = from_partner(shift_rows(head, amounts_for(0, False), head_width), "band", 0)
    for bit_index in range(bit_count):
        head, tail, partner_head = lax.optimization_barrier((head, tail, partner_head))
        head_width = head.shape[1] - SHIFT
        new_head = shift_rows(head, amounts_for(bit_index, True), head_width) + partner_head
        window = jnp.concatenate([head[:, head_width:], tail], axis=1)
        partner_tail = from_partner(
            shift_rows(window, amounts_for(bit_index, False), tail_width), "band", bit_index
        )
        if bit_index + 1 < bit_count:
            next_width = head_width - SHIFT
            next_partner_head = from_partner(
                shift_rows(new_head, amounts_for(bit_index + 1, False), next_width), "band", bit_index + 1
            )
            partner_tail, next_partner_head = lax.optimization_barrier((partner_tail, next_partner_head))
            partner_head = next_partner_head
        tail = shift_rows(window, amounts_for(bit_index, True), tail_width) + partner_tail
        head = new_head
    current = jnp.concatenate([head, tail], axis=1)
    dedispersed = current * (1.0 / math.sqrt(channels_all))
    detection = boxcar_max(dedispersed, widths)
    peak_series, _ = butterfly(jnp.max(detection, axis=0), "band", jnp.maximum)
    return (detection, peak_series)


def solution(mesh):
    placed = (P(("beam", "band"), None), P(None, "band"), P())
    return jax.shard_map(
        per_device,
        mesh=mesh,
        in_specs=placed,
        out_specs=(P(("beam", "band"), None), P("beam")),
        check_vma=False,
    )
```

```python
import functools
import math

import jax
import jax.numpy as jnp
from jax import lax
from jax.experimental import pallas as pl
from jax.experimental.pallas import tpu as pltpu
from jax.sharding import PartitionSpec as P

TS = 2048
TIN = 6144
SHIFT = 256
TAPS = 128
TEMPLATES = 8
TAIL_WIDTH = 1152


def from_partner(value, axis, distance):
    mask = 2**distance
    pairs = [(source, source ^ mask) for source in range(lax.axis_size(axis))]
    return lax.ppermute(value, axis, pairs)


def from_xor(value, axis, mask):
    pairs = [(source, source ^ mask) for source in range(lax.axis_size(axis))]
    return lax.ppermute(value, axis, pairs)


def butterfly(value, axis, combine):
    bit_count = lax.axis_size(axis).bit_length() - 1
    position = lax.axis_index(axis)
    low_bit = 0
    while low_bit < bit_count:
        width = min(2, bit_count - low_bit)
        group = 2**width
        received = [value] + [from_xor(value, axis, k << low_bit) for k in range(1, group)]
        mine = position >> low_bit & (group - 1)
        ordered = []
        for slot in range(group):
            chosen = received[0]
            for k in range(1, group):
                chosen = jnp.where((mine ^ slot) == k, received[k], chosen)
            ordered.append(chosen)
        while len(ordered) > 1:
            ordered = [combine(ordered[i], ordered[i + 1]) for i in range(0, len(ordered), 2)]
        value = ordered[0]
        low_bit += width
    return value


def shift_rows(trial_rows, amounts, length):
    current = jnp.pad(trial_rows, ((0, 0), (0, 2 * SHIFT)))
    top_bit = (SHIFT - 1).bit_length()
    for bit_index in reversed(range(top_bit)):
        span = 2**bit_index
        keep_len = length + span - 1
        chosen = (amounts >> bit_index & 1)[:, None] == 1
        current = jnp.where(chosen, current[:, span : span + keep_len], current[:, :keep_len])
    return current


def local_tree_kernel(widths_seq, channels_all, x_ref, total_ref, offsets_ref, head_ref, tail_ref):
    rows = x_ref.shape[0]
    cur = x_ref[:, : widths_seq[0]] - total_ref[:, : widths_seq[0]] / channels_all
    row_id = lax.broadcasted_iota(jnp.int32, (rows, 1), 0)
    diagonal = lax.broadcasted_iota(jnp.int32, (rows, rows), 0) == lax.broadcasted_iota(
        jnp.int32, (rows, rows), 1
    )
    for section_index in range(len(widths_seq) - 1):
        mask = 2**section_index
        width = widths_seq[section_index]
        new_width = widths_seq[section_index + 1]
        is_upper = (row_id & mask) != 0
        from_below = pltpu.roll(cur, rows - mask, axis=0)
        from_above = pltpu.roll(cur, mask, axis=0)
        partner = jnp.where(is_upper, from_above, from_below)
        lower = jnp.where(is_upper, partner, cur)
        shifted = jnp.where(is_upper, cur, partner)
        amount_row = jnp.broadcast_to(offsets_ref[section_index : section_index + 1, :], (rows, rows))
        amount = jnp.sum(jnp.where(diagonal, amount_row, 0), axis=1, keepdims=True)
        for bit_index in range((SHIFT - 1).bit_length()):
            span = 2**bit_index
            chosen = (amount >> bit_index & 1) == 1
            shifted = jnp.where(chosen, pltpu.roll(shifted, width - span, axis=1), shifted)
        cur = lower[:, :new_width] + shifted[:, :new_width]
    head_width = head_ref.shape[1]
    head_ref[...] = cur[:, :head_width]
    tail_ref[...] = cur[:, head_width:]


def local_tree(filterbank, channel_total, offsets, widths_seq, channels_all, tail_width):
    rows = filterbank.shape[0]
    vmem = pl.BlockSpec(memory_space=pltpu.VMEM)
    work = rows * sum(widths_seq[:-1])
    head_width = widths_seq[-1] - tail_width
    return pl.pallas_call(
        functools.partial(local_tree_kernel, tuple(widths_seq), float(channels_all)),
        out_shape=(
            jax.ShapeDtypeStruct((rows, head_width), jnp.float32),
            jax.ShapeDtypeStruct((rows, tail_width), jnp.float32),
        ),
        in_specs=[vmem, vmem, vmem],
        out_specs=(vmem, vmem),
        cost_estimate=pl.CostEstimate(
            flops=40 * work, transcendentals=0, bytes_accessed=4 * (rows * widths_seq[0] + rows * widths_seq[-1])
        ),
    )(filterbank, channel_total[None, :], offsets)


def merge_section(current, offsets_now, section_index, new_length):
    group_trials = 2**section_index
    total_rows = current.shape[0]
    groups = total_rows // (2 * group_trials)
    blocks = current.reshape(groups, 2, group_trials, current.shape[1])
    lower_part = blocks[:, 0, :, :new_length]
    upper_flat = blocks[:, 1].reshape(groups * group_trials, current.shape[1])
    amounts = offsets_now.reshape(groups, 2, group_trials)
    first_half = lower_part + shift_rows(upper_flat, amounts[:, 0].reshape(-1), new_length).reshape(
        groups, group_trials, new_length
    )
    second_half = lower_part + shift_rows(
        upper_flat, amounts[:, 1].reshape(-1), new_length
    ).reshape(groups, group_trials, new_length)
    return jnp.stack([first_half, second_half], axis=1).reshape(total_rows, new_length)


def template_tables(widths):
    source = lax.broadcasted_iota(jnp.int32, (2 * TAPS, TAPS), 0)
    target = lax.broadcasted_iota(jnp.int32, (2 * TAPS, TAPS), 1)
    tap_offset = source - target
    inside = (tap_offset[None] >= 0) & (tap_offset[None] < widths[:, None, None])
    tap_scale = 1.0 / jnp.sqrt(widths.astype(jnp.float32))
    return jnp.where(inside, tap_scale[:, None, None], jnp.zeros((), jnp.float32))


def boxcar_max(dedispersed, widths):
    total_rows = dedispersed.shape[0]
    blocks_time = TS // TAPS
    window = dedispersed.reshape(total_rows, blocks_time + 1, TAPS)
    paired = jnp.concatenate([window[:, :-1], window[:, 1:]], axis=2).reshape(
        total_rows * blocks_time, 2 * TAPS
    )
    tables = template_tables(widths)
    joined = jnp.transpose(tables, (1, 0, 2)).reshape(2 * TAPS, TEMPLATES * TAPS)
    result = jnp.dot(
        paired,
        joined,
        precision=lax.Precision.HIGH,
        preferred_element_type=jnp.float32,
    )
    best_value = jnp.max(result.reshape(total_rows * blocks_time, TEMPLATES, TAPS), axis=1)
    return best_value.reshape(total_rows, TS)


def per_device(filterbank, offsets, widths):
    levels = offsets.shape[0]
    local_count = filterbank.shape[0].bit_length() - 1
    band_count = lax.axis_size("band")
    channels_all = filterbank.shape[0] * band_count

    def length_after(sections_done):
        needed = TS + TAPS + (levels - sections_done) * (SHIFT - 1)
        needed = -(-needed // 128) * 128
        return min(TIN, needed)

    partial_value = jnp.sum(filterbank[:, : length_after(0)], axis=0)
    channel_total = butterfly(partial_value, "band", jnp.add)
    widths_seq = [length_after(section) for section in range(local_count + 1)]
    head, tail = local_tree(filterbank, channel_total, offsets, widths_seq, channels_all, TAIL_WIDTH)
    band_index = lax.axis_index("band")
    bit_count = band_count.bit_length() - 1
    tail_width = TAIL_WIDTH

    def halves(own, partner, bit_index):
        upper_half = band_index // 2**bit_index % 2 == 1
        return jnp.where(upper_half, partner, own), jnp.where(upper_half, own, partner)

    partner_head = from_partner(head, "band", 0)
    for bit_index in range(bit_count):
        amounts = offsets[local_count + bit_index]
        tail, partner_head = lax.optimization_barrier((tail, partner_head))
        lower_head, upper_head = halves(head, partner_head, bit_index)
        head_width = head.shape[1] - SHIFT
        new_head = lower_head[:, :head_width] + shift_rows(upper_head, amounts, head_width)
        partner_tail = from_partner(tail, "band", bit_index)
        if bit_index + 1 < bit_count:
            next_partner_head = from_partner(new_head, "band", bit_index + 1)
            partner_tail, next_partner_head = lax.optimization_barrier((partner_tail, next_partner_head))
            partner_head = next_partner_head
        lower_tail, upper_tail = halves(tail, partner_tail, bit_index)
        lower_window = jnp.concatenate([lower_head[:, head_width:], lower_tail], axis=1)
        upper_window = jnp.concatenate([upper_head[:, head_width:], upper_tail], axis=1)
        tail = lower_window[:, :tail_width] + shift_rows(upper_window, amounts, tail_width)
        head = new_head
    current = jnp.concatenate([head, tail], axis=1)
    dedispersed = current * (1.0 / math.sqrt(channels_all))
    detection = boxcar_max(dedispersed, widths)
    peak_series = butterfly(jnp.max(detection, axis=0), "band", jnp.maximum)
    return (detection, peak_series)


def solution(mesh):
    placed = (P(("beam", "band"), None), P(None, "band"), P())
    return jax.shard_map(
        per_device,
        mesh=mesh,
        in_specs=placed,
        out_specs=(P(("beam", "band"), None), P("beam")),
        check_vma=False,
    )
```

```python
import functools
import math

import jax
import jax.numpy as jnp
from jax import lax
from jax.experimental import pallas as pl
from jax.experimental.pallas import tpu as pltpu
from jax.sharding import PartitionSpec as P

TS = 2048
TIN = 6144
SHIFT = 256
TAPS = 128
TEMPLATES = 8
TAIL_WIDTH = 1280


def from_partner(value, axis, distance):
    mask = 2**distance
    pairs = [(source, source ^ mask) for source in range(lax.axis_size(axis))]
    return lax.ppermute(value, axis, pairs)


def from_xor(value, axis, mask):
    pairs = [(source, source ^ mask) for source in range(lax.axis_size(axis))]
    return lax.ppermute(value, axis, pairs)


def butterfly(value, axis, combine):
    bit_count = lax.axis_size(axis).bit_length() - 1
    position = lax.axis_index(axis)
    low_bit = 0
    while low_bit < bit_count:
        width = min(2, bit_count - low_bit)
        group = 2**width
        received = [value] + [from_xor(value, axis, k << low_bit) for k in range(1, group)]
        mine = position >> low_bit & (group - 1)
        ordered = []
        for slot in range(group):
            chosen = received[0]
            for k in range(1, group):
                chosen = jnp.where((mine ^ slot) == k, received[k], chosen)
            ordered.append(chosen)
        while len(ordered) > 1:
            ordered = [combine(ordered[i], ordered[i + 1]) for i in range(0, len(ordered), 2)]
        value = ordered[0]
        low_bit += width
    return value


def shift_rows(trial_rows, amounts, length):
    current = jnp.pad(trial_rows, ((0, 0), (0, 2 * SHIFT)))
    top_bit = (SHIFT - 1).bit_length()
    for bit_index in reversed(range(top_bit)):
        span = 2**bit_index
        keep_len = length + span - 1
        chosen = (amounts >> bit_index & 1)[:, None] == 1
        current = jnp.where(chosen, current[:, span : span + keep_len], current[:, :keep_len])
    return current


def local_tree_kernel(widths_seq, channels_all, x_ref, total_ref, offsets_ref, head_ref, tail_ref):
    rows = x_ref.shape[0]
    cur = x_ref[:, : widths_seq[0]] - total_ref[:, : widths_seq[0]] / channels_all
    row_id = lax.broadcasted_iota(jnp.int32, (rows, 1), 0)
    diagonal = lax.broadcasted_iota(jnp.int32, (rows, rows), 0) == lax.broadcasted_iota(
        jnp.int32, (rows, rows), 1
    )
    for section_index in range(len(widths_seq) - 1):
        mask = 2**section_index
        width = widths_seq[section_index]
        new_width = widths_seq[section_index + 1]
        is_upper = (row_id & mask) != 0
        from_below = pltpu.roll(cur, rows - mask, axis=0)
        from_above = pltpu.roll(cur, mask, axis=0)
        partner = jnp.where(is_upper, from_above, from_below)
        lower = jnp.where(is_upper, partner, cur)
        shifted = jnp.where(is_upper, cur, partner)
        amount_row = jnp.broadcast_to(offsets_ref[section_index : section_index + 1, :], (rows, rows))
        amount = jnp.sum(jnp.where(diagonal, amount_row, 0), axis=1, keepdims=True)
        for bit_index in range((SHIFT - 1).bit_length()):
            span = 2**bit_index
            chosen = (amount >> bit_index & 1) == 1
            shifted = jnp.where(chosen, pltpu.roll(shifted, width - span, axis=1), shifted)
        cur = lower[:, :new_width] + shifted[:, :new_width]
    head_width = head_ref.shape[1]
    head_ref[...] = cur[:, :head_width]
    tail_ref[...] = cur[:, head_width:]


def local_tree(filterbank, channel_total, offsets, widths_seq, channels_all, tail_width):
    rows = filterbank.shape[0]
    vmem = pl.BlockSpec(memory_space=pltpu.VMEM)
    work = rows * sum(widths_seq[:-1])
    head_width = widths_seq[-1] - tail_width
    return pl.pallas_call(
        functools.partial(local_tree_kernel, tuple(widths_seq), float(channels_all)),
        out_shape=(
            jax.ShapeDtypeStruct((rows, head_width), jnp.float32),
            jax.ShapeDtypeStruct((rows, tail_width), jnp.float32),
        ),
        in_specs=[vmem, vmem, vmem],
        out_specs=(vmem, vmem),
        cost_estimate=pl.CostEstimate(
            flops=40 * work, transcendentals=0, bytes_accessed=4 * (rows * widths_seq[0] + rows * widths_seq[-1])
        ),
    )(filterbank, channel_total[None, :], offsets)


def merge_section(current, offsets_now, section_index, new_length):
    group_trials = 2**section_index
    total_rows = current.shape[0]
    groups = total_rows // (2 * group_trials)
    blocks = current.reshape(groups, 2, group_trials, current.shape[1])
    lower_part = blocks[:, 0, :, :new_length]
    upper_flat = blocks[:, 1].reshape(groups * group_trials, current.shape[1])
    amounts = offsets_now.reshape(groups, 2, group_trials)
    first_half = lower_part + shift_rows(upper_flat, amounts[:, 0].reshape(-1), new_length).reshape(
        groups, group_trials, new_length
    )
    second_half = lower_part + shift_rows(
        upper_flat, amounts[:, 1].reshape(-1), new_length
    ).reshape(groups, group_trials, new_length)
    return jnp.stack([first_half, second_half], axis=1).reshape(total_rows, new_length)


def template_tables(widths):
    source = lax.broadcasted_iota(jnp.int32, (2 * TAPS, TAPS), 0)
    target = lax.broadcasted_iota(jnp.int32, (2 * TAPS, TAPS), 1)
    tap_offset = source - target
    inside = (tap_offset[None] >= 0) & (tap_offset[None] < widths[:, None, None])
    tap_scale = 1.0 / jnp.sqrt(widths.astype(jnp.float32))
    return jnp.where(inside, tap_scale[:, None, None], jnp.zeros((), jnp.float32))


def boxcar_max(dedispersed, widths):
    total_rows = dedispersed.shape[0]
    blocks_time = TS // TAPS
    window = dedispersed.reshape(total_rows, blocks_time + 1, TAPS)
    paired = jnp.concatenate([window[:, :-1], window[:, 1:]], axis=2).reshape(
        total_rows * blocks_time, 2 * TAPS
    )
    tables = template_tables(widths)
    joined = jnp.transpose(tables, (1, 0, 2)).reshape(2 * TAPS, TEMPLATES * TAPS)
    result = jnp.dot(
        paired,
        joined,
        precision=lax.Precision.HIGH,
        preferred_element_type=jnp.float32,
    )
    best_value = jnp.max(result.reshape(total_rows * blocks_time, TEMPLATES, TAPS), axis=1)
    return best_value.reshape(total_rows, TS)


def per_device(filterbank, offsets, widths):
    levels = offsets.shape[0]
    local_count = filterbank.shape[0].bit_length() - 1
    band_count = lax.axis_size("band")
    channels_all = filterbank.shape[0] * band_count

    def length_after(sections_done):
        needed = TS + TAPS + (levels - sections_done) * (SHIFT - 1)
        needed = -(-needed // 128) * 128
        return min(TIN, needed)

    partial_value = jnp.sum(filterbank[:, : length_after(0)], axis=0)
    channel_total = butterfly(partial_value, "band", jnp.add)
    widths_seq = [length_after(section) for section in range(local_count + 1)]
    head, tail = local_tree(filterbank, channel_total, offsets, widths_seq, channels_all, TAIL_WIDTH)
    band_index = lax.axis_index("band")
    bit_count = band_count.bit_length() - 1
    tail_width = TAIL_WIDTH

    def halves(own, partner, bit_index):
        upper_half = band_index // 2**bit_index % 2 == 1
        return jnp.where(upper_half, partner, own), jnp.where(upper_half, own, partner)

    partner_head = from_partner(head, "band", 0)
    for bit_index in range(bit_count):
        amounts = offsets[local_count + bit_index]
        tail, partner_head = lax.optimization_barrier((tail, partner_head))
        lower_head, upper_head = halves(head, partner_head, bit_index)
        head_width = head.shape[1] - SHIFT
        new_head = lower_head[:, :head_width] + shift_rows(upper_head, amounts, head_width)
        partner_tail = from_partner(tail, "band", bit_index)
        if bit_index + 1 < bit_count:
            next_partner_head = from_partner(new_head, "band", bit_index + 1)
            partner_tail, next_partner_head = lax.optimization_barrier((partner_tail, next_partner_head))
            partner_head = next_partner_head
        lower_tail, upper_tail = halves(tail, partner_tail, bit_index)
        lower_window = jnp.concatenate([lower_head[:, head_width:], lower_tail], axis=1)
        upper_window = jnp.concatenate([upper_head[:, head_width:], upper_tail], axis=1)
        tail = lower_window[:, :tail_width] + shift_rows(upper_window, amounts, tail_width)
        head = new_head
    current = jnp.concatenate([head, tail], axis=1)
    dedispersed = current * (1.0 / math.sqrt(channels_all))
    detection = boxcar_max(dedispersed, widths)
    peak_series = butterfly(jnp.max(detection, axis=0), "band", jnp.maximum)
    return (detection, peak_series)


def solution(mesh):
    placed = (P(("beam", "band"), None), P(None, "band"), P())
    return jax.shard_map(
        per_device,
        mesh=mesh,
        in_specs=placed,
        out_specs=(P(("beam", "band"), None), P("beam")),
        check_vma=False,
    )
```

```python
import functools
import math

import jax
import jax.numpy as jnp
from jax import lax
from jax.experimental import pallas as pl
from jax.experimental.pallas import tpu as pltpu
from jax.sharding import PartitionSpec as P

TS = 2048
TIN = 6144
SHIFT = 256
TAPS = 128
TEMPLATES = 8
TAIL_WIDTH = 1024


def from_partner(value, axis, distance):
    mask = 2**distance
    pairs = [(source, source ^ mask) for source in range(lax.axis_size(axis))]
    return lax.ppermute(value, axis, pairs)


def from_xor(value, axis, mask):
    pairs = [(source, source ^ mask) for source in range(lax.axis_size(axis))]
    return lax.ppermute(value, axis, pairs)


def butterfly(value, axis, combine):
    bit_count = lax.axis_size(axis).bit_length() - 1
    position = lax.axis_index(axis)
    low_bit = 0
    while low_bit < bit_count:
        width = min(2, bit_count - low_bit)
        group = 2**width
        received = [value] + [from_xor(value, axis, k << low_bit) for k in range(1, group)]
        mine = position >> low_bit & (group - 1)
        ordered = []
        for slot in range(group):
            chosen = received[0]
            for k in range(1, group):
                chosen = jnp.where((mine ^ slot) == k, received[k], chosen)
            ordered.append(chosen)
        while len(ordered) > 1:
            ordered = [combine(ordered[i], ordered[i + 1]) for i in range(0, len(ordered), 2)]
        value = ordered[0]
        low_bit += width
    return value


def shift_rows(trial_rows, amounts, length):
    current = jnp.pad(trial_rows, ((0, 0), (0, 2 * SHIFT)))
    top_bit = (SHIFT - 1).bit_length()
    for bit_index in reversed(range(top_bit)):
        span = 2**bit_index
        keep_len = length + span - 1
        chosen = (amounts >> bit_index & 1)[:, None] == 1
        current = jnp.where(chosen, current[:, span : span + keep_len], current[:, :keep_len])
    return current


def local_tree_kernel(widths_seq, channels_all, x_ref, total_ref, offsets_ref, head_ref, tail_ref):
    rows = x_ref.shape[0]
    cur = x_ref[:, : widths_seq[0]] - total_ref[:, : widths_seq[0]] / channels_all
    row_id = lax.broadcasted_iota(jnp.int32, (rows, 1), 0)
    diagonal = lax.broadcasted_iota(jnp.int32, (rows, rows), 0) == lax.broadcasted_iota(
        jnp.int32, (rows, rows), 1
    )
    for section_index in range(len(widths_seq) - 1):
        mask = 2**section_index
        width = widths_seq[section_index]
        new_width = widths_seq[section_index + 1]
        is_upper = (row_id & mask) != 0
        from_below = pltpu.roll(cur, rows - mask, axis=0)
        from_above = pltpu.roll(cur, mask, axis=0)
        partner = jnp.where(is_upper, from_above, from_below)
        lower = jnp.where(is_upper, partner, cur)
        shifted = jnp.where(is_upper, cur, partner)
        amount_row = jnp.broadcast_to(offsets_ref[section_index : section_index + 1, :], (rows, rows))
        amount = jnp.sum(jnp.where(diagonal, amount_row, 0), axis=1, keepdims=True)
        for bit_index in range((SHIFT - 1).bit_length()):
            span = 2**bit_index
            chosen = (amount >> bit_index & 1) == 1
            shifted = jnp.where(chosen, pltpu.roll(shifted, width - span, axis=1), shifted)
        cur = lower[:, :new_width] + shifted[:, :new_width]
    head_width = head_ref.shape[1]
    head_ref[...] = cur[:, :head_width]
    tail_ref[...] = cur[:, head_width:]


def local_tree(filterbank, channel_total, offsets, widths_seq, channels_all, tail_width):
    rows = filterbank.shape[0]
    vmem = pl.BlockSpec(memory_space=pltpu.VMEM)
    work = rows * sum(widths_seq[:-1])
    head_width = widths_seq[-1] - tail_width
    return pl.pallas_call(
        functools.partial(local_tree_kernel, tuple(widths_seq), float(channels_all)),
        out_shape=(
            jax.ShapeDtypeStruct((rows, head_width), jnp.float32),
            jax.ShapeDtypeStruct((rows, tail_width), jnp.float32),
        ),
        in_specs=[vmem, vmem, vmem],
        out_specs=(vmem, vmem),
        cost_estimate=pl.CostEstimate(
            flops=40 * work, transcendentals=0, bytes_accessed=4 * (rows * widths_seq[0] + rows * widths_seq[-1])
        ),
    )(filterbank, channel_total[None, :], offsets)


def merge_section(current, offsets_now, section_index, new_length):
    group_trials = 2**section_index
    total_rows = current.shape[0]
    groups = total_rows // (2 * group_trials)
    blocks = current.reshape(groups, 2, group_trials, current.shape[1])
    lower_part = blocks[:, 0, :, :new_length]
    upper_flat = blocks[:, 1].reshape(groups * group_trials, current.shape[1])
    amounts = offsets_now.reshape(groups, 2, group_trials)
    first_half = lower_part + shift_rows(upper_flat, amounts[:, 0].reshape(-1), new_length).reshape(
        groups, group_trials, new_length
    )
    second_half = lower_part + shift_rows(
        upper_flat, amounts[:, 1].reshape(-1), new_length
    ).reshape(groups, group_trials, new_length)
    return jnp.stack([first_half, second_half], axis=1).reshape(total_rows, new_length)


def template_tables(widths):
    source = lax.broadcasted_iota(jnp.int32, (2 * TAPS, TAPS), 0)
    target = lax.broadcasted_iota(jnp.int32, (2 * TAPS, TAPS), 1)
    tap_offset = source - target
    inside = (tap_offset[None] >= 0) & (tap_offset[None] < widths[:, None, None])
    tap_scale = 1.0 / jnp.sqrt(widths.astype(jnp.float32))
    return jnp.where(inside, tap_scale[:, None, None], jnp.zeros((), jnp.float32))


def boxcar_max(dedispersed, widths):
    total_rows = dedispersed.shape[0]
    blocks_time = TS // TAPS
    window = dedispersed.reshape(total_rows, blocks_time + 1, TAPS)
    paired = jnp.concatenate([window[:, :-1], window[:, 1:]], axis=2).reshape(
        total_rows * blocks_time, 2 * TAPS
    )
    tables = template_tables(widths)
    joined = jnp.transpose(tables, (1, 0, 2)).reshape(2 * TAPS, TEMPLATES * TAPS)
    result = jnp.dot(
        paired,
        joined,
        precision=lax.Precision.HIGH,
        preferred_element_type=jnp.float32,
    )
    best_value = jnp.max(result.reshape(total_rows * blocks_time, TEMPLATES, TAPS), axis=1)
    return best_value.reshape(total_rows, TS)


def per_device(filterbank, offsets, widths):
    levels = offsets.shape[0]
    local_count = filterbank.shape[0].bit_length() - 1
    band_count = lax.axis_size("band")
    channels_all = filterbank.shape[0] * band_count

    def length_after(sections_done):
        needed = TS + TAPS + (levels - sections_done) * (SHIFT - 1)
        needed = -(-needed // 128) * 128
        return min(TIN, needed)

    partial_value = jnp.sum(filterbank[:, : length_after(0)], axis=0)
    channel_total = butterfly(partial_value, "band", jnp.add)
    widths_seq = [length_after(section) for section in range(local_count + 1)]
    head, tail = local_tree(filterbank, channel_total, offsets, widths_seq, channels_all, TAIL_WIDTH)
    band_index = lax.axis_index("band")
    bit_count = band_count.bit_length() - 1
    tail_width = TAIL_WIDTH

    def halves(own, partner, bit_index):
        upper_half = band_index // 2**bit_index % 2 == 1
        return jnp.where(upper_half, partner, own), jnp.where(upper_half, own, partner)

    partner_head = from_partner(head, "band", 0)
    for bit_index in range(bit_count):
        amounts = offsets[local_count + bit_index]
        tail, partner_head = lax.optimization_barrier((tail, partner_head))
        lower_head, upper_head = halves(head, partner_head, bit_index)
        head_width = head.shape[1] - SHIFT
        new_head = lower_head[:, :head_width] + shift_rows(upper_head, amounts, head_width)
        partner_tail = from_partner(tail, "band", bit_index)
        if bit_index + 1 < bit_count:
            next_partner_head = from_partner(new_head, "band", bit_index + 1)
            partner_tail, next_partner_head = lax.optimization_barrier((partner_tail, next_partner_head))
            partner_head = next_partner_head
        lower_tail, upper_tail = halves(tail, partner_tail, bit_index)
        lower_window = jnp.concatenate([lower_head[:, head_width:], lower_tail], axis=1)
        upper_window = jnp.concatenate([upper_head[:, head_width:], upper_tail], axis=1)
        tail = lower_window[:, :tail_width] + shift_rows(upper_window, amounts, tail_width)
        head = new_head
    current = jnp.concatenate([head, tail], axis=1)
    dedispersed = current * (1.0 / math.sqrt(channels_all))
    detection = boxcar_max(dedispersed, widths)
    peak_series = butterfly(jnp.max(detection, axis=0), "band", jnp.maximum)
    return (detection, peak_series)


def solution(mesh):
    placed = (P(("beam", "band"), None), P(None, "band"), P())
    return jax.shard_map(
        per_device,
        mesh=mesh,
        in_specs=placed,
        out_specs=(P(("beam", "band"), None), P("beam")),
        check_vma=False,
    )
```

```python
import functools
import math

import jax
import jax.numpy as jnp
from jax import lax
from jax.experimental import pallas as pl
from jax.experimental.pallas import tpu as pltpu
from jax.sharding import PartitionSpec as P

TS = 2048
TIN = 6144
SHIFT = 256
TAPS = 128
TEMPLATES = 8
TAIL_WIDTH = 1152


def from_partner(value, axis, distance):
    mask = 2**distance
    pairs = [(source, source ^ mask) for source in range(lax.axis_size(axis))]
    return lax.ppermute(value, axis, pairs)


def from_xor(value, axis, mask):
    pairs = [(source, source ^ mask) for source in range(lax.axis_size(axis))]
    return lax.ppermute(value, axis, pairs)


def butterfly(value, axis, combine):
    bit_count = lax.axis_size(axis).bit_length() - 1
    position = lax.axis_index(axis)
    low_bit = 0
    while low_bit < bit_count:
        width = min(2, bit_count - low_bit)
        group = 2**width
        received = [value] + [from_xor(value, axis, k << low_bit) for k in range(1, group)]
        mine = position >> low_bit & (group - 1)
        ordered = []
        for slot in range(group):
            chosen = received[0]
            for k in range(1, group):
                chosen = jnp.where((mine ^ slot) == k, received[k], chosen)
            ordered.append(chosen)
        while len(ordered) > 1:
            ordered = [combine(ordered[i], ordered[i + 1]) for i in range(0, len(ordered), 2)]
        value = ordered[0]
        low_bit += width
    return value


def shift_rows(trial_rows, amounts, length):
    current = jnp.pad(trial_rows, ((0, 0), (0, 2 * SHIFT)))
    top_bit = (SHIFT - 1).bit_length()
    for bit_index in reversed(range(top_bit)):
        span = 2**bit_index
        keep_len = length + span - 1
        chosen = (amounts >> bit_index & 1)[:, None] == 1
        current = jnp.where(chosen, current[:, span : span + keep_len], current[:, :keep_len])
    return current


def local_tree_kernel(widths_seq, channels_all, x_ref, total_ref, offsets_ref, head_ref, tail_ref):
    rows = x_ref.shape[0]
    cur = x_ref[:, : widths_seq[0]] - total_ref[:, : widths_seq[0]] / channels_all
    row_id = lax.broadcasted_iota(jnp.int32, (rows, 1), 0)
    diagonal = lax.broadcasted_iota(jnp.int32, (rows, rows), 0) == lax.broadcasted_iota(
        jnp.int32, (rows, rows), 1
    )
    for section_index in range(len(widths_seq) - 1):
        mask = 2**section_index
        width = widths_seq[section_index]
        new_width = widths_seq[section_index + 1]
        is_upper = (row_id & mask) != 0
        from_below = pltpu.roll(cur, rows - mask, axis=0)
        from_above = pltpu.roll(cur, mask, axis=0)
        partner = jnp.where(is_upper, from_above, from_below)
        lower = jnp.where(is_upper, partner, cur)
        shifted = jnp.where(is_upper, cur, partner)
        amount_row = jnp.broadcast_to(offsets_ref[section_index : section_index + 1, :], (rows, rows))
        amount = jnp.sum(jnp.where(diagonal, amount_row, 0), axis=1, keepdims=True)
        for bit_index in range((SHIFT - 1).bit_length()):
            span = 2**bit_index
            chosen = (amount >> bit_index & 1) == 1
            shifted = jnp.where(chosen, pltpu.roll(shifted, width - span, axis=1), shifted)
        cur = lower[:, :new_width] + shifted[:, :new_width]
    head_width = head_ref.shape[1]
    head_ref[...] = cur[:, :head_width]
    tail_ref[...] = cur[:, head_width:]


def local_tree(filterbank, channel_total, offsets, widths_seq, channels_all, tail_width):
    rows = filterbank.shape[0]
    vmem = pl.BlockSpec(memory_space=pltpu.VMEM)
    work = rows * sum(widths_seq[:-1])
    head_width = widths_seq[-1] - tail_width
    return pl.pallas_call(
        functools.partial(local_tree_kernel, tuple(widths_seq), float(channels_all)),
        out_shape=(
            jax.ShapeDtypeStruct((rows, head_width), jnp.float32),
            jax.ShapeDtypeStruct((rows, tail_width), jnp.float32),
        ),
        in_specs=[vmem, vmem, vmem],
        out_specs=(vmem, vmem),
        cost_estimate=pl.CostEstimate(
            flops=40 * work, transcendentals=0, bytes_accessed=4 * (rows * widths_seq[0] + rows * widths_seq[-1])
        ),
    )(filterbank, channel_total[None, :], offsets)


def merge_section(current, offsets_now, section_index, new_length):
    group_trials = 2**section_index
    total_rows = current.shape[0]
    groups = total_rows // (2 * group_trials)
    blocks = current.reshape(groups, 2, group_trials, current.shape[1])
    lower_part = blocks[:, 0, :, :new_length]
    upper_flat = blocks[:, 1].reshape(groups * group_trials, current.shape[1])
    amounts = offsets_now.reshape(groups, 2, group_trials)
    first_half = lower_part + shift_rows(upper_flat, amounts[:, 0].reshape(-1), new_length).reshape(
        groups, group_trials, new_length
    )
    second_half = lower_part + shift_rows(
        upper_flat, amounts[:, 1].reshape(-1), new_length
    ).reshape(groups, group_trials, new_length)
    return jnp.stack([first_half, second_half], axis=1).reshape(total_rows, new_length)


def template_tables(widths):
    source = lax.broadcasted_iota(jnp.int32, (2 * TAPS, TAPS), 0)
    target = lax.broadcasted_iota(jnp.int32, (2 * TAPS, TAPS), 1)
    tap_offset = source - target
    inside = (tap_offset[None] >= 0) & (tap_offset[None] < widths[:, None, None])
    tap_scale = 1.0 / jnp.sqrt(widths.astype(jnp.float32))
    return jnp.where(inside, tap_scale[:, None, None], jnp.zeros((), jnp.float32))


def boxcar_max(dedispersed, widths):
    total_rows = dedispersed.shape[0]
    blocks_time = TS // TAPS
    window = dedispersed.reshape(total_rows, blocks_time + 1, TAPS)
    paired = jnp.concatenate([window[:, :-1], window[:, 1:]], axis=2).reshape(
        total_rows * blocks_time, 2 * TAPS
    )
    tables = template_tables(widths)
    joined = jnp.transpose(tables, (1, 0, 2)).reshape(2 * TAPS, TEMPLATES * TAPS)
    result = jnp.dot(
        paired,
        joined,
        precision=lax.Precision.HIGH,
        preferred_element_type=jnp.float32,
    )
    best_value = jnp.max(result.reshape(total_rows * blocks_time, TEMPLATES, TAPS), axis=1)
    return best_value.reshape(total_rows, TS)


def per_device(filterbank, offsets, widths):
    levels = offsets.shape[0]
    local_count = filterbank.shape[0].bit_length() - 1
    band_count = lax.axis_size("band")
    channels_all = filterbank.shape[0] * band_count

    def length_after(sections_done):
        needed = TS + TAPS + (levels - sections_done) * (SHIFT - 1)
        needed = -(-needed // 128) * 128
        return min(TIN, needed)

    partial_value = jnp.sum(filterbank[:, : length_after(0)], axis=0)
    channel_total = butterfly(partial_value, "band", jnp.add)
    widths_seq = [length_after(section) for section in range(local_count + 1)]
    head, tail = local_tree(filterbank, channel_total, offsets, widths_seq, channels_all, TAIL_WIDTH)
    band_index = lax.axis_index("band")
    bit_count = band_count.bit_length() - 1
    tail_width = TAIL_WIDTH

    def halves(own, partner, bit_index):
        upper_half = band_index // 2**bit_index % 2 == 1
        return jnp.where(upper_half, partner, own), jnp.where(upper_half, own, partner)

    partner_head = from_partner(head, "band", 0)
    for bit_index in range(bit_count):
        amounts = offsets[local_count + bit_index]
        tail, partner_head = lax.optimization_barrier((tail, partner_head))
        lower_head, upper_head = halves(head, partner_head, bit_index)
        head_width = head.shape[1] - SHIFT
        new_head = lower_head[:, :head_width] + shift_rows(upper_head, amounts, head_width)
        if bit_index + 1 < bit_count:
            next_partner_head = from_partner(new_head, "band", bit_index + 1)
            tail, new_head = lax.optimization_barrier((tail, new_head))
        partner_tail = from_partner(tail, "band", bit_index)
        if bit_index + 1 < bit_count:
            partner_tail, next_partner_head = lax.optimization_barrier((partner_tail, next_partner_head))
            partner_head = next_partner_head
        lower_tail, upper_tail = halves(tail, partner_tail, bit_index)
        lower_window = jnp.concatenate([lower_head[:, head_width:], lower_tail], axis=1)
        upper_window = jnp.concatenate([upper_head[:, head_width:], upper_tail], axis=1)
        tail = lower_window[:, :tail_width] + shift_rows(upper_window, amounts, tail_width)
        head = new_head
    current = jnp.concatenate([head, tail], axis=1)
    dedispersed = current * (1.0 / math.sqrt(channels_all))
    detection = boxcar_max(dedispersed, widths)
    peak_series = butterfly(jnp.max(detection, axis=0), "band", jnp.maximum)
    return (detection, peak_series)


def solution(mesh):
    placed = (P(("beam", "band"), None), P(None, "band"), P())
    return jax.shard_map(
        per_device,
        mesh=mesh,
        in_specs=placed,
        out_specs=(P(("beam", "band"), None), P("beam")),
        check_vma=False,
    )
```

```python
import functools
import math

import jax
import jax.numpy as jnp
from jax import lax
from jax.experimental import pallas as pl
from jax.experimental.pallas import tpu as pltpu
from jax.sharding import PartitionSpec as P

TS = 2048
TIN = 6144
SHIFT = 256
TAPS = 128
TEMPLATES = 8
TAIL_WIDTH = 1152


def from_partner(value, axis, distance):
    mask = 2**distance
    pairs = [(source, source ^ mask) for source in range(lax.axis_size(axis))]
    return lax.ppermute(value, axis, pairs)


def from_xor(value, axis, mask):
    pairs = [(source, source ^ mask) for source in range(lax.axis_size(axis))]
    return lax.ppermute(value, axis, pairs)


def butterfly(value, axis, combine):
    bit_count = lax.axis_size(axis).bit_length() - 1
    low_bit = 0
    while low_bit < bit_count:
        width = min(2, bit_count - low_bit)
        received = [value] + [from_xor(value, axis, k << low_bit) for k in range(1, 2**width)]
        while len(received) > 1:
            received = [combine(received[i], received[i + 1]) for i in range(0, len(received), 2)]
        value = received[0]
        low_bit += width
    return value


def shift_rows(trial_rows, amounts, length):
    current = jnp.pad(trial_rows, ((0, 0), (0, 2 * SHIFT)))
    top_bit = (SHIFT - 1).bit_length()
    for bit_index in reversed(range(top_bit)):
        span = 2**bit_index
        keep_len = length + span - 1
        chosen = (amounts >> bit_index & 1)[:, None] == 1
        current = jnp.where(chosen, current[:, span : span + keep_len], current[:, :keep_len])
    return current


def local_tree_kernel(widths_seq, channels_all, x_ref, total_ref, offsets_ref, head_ref, tail_ref):
    rows = x_ref.shape[0]
    cur = x_ref[:, : widths_seq[0]] - total_ref[:, : widths_seq[0]] / channels_all
    row_id = lax.broadcasted_iota(jnp.int32, (rows, 1), 0)
    diagonal = lax.broadcasted_iota(jnp.int32, (rows, rows), 0) == lax.broadcasted_iota(
        jnp.int32, (rows, rows), 1
    )
    for section_index in range(len(widths_seq) - 1):
        mask = 2**section_index
        width = widths_seq[section_index]
        new_width = widths_seq[section_index + 1]
        is_upper = (row_id & mask) != 0
        from_below = pltpu.roll(cur, rows - mask, axis=0)
        from_above = pltpu.roll(cur, mask, axis=0)
        partner = jnp.where(is_upper, from_above, from_below)
        lower = jnp.where(is_upper, partner, cur)
        shifted = jnp.where(is_upper, cur, partner)
        amount_row = jnp.broadcast_to(offsets_ref[section_index : section_index + 1, :], (rows, rows))
        amount = jnp.sum(jnp.where(diagonal, amount_row, 0), axis=1, keepdims=True)
        for bit_index in range((SHIFT - 1).bit_length()):
            span = 2**bit_index
            chosen = (amount >> bit_index & 1) == 1
            shifted = jnp.where(chosen, pltpu.roll(shifted, width - span, axis=1), shifted)
        cur = lower[:, :new_width] + shifted[:, :new_width]
    head_width = head_ref.shape[1]
    head_ref[...] = cur[:, :head_width]
    tail_ref[...] = cur[:, head_width:]


def local_tree(filterbank, channel_total, offsets, widths_seq, channels_all, tail_width):
    rows = filterbank.shape[0]
    vmem = pl.BlockSpec(memory_space=pltpu.VMEM)
    work = rows * sum(widths_seq[:-1])
    head_width = widths_seq[-1] - tail_width
    return pl.pallas_call(
        functools.partial(local_tree_kernel, tuple(widths_seq), float(channels_all)),
        out_shape=(
            jax.ShapeDtypeStruct((rows, head_width), jnp.float32),
            jax.ShapeDtypeStruct((rows, tail_width), jnp.float32),
        ),
        in_specs=[vmem, vmem, vmem],
        out_specs=(vmem, vmem),
        cost_estimate=pl.CostEstimate(
            flops=40 * work, transcendentals=0, bytes_accessed=4 * (rows * widths_seq[0] + rows * widths_seq[-1])
        ),
    )(filterbank, channel_total, offsets)


def merge_section(current, offsets_now, section_index, new_length):
    group_trials = 2**section_index
    total_rows = current.shape[0]
    groups = total_rows // (2 * group_trials)
    blocks = current.reshape(groups, 2, group_trials, current.shape[1])
    lower_part = blocks[:, 0, :, :new_length]
    upper_flat = blocks[:, 1].reshape(groups * group_trials, current.shape[1])
    amounts = offsets_now.reshape(groups, 2, group_trials)
    first_half = lower_part + shift_rows(upper_flat, amounts[:, 0].reshape(-1), new_length).reshape(
        groups, group_trials, new_length
    )
    second_half = lower_part + shift_rows(
        upper_flat, amounts[:, 1].reshape(-1), new_length
    ).reshape(groups, group_trials, new_length)
    return jnp.stack([first_half, second_half], axis=1).reshape(total_rows, new_length)


def template_tables(widths):
    source = lax.broadcasted_iota(jnp.int32, (2 * TAPS, TAPS), 0)
    target = lax.broadcasted_iota(jnp.int32, (2 * TAPS, TAPS), 1)
    tap_offset = source - target
    inside = (tap_offset[None] >= 0) & (tap_offset[None] < widths[:, None, None])
    tap_scale = 1.0 / jnp.sqrt(widths.astype(jnp.float32))
    return jnp.where(inside, tap_scale[:, None, None], jnp.zeros((), jnp.float32))


def boxcar_max(dedispersed, widths):
    total_rows = dedispersed.shape[0]
    blocks_time = TS // TAPS
    window = dedispersed.reshape(total_rows, blocks_time + 1, TAPS)
    paired = jnp.concatenate([window[:, :-1], window[:, 1:]], axis=2).reshape(
        total_rows * blocks_time, 2 * TAPS
    )
    tables = template_tables(widths)
    joined = jnp.transpose(tables, (1, 0, 2)).reshape(2 * TAPS, TEMPLATES * TAPS)
    result = jnp.dot(
        paired,
        joined,
        precision=lax.Precision.HIGH,
        preferred_element_type=jnp.float32,
    )
    best_value = jnp.max(result.reshape(total_rows * blocks_time, TEMPLATES, TAPS), axis=1)
    return best_value.reshape(total_rows, TS)


def per_device(filterbank, offsets, widths):
    levels = offsets.shape[0]
    local_count = filterbank.shape[0].bit_length() - 1
    band_count = lax.axis_size("band")
    channels_all = filterbank.shape[0] * band_count

    def length_after(sections_done):
        needed = TS + TAPS + (levels - sections_done) * (SHIFT - 1)
        needed = -(-needed // 128) * 128
        return min(TIN, needed)

    partial_value = jnp.sum(filterbank[:, : length_after(0)], axis=0, keepdims=True)
    channel_total = butterfly(partial_value, "band", jnp.add)
    widths_seq = [length_after(section) for section in range(local_count + 1)]
    head, tail = local_tree(filterbank, channel_total, offsets, widths_seq, channels_all, TAIL_WIDTH)
    band_index = lax.axis_index("band")
    bit_count = band_count.bit_length() - 1
    tail_width = TAIL_WIDTH

    def halves(own, partner, bit_index):
        upper_half = band_index // 2**bit_index % 2 == 1
        return jnp.where(upper_half, partner, own), jnp.where(upper_half, own, partner)

    partner_head = from_partner(head, "band", 0)
    for bit_index in range(bit_count):
        amounts = offsets[local_count + bit_index]
        tail, partner_head = lax.optimization_barrier((tail, partner_head))
        lower_head, upper_head = halves(head, partner_head, bit_index)
        head_width = head.shape[1] - SHIFT
        new_head = lower_head[:, :head_width] + shift_rows(upper_head, amounts, head_width)
        if bit_index + 1 < bit_count:
            next_partner_head = from_partner(new_head, "band", bit_index + 1)
            tail, new_head = lax.optimization_barrier((tail, new_head))
        partner_tail = from_partner(tail, "band", bit_index)
        if bit_index + 1 < bit_count:
            partner_tail, next_partner_head = lax.optimization_barrier((partner_tail, next_partner_head))
            partner_head = next_partner_head
        lower_tail, upper_tail = halves(tail, partner_tail, bit_index)
        lower_window = jnp.concatenate([lower_head[:, head_width:], lower_tail], axis=1)
        upper_window = jnp.concatenate([upper_head[:, head_width:], upper_tail], axis=1)
        tail = lower_window[:, :tail_width] + shift_rows(upper_window, amounts, tail_width)
        head = new_head
    current = jnp.concatenate([head, tail], axis=1)
    dedispersed = current * (1.0 / math.sqrt(channels_all))
    detection = boxcar_max(dedispersed, widths)
    peak_series = butterfly(jnp.max(detection, axis=0), "band", jnp.maximum)
    return (detection, peak_series)


def solution(mesh):
    placed = (P(("beam", "band"), None), P(None, "band"), P())
    return jax.shard_map(
        per_device,
        mesh=mesh,
        in_specs=placed,
        out_specs=(P(("beam", "band"), None), P("beam")),
        check_vma=False,
    )
```

```python
import functools
import math

import jax
import jax.numpy as jnp
from jax import lax
from jax.experimental import pallas as pl
from jax.experimental.pallas import tpu as pltpu
from jax.sharding import PartitionSpec as P

TS = 2048
TIN = 6144
SHIFT = 256
TAPS = 128
TEMPLATES = 8
TAIL_WIDTH = 1152


def from_partner(value, axis, distance):
    mask = 2**distance
    pairs = [(source, source ^ mask) for source in range(lax.axis_size(axis))]
    return lax.ppermute(value, axis, pairs)


def from_xor(value, axis, mask):
    pairs = [(source, source ^ mask) for source in range(lax.axis_size(axis))]
    return lax.ppermute(value, axis, pairs)


def butterfly(value, axis, combine):
    bit_count = lax.axis_size(axis).bit_length() - 1
    low_bit = 0
    while low_bit < bit_count:
        width = min(2, bit_count - low_bit)
        received = [value] + [from_xor(value, axis, k << low_bit) for k in range(1, 2**width)]
        while len(received) > 1:
            received = [combine(received[i], received[i + 1]) for i in range(0, len(received), 2)]
        value = received[0]
        low_bit += width
    return value


def shift_rows(trial_rows, amounts, length):
    current = jnp.pad(trial_rows, ((0, 0), (0, 2 * SHIFT)))
    top_bit = (SHIFT - 1).bit_length()
    for bit_index in reversed(range(top_bit)):
        span = 2**bit_index
        keep_len = length + span - 1
        chosen = (amounts >> bit_index & 1)[:, None] == 1
        current = jnp.where(chosen, current[:, span : span + keep_len], current[:, :keep_len])
    return current


def local_tree_kernel(widths_seq, channels_all, x_ref, total_ref, offsets_ref, head_ref, tail_ref):
    rows = x_ref.shape[0]
    cur = x_ref[:, : widths_seq[0]] - total_ref[:, : widths_seq[0]] / channels_all
    row_id = lax.broadcasted_iota(jnp.int32, (rows, 1), 0)
    diagonal = lax.broadcasted_iota(jnp.int32, (rows, rows), 0) == lax.broadcasted_iota(
        jnp.int32, (rows, rows), 1
    )
    for section_index in range(len(widths_seq) - 1):
        mask = 2**section_index
        width = widths_seq[section_index]
        new_width = widths_seq[section_index + 1]
        is_upper = (row_id & mask) != 0
        from_below = pltpu.roll(cur, rows - mask, axis=0)
        from_above = pltpu.roll(cur, mask, axis=0)
        partner = jnp.where(is_upper, from_above, from_below)
        lower = jnp.where(is_upper, partner, cur)
        shifted = jnp.where(is_upper, cur, partner)
        amount_row = jnp.broadcast_to(offsets_ref[section_index : section_index + 1, :], (rows, rows))
        amount = jnp.sum(jnp.where(diagonal, amount_row, 0), axis=1, keepdims=True)
        for bit_index in range((SHIFT - 1).bit_length()):
            span = 2**bit_index
            chosen = (amount >> bit_index & 1) == 1
            shifted = jnp.where(chosen, pltpu.roll(shifted, width - span, axis=1), shifted)
        cur = lower[:, :new_width] + shifted[:, :new_width]
    head_width = head_ref.shape[1]
    head_ref[...] = cur[:, :head_width]
    tail_ref[...] = cur[:, head_width:]


def local_tree(filterbank, channel_total, offsets, widths_seq, channels_all, tail_width):
    rows = filterbank.shape[0]
    vmem = pl.BlockSpec(memory_space=pltpu.VMEM)
    work = rows * sum(widths_seq[:-1])
    head_width = widths_seq[-1] - tail_width
    return pl.pallas_call(
        functools.partial(local_tree_kernel, tuple(widths_seq), float(channels_all)),
        out_shape=(
            jax.ShapeDtypeStruct((rows, head_width), jnp.float32),
            jax.ShapeDtypeStruct((rows, tail_width), jnp.float32),
        ),
        in_specs=[vmem, vmem, vmem],
        out_specs=(vmem, vmem),
        cost_estimate=pl.CostEstimate(
            flops=40 * work, transcendentals=0, bytes_accessed=4 * (rows * widths_seq[0] + rows * widths_seq[-1])
        ),
    )(filterbank, channel_total, offsets)


def merge_section(current, offsets_now, section_index, new_length):
    group_trials = 2**section_index
    total_rows = current.shape[0]
    groups = total_rows // (2 * group_trials)
    blocks = current.reshape(groups, 2, group_trials, current.shape[1])
    lower_part = blocks[:, 0, :, :new_length]
    upper_flat = blocks[:, 1].reshape(groups * group_trials, current.shape[1])
    amounts = offsets_now.reshape(groups, 2, group_trials)
    first_half = lower_part + shift_rows(upper_flat, amounts[:, 0].reshape(-1), new_length).reshape(
        groups, group_trials, new_length
    )
    second_half = lower_part + shift_rows(
        upper_flat, amounts[:, 1].reshape(-1), new_length
    ).reshape(groups, group_trials, new_length)
    return jnp.stack([first_half, second_half], axis=1).reshape(total_rows, new_length)


def template_tables(widths):
    source = lax.broadcasted_iota(jnp.int32, (2 * TAPS, TAPS), 0)
    target = lax.broadcasted_iota(jnp.int32, (2 * TAPS, TAPS), 1)
    tap_offset = source - target
    inside = (tap_offset[None] >= 0) & (tap_offset[None] < widths[:, None, None])
    tap_scale = 1.0 / jnp.sqrt(widths.astype(jnp.float32))
    return jnp.where(inside, tap_scale[:, None, None], jnp.zeros((), jnp.float32))


def boxcar_max(dedispersed, widths):
    total_rows = dedispersed.shape[0]
    blocks_time = TS // TAPS
    window = dedispersed.reshape(total_rows, blocks_time + 1, TAPS)
    paired = jnp.concatenate([window[:, :-1], window[:, 1:]], axis=2).reshape(
        total_rows * blocks_time, 2 * TAPS
    )
    tables = template_tables(widths)
    joined = jnp.transpose(tables, (1, 0, 2)).reshape(2 * TAPS, TEMPLATES * TAPS)
    result = jnp.dot(
        paired,
        joined,
        precision=lax.Precision.HIGH,
        preferred_element_type=jnp.float32,
    )
    best_value = jnp.max(result.reshape(total_rows * blocks_time, TEMPLATES, TAPS), axis=1)
    return best_value.reshape(total_rows, TS)


def per_device(filterbank, offsets, widths):
    levels = offsets.shape[0]
    local_count = filterbank.shape[0].bit_length() - 1
    band_count = lax.axis_size("band")
    channels_all = filterbank.shape[0] * band_count

    def length_after(sections_done):
        needed = TS + TAPS + (levels - sections_done) * (SHIFT - 1)
        needed = -(-needed // 128) * 128
        return min(TIN, needed)

    partial_value = jnp.sum(filterbank[:, : length_after(0)], axis=0, keepdims=True)
    channel_total = butterfly(partial_value, "band", jnp.add)
    widths_seq = [length_after(section) for section in range(local_count + 1)]
    head, tail = local_tree(filterbank, channel_total, offsets, widths_seq, channels_all, TAIL_WIDTH)
    band_index = lax.axis_index("band")
    bit_count = band_count.bit_length() - 1
    tail_width = TAIL_WIDTH

    def halves(own, partner, bit_index):
        upper_half = band_index // 2**bit_index % 2 == 1
        return jnp.where(upper_half, partner, own), jnp.where(upper_half, own, partner)

    def finish_tail(pending):
        own_tail, partner_tail, lower_edge, upper_edge, amounts, bit_index = pending
        lower_tail, upper_tail = halves(own_tail, partner_tail, bit_index)
        lower_window = jnp.concatenate([lower_edge, lower_tail], axis=1)
        upper_window = jnp.concatenate([upper_edge, upper_tail], axis=1)
        return lower_window[:, :tail_width] + shift_rows(upper_window, amounts, tail_width)

    partner_head = from_partner(head, "band", 0)
    tail, partner_head = lax.optimization_barrier((tail, partner_head))
    pending = None
    for bit_index in range(bit_count):
        amounts = offsets[local_count + bit_index]
        lower_head, upper_head = halves(head, partner_head, bit_index)
        head_width = head.shape[1] - SHIFT
        new_head = lower_head[:, :head_width] + shift_rows(upper_head, amounts, head_width)
        if bit_index + 1 < bit_count:
            next_partner_head = from_partner(new_head, "band", bit_index + 1)
        if pending is not None:
            waiting, ordered_head = lax.optimization_barrier((pending[1], new_head))
            tail = finish_tail(pending[:1] + (waiting,) + pending[2:])
        partner_tail = from_partner(tail, "band", bit_index)
        if bit_index + 1 < bit_count:
            partner_tail, next_partner_head = lax.optimization_barrier((partner_tail, next_partner_head))
            partner_head = next_partner_head
        pending = (tail, partner_tail, lower_head[:, head_width:], upper_head[:, head_width:], amounts, bit_index)
        head = new_head
    tail = finish_tail(pending)
    current = jnp.concatenate([head, tail], axis=1)
    dedispersed = current * (1.0 / math.sqrt(channels_all))
    detection = boxcar_max(dedispersed, widths)
    peak_series = butterfly(jnp.max(detection, axis=0), "band", jnp.maximum)
    return (detection, peak_series)


def solution(mesh):
    placed = (P(("beam", "band"), None), P(None, "band"), P())
    return jax.shard_map(
        per_device,
        mesh=mesh,
        in_specs=placed,
        out_specs=(P(("beam", "band"), None), P("beam")),
        check_vma=False,
    )
```

```python
import functools
import math

import jax
import jax.numpy as jnp
from jax import lax
from jax.experimental import pallas as pl
from jax.experimental.pallas import tpu as pltpu
from jax.sharding import PartitionSpec as P

TS = 2048
TIN = 6144
SHIFT = 256
TAPS = 128
TEMPLATES = 8
LATER_WIDTHS = (768, 1024)


def from_partner(value, axis, distance):
    mask = 2**distance
    pairs = [(source, source ^ mask) for source in range(lax.axis_size(axis))]
    return lax.ppermute(value, axis, pairs)


def from_xor(value, axis, mask):
    pairs = [(source, source ^ mask) for source in range(lax.axis_size(axis))]
    return lax.ppermute(value, axis, pairs)


def butterfly(value, axis, combine):
    bit_count = lax.axis_size(axis).bit_length() - 1
    low_bit = 0
    while low_bit < bit_count:
        width = min(2, bit_count - low_bit)
        received = [value] + [from_xor(value, axis, k << low_bit) for k in range(1, 2**width)]
        while len(received) > 1:
            received = [combine(received[i], received[i + 1]) for i in range(0, len(received), 2)]
        value = received[0]
        low_bit += width
    return value


def shift_rows(trial_rows, amounts, length):
    current = jnp.pad(trial_rows, ((0, 0), (0, 2 * SHIFT)))
    top_bit = (SHIFT - 1).bit_length()
    for bit_index in reversed(range(top_bit)):
        span = 2**bit_index
        keep_len = length + span - 1
        chosen = (amounts >> bit_index & 1)[:, None] == 1
        current = jnp.where(chosen, current[:, span : span + keep_len], current[:, :keep_len])
    return current


def local_tree_kernel(widths_seq, channels_all, x_ref, total_ref, offsets_ref, *chunk_refs):
    rows = x_ref.shape[0]
    cur = x_ref[:, : widths_seq[0]] - total_ref[:, : widths_seq[0]] / channels_all
    row_id = lax.broadcasted_iota(jnp.int32, (rows, 1), 0)
    diagonal = lax.broadcasted_iota(jnp.int32, (rows, rows), 0) == lax.broadcasted_iota(
        jnp.int32, (rows, rows), 1
    )
    for section_index in range(len(widths_seq) - 1):
        mask = 2**section_index
        width = widths_seq[section_index]
        new_width = widths_seq[section_index + 1]
        is_upper = (row_id & mask) != 0
        from_below = pltpu.roll(cur, rows - mask, axis=0)
        from_above = pltpu.roll(cur, mask, axis=0)
        partner = jnp.where(is_upper, from_above, from_below)
        lower = jnp.where(is_upper, partner, cur)
        shifted = jnp.where(is_upper, cur, partner)
        amount_row = jnp.broadcast_to(offsets_ref[section_index : section_index + 1, :], (rows, rows))
        amount = jnp.sum(jnp.where(diagonal, amount_row, 0), axis=1, keepdims=True)
        for bit_index in range((SHIFT - 1).bit_length()):
            span = 2**bit_index
            chosen = (amount >> bit_index & 1) == 1
            shifted = jnp.where(chosen, pltpu.roll(shifted, width - span, axis=1), shifted)
        cur = lower[:, :new_width] + shifted[:, :new_width]
    start = 0
    for chunk_ref in chunk_refs:
        chunk_ref[...] = cur[:, start : start + chunk_ref.shape[1]]
        start += chunk_ref.shape[1]


def local_tree(filterbank, channel_total, offsets, widths_seq, channels_all, later_widths):
    rows = filterbank.shape[0]
    vmem = pl.BlockSpec(memory_space=pltpu.VMEM)
    work = rows * sum(widths_seq[:-1])
    chunk_widths = (widths_seq[-1] - sum(later_widths),) + tuple(later_widths)
    return pl.pallas_call(
        functools.partial(local_tree_kernel, tuple(widths_seq), float(channels_all)),
        out_shape=tuple(jax.ShapeDtypeStruct((rows, width), jnp.float32) for width in chunk_widths),
        in_specs=[vmem, vmem, vmem],
        out_specs=tuple(vmem for _ in chunk_widths),
        cost_estimate=pl.CostEstimate(
            flops=40 * work, transcendentals=0, bytes_accessed=4 * (rows * widths_seq[0] + rows * widths_seq[-1])
        ),
    )(filterbank, channel_total, offsets)


def merge_section(current, offsets_now, section_index, new_length):
    group_trials = 2**section_index
    total_rows = current.shape[0]
    groups = total_rows // (2 * group_trials)
    blocks = current.reshape(groups, 2, group_trials, current.shape[1])
    lower_part = blocks[:, 0, :, :new_length]
    upper_flat = blocks[:, 1].reshape(groups * group_trials, current.shape[1])
    amounts = offsets_now.reshape(groups, 2, group_trials)
    first_half = lower_part + shift_rows(upper_flat, amounts[:, 0].reshape(-1), new_length).reshape(
        groups, group_trials, new_length
    )
    second_half = lower_part + shift_rows(
        upper_flat, amounts[:, 1].reshape(-1), new_length
    ).reshape(groups, group_trials, new_length)
    return jnp.stack([first_half, second_half], axis=1).reshape(total_rows, new_length)


def template_tables(widths):
    source = lax.broadcasted_iota(jnp.int32, (2 * TAPS, TAPS), 0)
    target = lax.broadcasted_iota(jnp.int32, (2 * TAPS, TAPS), 1)
    tap_offset = source - target
    inside = (tap_offset[None] >= 0) & (tap_offset[None] < widths[:, None, None])
    tap_scale = 1.0 / jnp.sqrt(widths.astype(jnp.float32))
    return jnp.where(inside, tap_scale[:, None, None], jnp.zeros((), jnp.float32))


def boxcar_max(dedispersed, widths):
    total_rows = dedispersed.shape[0]
    blocks_time = TS // TAPS
    window = dedispersed.reshape(total_rows, blocks_time + 1, TAPS)
    paired = jnp.concatenate([window[:, :-1], window[:, 1:]], axis=2).reshape(
        total_rows * blocks_time, 2 * TAPS
    )
    tables = template_tables(widths)
    joined = jnp.transpose(tables, (1, 0, 2)).reshape(2 * TAPS, TEMPLATES * TAPS)
    result = jnp.dot(
        paired,
        joined,
        precision=lax.Precision.HIGH,
        preferred_element_type=jnp.float32,
    )
    best_value = jnp.max(result.reshape(total_rows * blocks_time, TEMPLATES, TAPS), axis=1)
    return best_value.reshape(total_rows, TS)


def per_device(filterbank, offsets, widths):
    levels = offsets.shape[0]
    local_count = filterbank.shape[0].bit_length() - 1
    band_count = lax.axis_size("band")
    channels_all = filterbank.shape[0] * band_count

    def length_after(sections_done):
        needed = TS + TAPS + (levels - sections_done) * (SHIFT - 1)
        needed = -(-needed // 128) * 128
        return min(TIN, needed)

    partial_value = jnp.sum(filterbank[:, : length_after(0)], axis=0, keepdims=True)
    channel_total = butterfly(partial_value, "band", jnp.add)
    widths_seq = [length_after(section) for section in range(local_count + 1)]
    chunks = list(local_tree(filterbank, channel_total, offsets, widths_seq, channels_all, LATER_WIDTHS))
    band_index = lax.axis_index("band")
    bit_count = band_count.bit_length() - 1
    chunk_count = len(chunks)

    def halves(own, partner, bit_index):
        upper_half = band_index // 2**bit_index % 2 == 1
        return jnp.where(upper_half, partner, own), jnp.where(upper_half, own, partner)

    own = {(0, k): chunks[k] for k in range(chunk_count)}
    received = {}
    edges = {}
    final = {}
    for wave in range(bit_count + chunk_count - 1):
        cells = [(wave - k, k) for k in range(chunk_count) if 0 <= wave - k < bit_count]
        for level, k in cells:
            value = own[(level, k)]
            if level == 0 and k > 0:
                value, earlier = lax.optimization_barrier((value, received[(0, k - 1)]))
                received[(0, k - 1)] = earlier
            received[(level, k)] = from_partner(value, "band", level)
        if len(cells) > 1:
            grouped = lax.optimization_barrier(tuple(received[cell] for cell in cells))
            for cell, value in zip(cells, grouped):
                received[cell] = value
        for level, k in cells:
            amounts = offsets[local_count + level]
            lower, upper = halves(own[(level, k)], received[(level, k)], level)
            if k == 0:
                width = lower.shape[1] - SHIFT
                merged = lower[:, :width] + shift_rows(upper, amounts, width)
                edge_lower, edge_upper = lower[:, width:], upper[:, width:]
            else:
                width = lower.shape[1]
                prior_lower, prior_upper = edges[(level, k - 1)]
                lower_window = jnp.concatenate([prior_lower, lower], axis=1)
                upper_window = jnp.concatenate([prior_upper, upper], axis=1)
                merged = lower_window[:, :width] + shift_rows(upper_window, amounts, width)
                edge_lower, edge_upper = lower[:, width - SHIFT :], upper[:, width - SHIFT :]
            edges[(level, k)] = (edge_lower, edge_upper)
            if level + 1 < bit_count:
                own[(level + 1, k)] = merged
            else:
                final[k] = merged
    current = jnp.concatenate([final[k] for k in range(chunk_count)], axis=1)
    dedispersed = current * (1.0 / math.sqrt(channels_all))
    detection = boxcar_max(dedispersed, widths)
    peak_series = butterfly(jnp.max(detection, axis=0), "band", jnp.maximum)
    return (detection, peak_series)


def solution(mesh):
    placed = (P(("beam", "band"), None), P(None, "band"), P())
    return jax.shard_map(
        per_device,
        mesh=mesh,
        in_specs=placed,
        out_specs=(P(("beam", "band"), None), P("beam")),
        check_vma=False,
    )
```

```python
import functools
import math

import jax
import jax.numpy as jnp
from jax import lax
from jax.experimental import pallas as pl
from jax.experimental.pallas import tpu as pltpu
from jax.sharding import PartitionSpec as P

TS = 2048
TIN = 6144
SHIFT = 256
TAPS = 128
TEMPLATES = 8
TAIL_WIDTH = 1152


def from_partner(value, axis, distance):
    mask = 2**distance
    pairs = [(source, source ^ mask) for source in range(lax.axis_size(axis))]
    return lax.ppermute(value, axis, pairs)


def from_xor(value, axis, mask):
    pairs = [(source, source ^ mask) for source in range(lax.axis_size(axis))]
    return lax.ppermute(value, axis, pairs)


def butterfly(value, axis, combine):
    bit_count = lax.axis_size(axis).bit_length() - 1
    low_bit = 0
    while low_bit < bit_count:
        width = min(2, bit_count - low_bit)
        received = [value] + [from_xor(value, axis, k << low_bit) for k in range(1, 2**width)]
        while len(received) > 1:
            received = [combine(received[i], received[i + 1]) for i in range(0, len(received), 2)]
        value = received[0]
        low_bit += width
    return value


def shift_rows(trial_rows, amounts, length):
    current = jnp.pad(trial_rows, ((0, 0), (0, 2 * SHIFT)))
    top_bit = (SHIFT - 1).bit_length()
    for bit_index in reversed(range(top_bit)):
        span = 2**bit_index
        keep_len = length + span - 1
        chosen = (amounts >> bit_index & 1)[:, None] == 1
        current = jnp.where(chosen, current[:, span : span + keep_len], current[:, :keep_len])
    return current


def local_tree_kernel(widths_seq, channels_all, x_ref, total_ref, offsets_ref, head_ref, tail_ref):
    rows = x_ref.shape[0]
    cur = x_ref[:, : widths_seq[0]] - total_ref[:, : widths_seq[0]] / channels_all
    row_id = lax.broadcasted_iota(jnp.int32, (rows, 1), 0)
    diagonal = lax.broadcasted_iota(jnp.int32, (rows, rows), 0) == lax.broadcasted_iota(
        jnp.int32, (rows, rows), 1
    )
    for section_index in range(len(widths_seq) - 1):
        mask = 2**section_index
        width = widths_seq[section_index]
        new_width = widths_seq[section_index + 1]
        is_upper = (row_id & mask) != 0
        from_below = pltpu.roll(cur, rows - mask, axis=0)
        from_above = pltpu.roll(cur, mask, axis=0)
        partner = jnp.where(is_upper, from_above, from_below)
        lower = jnp.where(is_upper, partner, cur)
        shifted = jnp.where(is_upper, cur, partner)
        amount_row = jnp.broadcast_to(offsets_ref[section_index : section_index + 1, :], (rows, rows))
        amount = jnp.sum(jnp.where(diagonal, amount_row, 0), axis=1, keepdims=True)
        for bit_index in range((SHIFT - 1).bit_length()):
            span = 2**bit_index
            chosen = (amount >> bit_index & 1) == 1
            shifted = jnp.where(chosen, pltpu.roll(shifted, width - span, axis=1), shifted)
        cur = lower[:, :new_width] + shifted[:, :new_width]
    head_width = head_ref.shape[1]
    head_ref[...] = cur[:, :head_width]
    tail_ref[...] = cur[:, head_width:]


def local_tree(filterbank, channel_total, offsets, widths_seq, channels_all, tail_width):
    rows = filterbank.shape[0]
    vmem = pl.BlockSpec(memory_space=pltpu.VMEM)
    work = rows * sum(widths_seq[:-1])
    head_width = widths_seq[-1] - tail_width
    return pl.pallas_call(
        functools.partial(local_tree_kernel, tuple(widths_seq), float(channels_all)),
        out_shape=(
            jax.ShapeDtypeStruct((rows, head_width), jnp.float32),
            jax.ShapeDtypeStruct((rows, tail_width), jnp.float32),
        ),
        in_specs=[vmem, vmem, vmem],
        out_specs=(vmem, vmem),
        cost_estimate=pl.CostEstimate(
            flops=40 * work, transcendentals=0, bytes_accessed=4 * (rows * widths_seq[0] + rows * widths_seq[-1])
        ),
    )(filterbank, channel_total, offsets)


def merge_head_kernel(level, flag_ref, own_ref, partner_ref, offsets_ref, out_ref):
    rows, width = own_ref.shape
    upper_half = flag_ref[0] == 1
    own = own_ref[...]
    partner = partner_ref[...]
    lower = jnp.where(upper_half, partner, own)
    shifted = jnp.where(upper_half, own, partner)
    diagonal = lax.broadcasted_iota(jnp.int32, (rows, rows), 0) == lax.broadcasted_iota(
        jnp.int32, (rows, rows), 1
    )
    amount_row = jnp.broadcast_to(offsets_ref[level : level + 1, :], (rows, rows))
    amount = jnp.sum(jnp.where(diagonal, amount_row, 0), axis=1, keepdims=True)
    for bit_index in range((SHIFT - 1).bit_length()):
        span = 2**bit_index
        chosen = (amount >> bit_index & 1) == 1
        shifted = jnp.where(chosen, pltpu.roll(shifted, width - span, axis=1), shifted)
    new_width = out_ref.shape[1]
    out_ref[...] = lower[:, :new_width] + shifted[:, :new_width]


def merge_head(own, partner, offsets, level, upper_half):
    rows, width = own.shape
    vmem = pl.BlockSpec(memory_space=pltpu.VMEM)
    flag = jnp.where(upper_half, 1, 0).astype(jnp.int32).reshape(1)
    return pl.pallas_call(
        functools.partial(merge_head_kernel, level),
        out_shape=jax.ShapeDtypeStruct((rows, width - SHIFT), jnp.float32),
        in_specs=[pl.BlockSpec(memory_space=pltpu.SMEM), vmem, vmem, vmem],
        out_specs=vmem,
        cost_estimate=pl.CostEstimate(flops=40 * rows * width, transcendentals=0, bytes_accessed=12 * rows * width),
    )(flag, own, partner, offsets)


def merge_section(current, offsets_now, section_index, new_length):
    group_trials = 2**section_index
    total_rows = current.shape[0]
    groups = total_rows // (2 * group_trials)
    blocks = current.reshape(groups, 2, group_trials, current.shape[1])
    lower_part = blocks[:, 0, :, :new_length]
    upper_flat = blocks[:, 1].reshape(groups * group_trials, current.shape[1])
    amounts = offsets_now.reshape(groups, 2, group_trials)
    first_half = lower_part + shift_rows(upper_flat, amounts[:, 0].reshape(-1), new_length).reshape(
        groups, group_trials, new_length
    )
    second_half = lower_part + shift_rows(
        upper_flat, amounts[:, 1].reshape(-1), new_length
    ).reshape(groups, group_trials, new_length)
    return jnp.stack([first_half, second_half], axis=1).reshape(total_rows, new_length)


def template_tables(widths):
    source = lax.broadcasted_iota(jnp.int32, (2 * TAPS, TAPS), 0)
    target = lax.broadcasted_iota(jnp.int32, (2 * TAPS, TAPS), 1)
    tap_offset = source - target
    inside = (tap_offset[None] >= 0) & (tap_offset[None] < widths[:, None, None])
    tap_scale = 1.0 / jnp.sqrt(widths.astype(jnp.float32))
    return jnp.where(inside, tap_scale[:, None, None], jnp.zeros((), jnp.float32))


def boxcar_max(dedispersed, widths):
    total_rows = dedispersed.shape[0]
    blocks_time = TS // TAPS
    window = dedispersed.reshape(total_rows, blocks_time + 1, TAPS)
    paired = jnp.concatenate([window[:, :-1], window[:, 1:]], axis=2).reshape(
        total_rows * blocks_time, 2 * TAPS
    )
    tables = template_tables(widths)
    joined = jnp.transpose(tables, (1, 0, 2)).reshape(2 * TAPS, TEMPLATES * TAPS)
    result = jnp.dot(
        paired,
        joined,
        precision=lax.Precision.HIGH,
        preferred_element_type=jnp.float32,
    )
    best_value = jnp.max(result.reshape(total_rows * blocks_time, TEMPLATES, TAPS), axis=1)
    return best_value.reshape(total_rows, TS)


def per_device(filterbank, offsets, widths):
    levels = offsets.shape[0]
    local_count = filterbank.shape[0].bit_length() - 1
    band_count = lax.axis_size("band")
    channels_all = filterbank.shape[0] * band_count

    def length_after(sections_done):
        needed = TS + TAPS + (levels - sections_done) * (SHIFT - 1)
        needed = -(-needed // 128) * 128
        return min(TIN, needed)

    partial_value = jnp.sum(filterbank[:, : length_after(0)], axis=0, keepdims=True)
    channel_total = butterfly(partial_value, "band", jnp.add)
    widths_seq = [length_after(section) for section in range(local_count + 1)]
    head, tail = local_tree(filterbank, channel_total, offsets, widths_seq, channels_all, TAIL_WIDTH)
    band_index = lax.axis_index("band")
    bit_count = band_count.bit_length() - 1
    tail_width = TAIL_WIDTH

    def halves(own, partner, bit_index):
        upper_half = band_index // 2**bit_index % 2 == 1
        return jnp.where(upper_half, partner, own), jnp.where(upper_half, own, partner)

    def finish_tail(pending):
        own_tail, partner_tail, lower_edge, upper_edge, amounts, bit_index = pending
        lower_tail, upper_tail = halves(own_tail, partner_tail, bit_index)
        lower_window = jnp.concatenate([lower_edge, lower_tail], axis=1)
        upper_window = jnp.concatenate([upper_edge, upper_tail], axis=1)
        return lower_window[:, :tail_width] + shift_rows(upper_window, amounts, tail_width)

    partner_head = from_partner(head, "band", 0)
    tail, partner_head = lax.optimization_barrier((tail, partner_head))
    pending = None
    for bit_index in range(bit_count):
        amounts = offsets[local_count + bit_index]
        head_width = head.shape[1] - SHIFT
        upper_half = band_index // 2**bit_index % 2 == 1
        new_head = merge_head(head, partner_head, offsets, local_count + bit_index, upper_half)
        lower_edge, upper_edge = halves(head[:, head_width:], partner_head[:, head_width:], bit_index)
        if bit_index + 1 < bit_count:
            next_partner_head = from_partner(new_head, "band", bit_index + 1)
        if pending is not None:
            waiting, ordered_head = lax.optimization_barrier((pending[1], new_head))
            tail = finish_tail(pending[:1] + (waiting,) + pending[2:])
        partner_tail = from_partner(tail, "band", bit_index)
        if bit_index + 1 < bit_count:
            partner_tail, next_partner_head = lax.optimization_barrier((partner_tail, next_partner_head))
            partner_head = next_partner_head
        pending = (tail, partner_tail, lower_edge, upper_edge, amounts, bit_index)
        head = new_head
    tail = finish_tail(pending)
    current = jnp.concatenate([head, tail], axis=1)
    dedispersed = current * (1.0 / math.sqrt(channels_all))
    detection = boxcar_max(dedispersed, widths)
    peak_series = butterfly(jnp.max(detection, axis=0), "band", jnp.maximum)
    return (detection, peak_series)


def solution(mesh):
    placed = (P(("beam", "band"), None), P(None, "band"), P())
    return jax.shard_map(
        per_device,
        mesh=mesh,
        in_specs=placed,
        out_specs=(P(("beam", "band"), None), P("beam")),
        check_vma=False,
    )
```

```python
import functools
import math

import jax
import jax.numpy as jnp
from jax import lax
from jax.experimental import pallas as pl
from jax.experimental.pallas import tpu as pltpu
from jax.sharding import PartitionSpec as P

TS = 2048
TIN = 6144
SHIFT = 256
TAPS = 128
TEMPLATES = 8
TAIL_WIDTH = 1152


def from_partner(value, axis, distance):
    mask = 2**distance
    pairs = [(source, source ^ mask) for source in range(lax.axis_size(axis))]
    return lax.ppermute(value, axis, pairs)


def from_xor(value, axis, mask):
    pairs = [(source, source ^ mask) for source in range(lax.axis_size(axis))]
    return lax.ppermute(value, axis, pairs)


def butterfly_terms(value, axis, combine):
    bit_count = lax.axis_size(axis).bit_length() - 1
    low_bit = 0
    received = [value]
    while low_bit < bit_count:
        while len(received) > 1:
            received = [combine(received[i], received[i + 1]) for i in range(0, len(received), 2)]
        value = received[0]
        width = min(2, bit_count - low_bit)
        received = [value] + [from_xor(value, axis, k << low_bit) for k in range(1, 2**width)]
        low_bit += width
    return received


def combine_terms(terms, combine):
    while len(terms) > 1:
        terms = [combine(terms[i], terms[i + 1]) for i in range(0, len(terms), 2)]
    return terms[0]


def butterfly(value, axis, combine):
    return combine_terms(butterfly_terms(value, axis, combine), combine)


def shift_rows(trial_rows, amounts, length):
    current = jnp.pad(trial_rows, ((0, 0), (0, 2 * SHIFT)))
    top_bit = (SHIFT - 1).bit_length()
    for bit_index in reversed(range(top_bit)):
        span = 2**bit_index
        keep_len = length + span - 1
        chosen = (amounts >> bit_index & 1)[:, None] == 1
        current = jnp.where(chosen, current[:, span : span + keep_len], current[:, :keep_len])
    return current


def local_tree_kernel(widths_seq, channels_all, term_count, x_ref, *refs):
    term_refs = refs[:term_count]
    offsets_ref, head_ref, tail_ref = refs[term_count:]
    rows = x_ref.shape[0]
    total = combine_terms([ref[:, : widths_seq[0]] for ref in term_refs], jnp.add)
    cur = x_ref[:, : widths_seq[0]] - total / channels_all
    row_id = lax.broadcasted_iota(jnp.int32, (rows, 1), 0)
    diagonal = lax.broadcasted_iota(jnp.int32, (rows, rows), 0) == lax.broadcasted_iota(
        jnp.int32, (rows, rows), 1
    )
    for section_index in range(len(widths_seq) - 1):
        mask = 2**section_index
        width = widths_seq[section_index]
        new_width = widths_seq[section_index + 1]
        is_upper = (row_id & mask) != 0
        from_below = pltpu.roll(cur, rows - mask, axis=0)
        from_above = pltpu.roll(cur, mask, axis=0)
        partner = jnp.where(is_upper, from_above, from_below)
        lower = jnp.where(is_upper, partner, cur)
        shifted = jnp.where(is_upper, cur, partner)
        amount_row = jnp.broadcast_to(offsets_ref[section_index : section_index + 1, :], (rows, rows))
        amount = jnp.sum(jnp.where(diagonal, amount_row, 0), axis=1, keepdims=True)
        for bit_index in range((SHIFT - 1).bit_length()):
            span = 2**bit_index
            chosen = (amount >> bit_index & 1) == 1
            shifted = jnp.where(chosen, pltpu.roll(shifted, width - span, axis=1), shifted)
        cur = lower[:, :new_width] + shifted[:, :new_width]
    head_width = head_ref.shape[1]
    head_ref[...] = cur[:, :head_width]
    tail_ref[...] = cur[:, head_width:]


def local_tree(filterbank, total_terms, offsets, widths_seq, channels_all, tail_width):
    rows = filterbank.shape[0]
    vmem = pl.BlockSpec(memory_space=pltpu.VMEM)
    work = rows * sum(widths_seq[:-1])
    head_width = widths_seq[-1] - tail_width
    return pl.pallas_call(
        functools.partial(local_tree_kernel, tuple(widths_seq), float(channels_all), len(total_terms)),
        out_shape=(
            jax.ShapeDtypeStruct((rows, head_width), jnp.float32),
            jax.ShapeDtypeStruct((rows, tail_width), jnp.float32),
        ),
        in_specs=[vmem] * (len(total_terms) + 2),
        out_specs=(vmem, vmem),
        cost_estimate=pl.CostEstimate(
            flops=40 * work, transcendentals=0, bytes_accessed=4 * (rows * widths_seq[0] + rows * widths_seq[-1])
        ),
    )(filterbank, *total_terms, offsets)


def merge_section(current, offsets_now, section_index, new_length):
    group_trials = 2**section_index
    total_rows = current.shape[0]
    groups = total_rows // (2 * group_trials)
    blocks = current.reshape(groups, 2, group_trials, current.shape[1])
    lower_part = blocks[:, 0, :, :new_length]
    upper_flat = blocks[:, 1].reshape(groups * group_trials, current.shape[1])
    amounts = offsets_now.reshape(groups, 2, group_trials)
    first_half = lower_part + shift_rows(upper_flat, amounts[:, 0].reshape(-1), new_length).reshape(
        groups, group_trials, new_length
    )
    second_half = lower_part + shift_rows(
        upper_flat, amounts[:, 1].reshape(-1), new_length
    ).reshape(groups, group_trials, new_length)
    return jnp.stack([first_half, second_half], axis=1).reshape(total_rows, new_length)


def template_tables(widths):
    source = lax.broadcasted_iota(jnp.int32, (2 * TAPS, TAPS), 0)
    target = lax.broadcasted_iota(jnp.int32, (2 * TAPS, TAPS), 1)
    tap_offset = source - target
    inside = (tap_offset[None] >= 0) & (tap_offset[None] < widths[:, None, None])
    tap_scale = 1.0 / jnp.sqrt(widths.astype(jnp.float32))
    return jnp.where(inside, tap_scale[:, None, None], jnp.zeros((), jnp.float32))


def boxcar_max(dedispersed, widths):
    total_rows = dedispersed.shape[0]
    blocks_time = TS // TAPS
    window = dedispersed.reshape(total_rows, blocks_time + 1, TAPS)
    paired = jnp.concatenate([window[:, :-1], window[:, 1:]], axis=2).reshape(
        total_rows * blocks_time, 2 * TAPS
    )
    tables = template_tables(widths)
    joined = jnp.transpose(tables, (1, 0, 2)).reshape(2 * TAPS, TEMPLATES * TAPS)
    result = jnp.dot(
        paired,
        joined,
        precision=lax.Precision.HIGH,
        preferred_element_type=jnp.float32,
    )
    best_value = jnp.max(result.reshape(total_rows * blocks_time, TEMPLATES, TAPS), axis=1)
    return best_value.reshape(total_rows, TS)


def per_device(filterbank, offsets, widths):
    levels = offsets.shape[0]
    local_count = filterbank.shape[0].bit_length() - 1
    band_count = lax.axis_size("band")
    channels_all = filterbank.shape[0] * band_count

    def length_after(sections_done):
        needed = TS + TAPS + (levels - sections_done) * (SHIFT - 1)
        needed = -(-needed // 128) * 128
        return min(TIN, needed)

    partial_value = jnp.sum(filterbank[:, : length_after(0)], axis=0, keepdims=True)
    total_terms = butterfly_terms(partial_value, "band", jnp.add)
    widths_seq = [length_after(section) for section in range(local_count + 1)]
    head, tail = local_tree(filterbank, total_terms, offsets, widths_seq, channels_all, TAIL_WIDTH)
    band_index = lax.axis_index("band")
    bit_count = band_count.bit_length() - 1
    tail_width = TAIL_WIDTH

    def halves(own, partner, bit_index):
        upper_half = band_index // 2**bit_index % 2 == 1
        return jnp.where(upper_half, partner, own), jnp.where(upper_half, own, partner)

    def finish_tail(pending):
        own_tail, partner_tail, lower_edge, upper_edge, amounts, bit_index = pending
        lower_tail, upper_tail = halves(own_tail, partner_tail, bit_index)
        lower_window = jnp.concatenate([lower_edge, lower_tail], axis=1)
        upper_window = jnp.concatenate([upper_edge, upper_tail], axis=1)
        return lower_window[:, :tail_width] + shift_rows(upper_window, amounts, tail_width)

    partner_head = from_partner(head, "band", 0)
    tail, partner_head = lax.optimization_barrier((tail, partner_head))
    pending = None
    for bit_index in range(bit_count):
        amounts = offsets[local_count + bit_index]
        lower_head, upper_head = halves(head, partner_head, bit_index)
        head_width = head.shape[1] - SHIFT
        new_head = lower_head[:, :head_width] + shift_rows(upper_head, amounts, head_width)
        if bit_index + 1 < bit_count:
            next_partner_head = from_partner(new_head, "band", bit_index + 1)
        if pending is not None:
            waiting, ordered_head = lax.optimization_barrier((pending[1], new_head))
            tail = finish_tail(pending[:1] + (waiting,) + pending[2:])
        partner_tail = from_partner(tail, "band", bit_index)
        if bit_index + 1 < bit_count:
            partner_tail, next_partner_head = lax.optimization_barrier((partner_tail, next_partner_head))
            partner_head = next_partner_head
        pending = (tail, partner_tail, lower_head[:, head_width:], upper_head[:, head_width:], amounts, bit_index)
        head = new_head
    tail = finish_tail(pending)
    current = jnp.concatenate([head, tail], axis=1)
    dedispersed = current * (1.0 / math.sqrt(channels_all))
    detection = boxcar_max(dedispersed, widths)
    peak_series = butterfly(jnp.max(detection, axis=0), "band", jnp.maximum)
    return (detection, peak_series)


def solution(mesh):
    placed = (P(("beam", "band"), None), P(None, "band"), P())
    return jax.shard_map(
        per_device,
        mesh=mesh,
        in_specs=placed,
        out_specs=(P(("beam", "band"), None), P("beam")),
        check_vma=False,
    )
```

```python
import functools
import math

import jax
import jax.numpy as jnp
from jax import lax
from jax.experimental import pallas as pl
from jax.experimental.pallas import tpu as pltpu
from jax.sharding import PartitionSpec as P

TS = 2048
TIN = 6144
SHIFT = 256
TAPS = 128
TEMPLATES = 8
TAIL_WIDTH = 1152


def from_partner(value, axis, distance):
    mask = 2**distance
    pairs = [(source, source ^ mask) for source in range(lax.axis_size(axis))]
    return lax.ppermute(value, axis, pairs)


def from_xor(value, axis, mask):
    pairs = [(source, source ^ mask) for source in range(lax.axis_size(axis))]
    return lax.ppermute(value, axis, pairs)


def butterfly_terms(value, axis, combine):
    bit_count = lax.axis_size(axis).bit_length() - 1
    low_bit = 0
    received = [value]
    while low_bit < bit_count:
        while len(received) > 1:
            received = [combine(received[i], received[i + 1]) for i in range(0, len(received), 2)]
        value = received[0]
        width = min(2, bit_count - low_bit)
        received = [value] + [from_xor(value, axis, k << low_bit) for k in range(1, 2**width)]
        low_bit += width
    return received


def combine_terms(terms, combine):
    while len(terms) > 1:
        terms = [combine(terms[i], terms[i + 1]) for i in range(0, len(terms), 2)]
    return terms[0]


def butterfly(value, axis, combine):
    return combine_terms(butterfly_terms(value, axis, combine), combine)


def shift_rows(trial_rows, amounts, length):
    current = jnp.pad(trial_rows, ((0, 0), (0, 2 * SHIFT)))
    top_bit = (SHIFT - 1).bit_length()
    for bit_index in reversed(range(top_bit)):
        span = 2**bit_index
        keep_len = length + span - 1
        chosen = (amounts >> bit_index & 1)[:, None] == 1
        current = jnp.where(chosen, current[:, span : span + keep_len], current[:, :keep_len])
    return current


def local_tree_kernel(widths_seq, channels_all, term_count, x_ref, *refs):
    term_refs = refs[:term_count]
    offsets_ref, head_ref, tail_ref = refs[term_count:]
    rows = x_ref.shape[0]
    total = combine_terms([ref[:, : widths_seq[0]] for ref in term_refs], jnp.add)
    cur = x_ref[:, : widths_seq[0]] - total / channels_all
    row_id = lax.broadcasted_iota(jnp.int32, (rows, 1), 0)
    diagonal = lax.broadcasted_iota(jnp.int32, (rows, rows), 0) == lax.broadcasted_iota(
        jnp.int32, (rows, rows), 1
    )
    for section_index in range(len(widths_seq) - 1):
        mask = 2**section_index
        width = widths_seq[section_index]
        new_width = widths_seq[section_index + 1]
        is_upper = (row_id & mask) != 0
        from_below = pltpu.roll(cur, rows - mask, axis=0)
        from_above = pltpu.roll(cur, mask, axis=0)
        partner = jnp.where(is_upper, from_above, from_below)
        lower = jnp.where(is_upper, partner, cur)
        shifted = jnp.where(is_upper, cur, partner)
        amount_row = jnp.broadcast_to(offsets_ref[section_index : section_index + 1, :], (rows, rows))
        amount = jnp.sum(jnp.where(diagonal, amount_row, 0), axis=1, keepdims=True)
        for bit_index in range((SHIFT - 1).bit_length()):
            span = 2**bit_index
            chosen = (amount >> bit_index & 1) == 1
            shifted = jnp.where(chosen, pltpu.roll(shifted, width - span, axis=1), shifted)
        cur = lower[:, :new_width] + shifted[:, :new_width]
    head_width = head_ref.shape[1]
    head_ref[...] = cur[:, :head_width]
    tail_ref[...] = cur[:, head_width:]


def local_tree(filterbank, total_terms, offsets, widths_seq, channels_all, tail_width):
    rows = filterbank.shape[0]
    vmem = pl.BlockSpec(memory_space=pltpu.VMEM)
    work = rows * sum(widths_seq[:-1])
    head_width = widths_seq[-1] - tail_width
    return pl.pallas_call(
        functools.partial(local_tree_kernel, tuple(widths_seq), float(channels_all), len(total_terms)),
        out_shape=(
            jax.ShapeDtypeStruct((rows, head_width), jnp.float32),
            jax.ShapeDtypeStruct((rows, tail_width), jnp.float32),
        ),
        in_specs=[vmem] * (len(total_terms) + 2),
        out_specs=(vmem, vmem),
        cost_estimate=pl.CostEstimate(
            flops=40 * work, transcendentals=0, bytes_accessed=4 * (rows * widths_seq[0] + rows * widths_seq[-1])
        ),
    )(filterbank, *total_terms, offsets)


def merge_section(current, offsets_now, section_index, new_length):
    group_trials = 2**section_index
    total_rows = current.shape[0]
    groups = total_rows // (2 * group_trials)
    blocks = current.reshape(groups, 2, group_trials, current.shape[1])
    lower_part = blocks[:, 0, :, :new_length]
    upper_flat = blocks[:, 1].reshape(groups * group_trials, current.shape[1])
    amounts = offsets_now.reshape(groups, 2, group_trials)
    first_half = lower_part + shift_rows(upper_flat, amounts[:, 0].reshape(-1), new_length).reshape(
        groups, group_trials, new_length
    )
    second_half = lower_part + shift_rows(
        upper_flat, amounts[:, 1].reshape(-1), new_length
    ).reshape(groups, group_trials, new_length)
    return jnp.stack([first_half, second_half], axis=1).reshape(total_rows, new_length)


def template_tables(widths):
    source = lax.broadcasted_iota(jnp.int32, (2 * TAPS, TAPS), 0)
    target = lax.broadcasted_iota(jnp.int32, (2 * TAPS, TAPS), 1)
    tap_offset = source - target
    inside = (tap_offset[None] >= 0) & (tap_offset[None] < widths[:, None, None])
    tap_scale = 1.0 / jnp.sqrt(widths.astype(jnp.float32))
    return jnp.where(inside, tap_scale[:, None, None], jnp.zeros((), jnp.float32))


def boxcar_max(dedispersed, widths):
    total_rows = dedispersed.shape[0]
    blocks_time = TS // TAPS
    window = dedispersed.reshape(total_rows, blocks_time + 1, TAPS)
    paired = jnp.concatenate([window[:, :-1], window[:, 1:]], axis=2).reshape(
        total_rows * blocks_time, 2 * TAPS
    )
    tables = template_tables(widths)
    joined = jnp.transpose(tables, (1, 0, 2)).reshape(2 * TAPS, TEMPLATES * TAPS)
    result = jnp.dot(
        paired,
        joined,
        precision=lax.Precision.HIGH,
        preferred_element_type=jnp.float32,
    )
    best_value = jnp.max(result.reshape(total_rows * blocks_time, TEMPLATES, TAPS), axis=1)
    return best_value.reshape(total_rows, TS)


def per_device(filterbank, offsets, widths):
    levels = offsets.shape[0]
    local_count = filterbank.shape[0].bit_length() - 1
    band_count = lax.axis_size("band")
    channels_all = filterbank.shape[0] * band_count

    def length_after(sections_done):
        needed = TS + TAPS + (levels - sections_done) * (SHIFT - 1)
        needed = -(-needed // 128) * 128
        return min(TIN, needed)

    needed = filterbank[:, : length_after(0)]
    stage = jnp.sum(needed.reshape(-1, 8, needed.shape[1]), axis=0)
    stage = lax.optimization_barrier(stage)
    partial_value = jnp.sum(stage, axis=0, keepdims=True)
    total_terms = butterfly_terms(partial_value, "band", jnp.add)
    widths_seq = [length_after(section) for section in range(local_count + 1)]
    head, tail = local_tree(filterbank, total_terms, offsets, widths_seq, channels_all, TAIL_WIDTH)
    band_index = lax.axis_index("band")
    bit_count = band_count.bit_length() - 1
    tail_width = TAIL_WIDTH

    def halves(own, partner, bit_index):
        upper_half = band_index // 2**bit_index % 2 == 1
        return jnp.where(upper_half, partner, own), jnp.where(upper_half, own, partner)

    def finish_tail(pending):
        own_tail, partner_tail, lower_edge, upper_edge, amounts, bit_index = pending
        lower_tail, upper_tail = halves(own_tail, partner_tail, bit_index)
        lower_window = jnp.concatenate([lower_edge, lower_tail], axis=1)
        upper_window = jnp.concatenate([upper_edge, upper_tail], axis=1)
        return lower_window[:, :tail_width] + shift_rows(upper_window, amounts, tail_width)

    partner_head = from_partner(head, "band", 0)
    tail, partner_head = lax.optimization_barrier((tail, partner_head))
    pending = None
    for bit_index in range(bit_count):
        amounts = offsets[local_count + bit_index]
        lower_head, upper_head = halves(head, partner_head, bit_index)
        head_width = head.shape[1] - SHIFT
        new_head = lower_head[:, :head_width] + shift_rows(upper_head, amounts, head_width)
        if bit_index + 1 < bit_count:
            next_partner_head = from_partner(new_head, "band", bit_index + 1)
        if pending is not None:
            waiting, ordered_head = lax.optimization_barrier((pending[1], new_head))
            tail = finish_tail(pending[:1] + (waiting,) + pending[2:])
        partner_tail = from_partner(tail, "band", bit_index)
        if bit_index + 1 < bit_count:
            partner_tail, next_partner_head = lax.optimization_barrier((partner_tail, next_partner_head))
            partner_head = next_partner_head
        pending = (tail, partner_tail, lower_head[:, head_width:], upper_head[:, head_width:], amounts, bit_index)
        head = new_head
    tail = finish_tail(pending)
    current = jnp.concatenate([head, tail], axis=1)
    dedispersed = current * (1.0 / math.sqrt(channels_all))
    detection = boxcar_max(dedispersed, widths)
    peak_series = butterfly(jnp.max(detection, axis=0), "band", jnp.maximum)
    return (detection, peak_series)


def solution(mesh):
    placed = (P(("beam", "band"), None), P(None, "band"), P())
    return jax.shard_map(
        per_device,
        mesh=mesh,
        in_specs=placed,
        out_specs=(P(("beam", "band"), None), P("beam")),
        check_vma=False,
    )
```

```python
import functools
import math

import jax
import jax.numpy as jnp
from jax import lax
from jax.experimental import pallas as pl
from jax.experimental.pallas import tpu as pltpu
from jax.sharding import PartitionSpec as P

TS = 2048
TIN = 6144
SHIFT = 256
TAPS = 128
TEMPLATES = 8
TAIL_WIDTH = 1152


def from_partner(value, axis, distance):
    mask = 2**distance
    pairs = [(source, source ^ mask) for source in range(lax.axis_size(axis))]
    return lax.ppermute(value, axis, pairs)


def from_xor(value, axis, mask):
    pairs = [(source, source ^ mask) for source in range(lax.axis_size(axis))]
    return lax.ppermute(value, axis, pairs)


def butterfly_terms(value, axis, combine):
    bit_count = lax.axis_size(axis).bit_length() - 1
    low_bit = 0
    received = [value]
    while low_bit < bit_count:
        while len(received) > 1:
            received = [combine(received[i], received[i + 1]) for i in range(0, len(received), 2)]
        value = received[0]
        width = min(2, bit_count - low_bit)
        received = [value] + [from_xor(value, axis, k << low_bit) for k in range(1, 2**width)]
        low_bit += width
    return received


def combine_terms(terms, combine):
    while len(terms) > 1:
        terms = [combine(terms[i], terms[i + 1]) for i in range(0, len(terms), 2)]
    return terms[0]


def butterfly(value, axis, combine):
    return combine_terms(butterfly_terms(value, axis, combine), combine)


def shift_rows(trial_rows, amounts, length):
    current = jnp.pad(trial_rows, ((0, 0), (0, 2 * SHIFT)))
    top_bit = (SHIFT - 1).bit_length()
    for bit_index in reversed(range(top_bit)):
        span = 2**bit_index
        keep_len = length + span - 1
        chosen = (amounts >> bit_index & 1)[:, None] == 1
        current = jnp.where(chosen, current[:, span : span + keep_len], current[:, :keep_len])
    return current


def local_tree_kernel(widths_seq, channels_all, term_count, column, x_ref, *refs):
    term_refs = refs[:term_count]
    offsets_ref, out_ref = refs[term_count:]
    rows = x_ref.shape[0]
    window = pl.ds(column, widths_seq[0])
    total = combine_terms([ref[:, window] for ref in term_refs], jnp.add)
    cur = x_ref[:, window] - total / channels_all
    row_id = lax.broadcasted_iota(jnp.int32, (rows, 1), 0)
    diagonal = lax.broadcasted_iota(jnp.int32, (rows, rows), 0) == lax.broadcasted_iota(
        jnp.int32, (rows, rows), 1
    )
    for section_index in range(len(widths_seq) - 1):
        mask = 2**section_index
        width = widths_seq[section_index]
        new_width = widths_seq[section_index + 1]
        is_upper = (row_id & mask) != 0
        from_below = pltpu.roll(cur, rows - mask, axis=0)
        from_above = pltpu.roll(cur, mask, axis=0)
        partner = jnp.where(is_upper, from_above, from_below)
        lower = jnp.where(is_upper, partner, cur)
        shifted = jnp.where(is_upper, cur, partner)
        amount_row = jnp.broadcast_to(offsets_ref[section_index : section_index + 1, :], (rows, rows))
        amount = jnp.sum(jnp.where(diagonal, amount_row, 0), axis=1, keepdims=True)
        for bit_index in range((SHIFT - 1).bit_length()):
            span = 2**bit_index
            chosen = (amount >> bit_index & 1) == 1
            shifted = jnp.where(chosen, pltpu.roll(shifted, width - span, axis=1), shifted)
        cur = lower[:, :new_width] + shifted[:, :new_width]
    out_ref[...] = cur


def local_tree(filterbank, total_terms, offsets, widths_seq, channels_all, column):
    rows = filterbank.shape[0]
    vmem = pl.BlockSpec(memory_space=pltpu.VMEM)
    work = rows * sum(widths_seq[:-1])
    return pl.pallas_call(
        functools.partial(local_tree_kernel, tuple(widths_seq), float(channels_all), len(total_terms), column),
        out_shape=jax.ShapeDtypeStruct((rows, widths_seq[-1]), jnp.float32),
        in_specs=[vmem] * (len(total_terms) + 2),
        out_specs=vmem,
        cost_estimate=pl.CostEstimate(
            flops=40 * work, transcendentals=0, bytes_accessed=4 * (rows * widths_seq[0] + rows * widths_seq[-1])
        ),
    )(filterbank, *total_terms, offsets)


def merge_section(current, offsets_now, section_index, new_length):
    group_trials = 2**section_index
    total_rows = current.shape[0]
    groups = total_rows // (2 * group_trials)
    blocks = current.reshape(groups, 2, group_trials, current.shape[1])
    lower_part = blocks[:, 0, :, :new_length]
    upper_flat = blocks[:, 1].reshape(groups * group_trials, current.shape[1])
    amounts = offsets_now.reshape(groups, 2, group_trials)
    first_half = lower_part + shift_rows(upper_flat, amounts[:, 0].reshape(-1), new_length).reshape(
        groups, group_trials, new_length
    )
    second_half = lower_part + shift_rows(
        upper_flat, amounts[:, 1].reshape(-1), new_length
    ).reshape(groups, group_trials, new_length)
    return jnp.stack([first_half, second_half], axis=1).reshape(total_rows, new_length)


def template_tables(widths):
    source = lax.broadcasted_iota(jnp.int32, (2 * TAPS, TAPS), 0)
    target = lax.broadcasted_iota(jnp.int32, (2 * TAPS, TAPS), 1)
    tap_offset = source - target
    inside = (tap_offset[None] >= 0) & (tap_offset[None] < widths[:, None, None])
    tap_scale = 1.0 / jnp.sqrt(widths.astype(jnp.float32))
    return jnp.where(inside, tap_scale[:, None, None], jnp.zeros((), jnp.float32))


def boxcar_max(dedispersed, widths):
    total_rows = dedispersed.shape[0]
    blocks_time = TS // TAPS
    window = dedispersed.reshape(total_rows, blocks_time + 1, TAPS)
    paired = jnp.concatenate([window[:, :-1], window[:, 1:]], axis=2).reshape(
        total_rows * blocks_time, 2 * TAPS
    )
    tables = template_tables(widths)
    joined = jnp.transpose(tables, (1, 0, 2)).reshape(2 * TAPS, TEMPLATES * TAPS)
    result = jnp.dot(
        paired,
        joined,
        precision=lax.Precision.HIGH,
        preferred_element_type=jnp.float32,
    )
    best_value = jnp.max(result.reshape(total_rows * blocks_time, TEMPLATES, TAPS), axis=1)
    return best_value.reshape(total_rows, TS)


def per_device(filterbank, offsets, widths):
    levels = offsets.shape[0]
    local_count = filterbank.shape[0].bit_length() - 1
    band_count = lax.axis_size("band")
    channels_all = filterbank.shape[0] * band_count

    def length_after(sections_done):
        needed = TS + TAPS + (levels - sections_done) * (SHIFT - 1)
        needed = -(-needed // 128) * 128
        return min(TIN, needed)

    partial_value = jnp.sum(filterbank[:, : length_after(0)], axis=0, keepdims=True)
    total_terms = butterfly_terms(partial_value, "band", jnp.add)
    widths_seq = [length_after(section) for section in range(local_count + 1)]
    head_widths = [width - widths_seq[-1] + (widths_seq[-1] - TAIL_WIDTH) for width in widths_seq]
    tail_widths = [width - (widths_seq[-1] - TAIL_WIDTH) for width in widths_seq]
    head = local_tree(filterbank, total_terms, offsets, head_widths, channels_all, 0)
    band_index = lax.axis_index("band")
    bit_count = band_count.bit_length() - 1
    tail_width = TAIL_WIDTH

    def halves(own, partner, bit_index):
        upper_half = band_index // 2**bit_index % 2 == 1
        return jnp.where(upper_half, partner, own), jnp.where(upper_half, own, partner)

    def finish_tail(pending):
        own_tail, partner_tail, lower_edge, upper_edge, amounts, bit_index = pending
        lower_tail, upper_tail = halves(own_tail, partner_tail, bit_index)
        lower_window = jnp.concatenate([lower_edge, lower_tail], axis=1)
        upper_window = jnp.concatenate([upper_edge, upper_tail], axis=1)
        return lower_window[:, :tail_width] + shift_rows(upper_window, amounts, tail_width)

    partner_head = from_partner(head, "band", 0)
    pending = None
    for bit_index in range(bit_count):
        amounts = offsets[local_count + bit_index]
        lower_head, upper_head = halves(head, partner_head, bit_index)
        head_width = head.shape[1] - SHIFT
        new_head = lower_head[:, :head_width] + shift_rows(upper_head, amounts, head_width)
        if bit_index + 1 < bit_count:
            next_partner_head = from_partner(new_head, "band", bit_index + 1)
        if bit_index == 0:
            late_input, new_head = lax.optimization_barrier((filterbank, new_head))
            tail = local_tree(
                late_input, total_terms, offsets, tail_widths, channels_all, widths_seq[-1] - TAIL_WIDTH
            )
        if pending is not None:
            waiting, ordered_head = lax.optimization_barrier((pending[1], new_head))
            tail = finish_tail(pending[:1] + (waiting,) + pending[2:])
        partner_tail = from_partner(tail, "band", bit_index)
        if bit_index + 1 < bit_count:
            partner_tail, next_partner_head = lax.optimization_barrier((partner_tail, next_partner_head))
            partner_head = next_partner_head
        pending = (tail, partner_tail, lower_head[:, head_width:], upper_head[:, head_width:], amounts, bit_index)
        head = new_head
    tail = finish_tail(pending)
    current = jnp.concatenate([head, tail], axis=1)
    dedispersed = current * (1.0 / math.sqrt(channels_all))
    detection = boxcar_max(dedispersed, widths)
    peak_series = butterfly(jnp.max(detection, axis=0), "band", jnp.maximum)
    return (detection, peak_series)


def solution(mesh):
    placed = (P(("beam", "band"), None), P(None, "band"), P())
    return jax.shard_map(
        per_device,
        mesh=mesh,
        in_specs=placed,
        out_specs=(P(("beam", "band"), None), P("beam")),
        check_vma=False,
    )
```

```python
import functools
import math

import jax
import jax.numpy as jnp
from jax import lax
from jax.experimental import pallas as pl
from jax.experimental.pallas import tpu as pltpu
from jax.sharding import PartitionSpec as P

TS = 2048
TIN = 6144
SHIFT = 256
TAPS = 128
TEMPLATES = 8
TAIL_WIDTH = 1280


def from_partner(value, axis, distance):
    mask = 2**distance
    pairs = [(source, source ^ mask) for source in range(lax.axis_size(axis))]
    return lax.ppermute(value, axis, pairs)


def from_xor(value, axis, mask):
    pairs = [(source, source ^ mask) for source in range(lax.axis_size(axis))]
    return lax.ppermute(value, axis, pairs)


def butterfly_terms(value, axis, combine):
    bit_count = lax.axis_size(axis).bit_length() - 1
    low_bit = 0
    received = [value]
    while low_bit < bit_count:
        while len(received) > 1:
            received = [combine(received[i], received[i + 1]) for i in range(0, len(received), 2)]
        value = received[0]
        width = min(2, bit_count - low_bit)
        received = [value] + [from_xor(value, axis, k << low_bit) for k in range(1, 2**width)]
        low_bit += width
    return received


def combine_terms(terms, combine):
    while len(terms) > 1:
        terms = [combine(terms[i], terms[i + 1]) for i in range(0, len(terms), 2)]
    return terms[0]


def butterfly(value, axis, combine):
    return combine_terms(butterfly_terms(value, axis, combine), combine)


def shift_rows(trial_rows, amounts, length):
    current = jnp.pad(trial_rows, ((0, 0), (0, 2 * SHIFT)))
    top_bit = (SHIFT - 1).bit_length()
    for bit_index in reversed(range(top_bit)):
        span = 2**bit_index
        keep_len = length + span - 1
        chosen = (amounts >> bit_index & 1)[:, None] == 1
        current = jnp.where(chosen, current[:, span : span + keep_len], current[:, :keep_len])
    return current


def local_tree_kernel(widths_seq, channels_all, term_count, x_ref, *refs):
    term_refs = refs[:term_count]
    offsets_ref, head_ref, tail_ref = refs[term_count:]
    rows = x_ref.shape[0]
    total = combine_terms([ref[:, : widths_seq[0]] for ref in term_refs], jnp.add)
    cur = x_ref[:, : widths_seq[0]] - total / channels_all
    row_id = lax.broadcasted_iota(jnp.int32, (rows, 1), 0)
    diagonal = lax.broadcasted_iota(jnp.int32, (rows, rows), 0) == lax.broadcasted_iota(
        jnp.int32, (rows, rows), 1
    )
    for section_index in range(len(widths_seq) - 1):
        mask = 2**section_index
        width = widths_seq[section_index]
        new_width = widths_seq[section_index + 1]
        is_upper = (row_id & mask) != 0
        from_below = pltpu.roll(cur, rows - mask, axis=0)
        from_above = pltpu.roll(cur, mask, axis=0)
        partner = jnp.where(is_upper, from_above, from_below)
        lower = jnp.where(is_upper, partner, cur)
        shifted = jnp.where(is_upper, cur, partner)
        amount_row = jnp.broadcast_to(offsets_ref[section_index : section_index + 1, :], (rows, rows))
        amount = jnp.sum(jnp.where(diagonal, amount_row, 0), axis=1, keepdims=True)
        for bit_index in range((SHIFT - 1).bit_length()):
            span = 2**bit_index
            chosen = (amount >> bit_index & 1) == 1
            shifted = jnp.where(chosen, pltpu.roll(shifted, width - span, axis=1), shifted)
        cur = lower[:, :new_width] + shifted[:, :new_width]
    head_width = head_ref.shape[1]
    head_ref[...] = cur[:, :head_width]
    tail_ref[...] = cur[:, head_width:]


def local_tree(filterbank, total_terms, offsets, widths_seq, channels_all, tail_width):
    rows = filterbank.shape[0]
    vmem = pl.BlockSpec(memory_space=pltpu.VMEM)
    work = rows * sum(widths_seq[:-1])
    head_width = widths_seq[-1] - tail_width
    return pl.pallas_call(
        functools.partial(local_tree_kernel, tuple(widths_seq), float(channels_all), len(total_terms)),
        out_shape=(
            jax.ShapeDtypeStruct((rows, head_width), jnp.float32),
            jax.ShapeDtypeStruct((rows, tail_width), jnp.float32),
        ),
        in_specs=[vmem] * (len(total_terms) + 2),
        out_specs=(vmem, vmem),
        cost_estimate=pl.CostEstimate(
            flops=40 * work, transcendentals=0, bytes_accessed=4 * (rows * widths_seq[0] + rows * widths_seq[-1])
        ),
    )(filterbank, *total_terms, offsets)


def merge_section(current, offsets_now, section_index, new_length):
    group_trials = 2**section_index
    total_rows = current.shape[0]
    groups = total_rows // (2 * group_trials)
    blocks = current.reshape(groups, 2, group_trials, current.shape[1])
    lower_part = blocks[:, 0, :, :new_length]
    upper_flat = blocks[:, 1].reshape(groups * group_trials, current.shape[1])
    amounts = offsets_now.reshape(groups, 2, group_trials)
    first_half = lower_part + shift_rows(upper_flat, amounts[:, 0].reshape(-1), new_length).reshape(
        groups, group_trials, new_length
    )
    second_half = lower_part + shift_rows(
        upper_flat, amounts[:, 1].reshape(-1), new_length
    ).reshape(groups, group_trials, new_length)
    return jnp.stack([first_half, second_half], axis=1).reshape(total_rows, new_length)


def template_tables(widths):
    source = lax.broadcasted_iota(jnp.int32, (2 * TAPS, TAPS), 0)
    target = lax.broadcasted_iota(jnp.int32, (2 * TAPS, TAPS), 1)
    tap_offset = source - target
    inside = (tap_offset[None] >= 0) & (tap_offset[None] < widths[:, None, None])
    tap_scale = 1.0 / jnp.sqrt(widths.astype(jnp.float32))
    return jnp.where(inside, tap_scale[:, None, None], jnp.zeros((), jnp.float32))


def boxcar_max(dedispersed, widths):
    total_rows = dedispersed.shape[0]
    blocks_time = TS // TAPS
    window = dedispersed.reshape(total_rows, blocks_time + 1, TAPS)
    paired = jnp.concatenate([window[:, :-1], window[:, 1:]], axis=2).reshape(
        total_rows * blocks_time, 2 * TAPS
    )
    tables = template_tables(widths)
    joined = jnp.transpose(tables, (1, 0, 2)).reshape(2 * TAPS, TEMPLATES * TAPS)
    result = jnp.dot(
        paired,
        joined,
        precision=lax.Precision.HIGH,
        preferred_element_type=jnp.float32,
    )
    best_value = jnp.max(result.reshape(total_rows * blocks_time, TEMPLATES, TAPS), axis=1)
    return best_value.reshape(total_rows, TS)


def per_device(filterbank, offsets, widths):
    levels = offsets.shape[0]
    local_count = filterbank.shape[0].bit_length() - 1
    band_count = lax.axis_size("band")
    channels_all = filterbank.shape[0] * band_count

    def length_after(sections_done):
        needed = TS + TAPS + (levels - sections_done) * (SHIFT - 1)
        needed = -(-needed // 128) * 128
        return min(TIN, needed)

    partial_value = jnp.sum(filterbank[:, : length_after(0)], axis=0, keepdims=True)
    total_terms = butterfly_terms(partial_value, "band", jnp.add)
    widths_seq = [length_after(section) for section in range(local_count + 1)]
    head, tail = local_tree(filterbank, total_terms, offsets, widths_seq, channels_all, TAIL_WIDTH)
    band_index = lax.axis_index("band")
    bit_count = band_count.bit_length() - 1
    tail_width = TAIL_WIDTH

    def halves(own, partner, bit_index):
        upper_half = band_index // 2**bit_index % 2 == 1
        return jnp.where(upper_half, partner, own), jnp.where(upper_half, own, partner)

    def finish_tail(pending):
        own_tail, partner_tail, lower_edge, upper_edge, amounts, bit_index = pending
        lower_tail, upper_tail = halves(own_tail, partner_tail, bit_index)
        lower_window = jnp.concatenate([lower_edge, lower_tail], axis=1)
        upper_window = jnp.concatenate([upper_edge, upper_tail], axis=1)
        return lower_window[:, :tail_width] + shift_rows(upper_window, amounts, tail_width)

    partner_head = from_partner(head, "band", 0)
    tail, partner_head = lax.optimization_barrier((tail, partner_head))
    pending = None
    for bit_index in range(bit_count):
        amounts = offsets[local_count + bit_index]
        lower_head, upper_head = halves(head, partner_head, bit_index)
        head_width = head.shape[1] - SHIFT
        new_head = lower_head[:, :head_width] + shift_rows(upper_head, amounts, head_width)
        if bit_index + 1 < bit_count:
            next_partner_head = from_partner(new_head, "band", bit_index + 1)
        if pending is not None:
            waiting, ordered_head = lax.optimization_barrier((pending[1], new_head))
            tail = finish_tail(pending[:1] + (waiting,) + pending[2:])
        partner_tail = from_partner(tail, "band", bit_index)
        if bit_index + 1 < bit_count:
            partner_tail, next_partner_head = lax.optimization_barrier((partner_tail, next_partner_head))
            partner_head = next_partner_head
        pending = (tail, partner_tail, lower_head[:, head_width:], upper_head[:, head_width:], amounts, bit_index)
        head = new_head
    tail = finish_tail(pending)
    current = jnp.concatenate([head, tail], axis=1)
    dedispersed = current * (1.0 / math.sqrt(channels_all))
    detection = boxcar_max(dedispersed, widths)
    peak_series = butterfly(jnp.max(detection, axis=0), "band", jnp.maximum)
    return (detection, peak_series)


def solution(mesh):
    placed = (P(("beam", "band"), None), P(None, "band"), P())
    return jax.shard_map(
        per_device,
        mesh=mesh,
        in_specs=placed,
        out_specs=(P(("beam", "band"), None), P("beam")),
        check_vma=False,
    )
```

```python
import functools
import math

import jax
import jax.numpy as jnp
from jax import lax
from jax.experimental import pallas as pl
from jax.experimental.pallas import tpu as pltpu
from jax.sharding import PartitionSpec as P

TS = 2048
TIN = 6144
SHIFT = 256
TAPS = 128
TEMPLATES = 8
TAIL_WIDTH = 1152


def from_partner(value, axis, distance):
    mask = 2**distance
    pairs = [(source, source ^ mask) for source in range(lax.axis_size(axis))]
    return lax.ppermute(value, axis, pairs)


def from_xor(value, axis, mask):
    pairs = [(source, source ^ mask) for source in range(lax.axis_size(axis))]
    return lax.ppermute(value, axis, pairs)


def butterfly_terms(value, axis, combine):
    bit_count = lax.axis_size(axis).bit_length() - 1
    low_bit = 0
    received = [value]
    while low_bit < bit_count:
        while len(received) > 1:
            received = [combine(received[i], received[i + 1]) for i in range(0, len(received), 2)]
        value = received[0]
        width = min(2, bit_count - low_bit)
        received = [value] + [from_xor(value, axis, k << low_bit) for k in range(1, 2**width)]
        low_bit += width
    return received


def combine_terms(terms, combine):
    while len(terms) > 1:
        terms = [combine(terms[i], terms[i + 1]) for i in range(0, len(terms), 2)]
    return terms[0]


def butterfly(value, axis, combine):
    return combine_terms(butterfly_terms(value, axis, combine), combine)


def shift_rows(trial_rows, amounts, length):
    current = jnp.pad(trial_rows, ((0, 0), (0, 2 * SHIFT)))
    top_bit = (SHIFT - 1).bit_length()
    for bit_index in reversed(range(top_bit)):
        span = 2**bit_index
        keep_len = length + span - 1
        chosen = (amounts >> bit_index & 1)[:, None] == 1
        current = jnp.where(chosen, current[:, span : span + keep_len], current[:, :keep_len])
    return current


def local_tree_kernel(widths_seq, channels_all, term_count, x_ref, *refs):
    term_refs = refs[:term_count]
    offsets_ref, head_ref, tail_ref = refs[term_count:]
    rows = x_ref.shape[0]
    total = combine_terms([ref[:, : widths_seq[0]] for ref in term_refs], jnp.add)
    cur = x_ref[:, : widths_seq[0]] - total / channels_all
    row_id = lax.broadcasted_iota(jnp.int32, (rows, 1), 0)
    diagonal = lax.broadcasted_iota(jnp.int32, (rows, rows), 0) == lax.broadcasted_iota(
        jnp.int32, (rows, rows), 1
    )
    for section_index in range(len(widths_seq) - 1):
        mask = 2**section_index
        width = widths_seq[section_index]
        new_width = widths_seq[section_index + 1]
        is_upper = (row_id & mask) != 0
        from_below = pltpu.roll(cur, rows - mask, axis=0)
        from_above = pltpu.roll(cur, mask, axis=0)
        partner = jnp.where(is_upper, from_above, from_below)
        lower = jnp.where(is_upper, partner, cur)
        shifted = jnp.where(is_upper, cur, partner)
        amount_row = jnp.broadcast_to(offsets_ref[section_index : section_index + 1, :], (rows, rows))
        amount = jnp.sum(jnp.where(diagonal, amount_row, 0), axis=1, keepdims=True)
        for bit_index in range((SHIFT - 1).bit_length()):
            span = 2**bit_index
            chosen = (amount >> bit_index & 1) == 1
            shifted = jnp.where(chosen, pltpu.roll(shifted, width - span, axis=1), shifted)
        cur = lower[:, :new_width] + shifted[:, :new_width]
    head_width = head_ref.shape[1]
    head_ref[...] = cur[:, :head_width]
    tail_ref[...] = cur[:, head_width:]


def local_tree(filterbank, total_terms, offsets, widths_seq, channels_all, tail_width):
    rows = filterbank.shape[0]
    vmem = pl.BlockSpec(memory_space=pltpu.VMEM)
    work = rows * sum(widths_seq[:-1])
    head_width = widths_seq[-1] - tail_width
    return pl.pallas_call(
        functools.partial(local_tree_kernel, tuple(widths_seq), float(channels_all), len(total_terms)),
        out_shape=(
            jax.ShapeDtypeStruct((rows, head_width), jnp.float32),
            jax.ShapeDtypeStruct((rows, tail_width), jnp.float32),
        ),
        in_specs=[vmem] * (len(total_terms) + 2),
        out_specs=(vmem, vmem),
        cost_estimate=pl.CostEstimate(
            flops=40 * work, transcendentals=0, bytes_accessed=4 * (rows * widths_seq[0] + rows * widths_seq[-1])
        ),
    )(filterbank, *total_terms, offsets)


def merge_section(current, offsets_now, section_index, new_length):
    group_trials = 2**section_index
    total_rows = current.shape[0]
    groups = total_rows // (2 * group_trials)
    blocks = current.reshape(groups, 2, group_trials, current.shape[1])
    lower_part = blocks[:, 0, :, :new_length]
    upper_flat = blocks[:, 1].reshape(groups * group_trials, current.shape[1])
    amounts = offsets_now.reshape(groups, 2, group_trials)
    first_half = lower_part + shift_rows(upper_flat, amounts[:, 0].reshape(-1), new_length).reshape(
        groups, group_trials, new_length
    )
    second_half = lower_part + shift_rows(
        upper_flat, amounts[:, 1].reshape(-1), new_length
    ).reshape(groups, group_trials, new_length)
    return jnp.stack([first_half, second_half], axis=1).reshape(total_rows, new_length)


def template_tables(widths):
    source = lax.broadcasted_iota(jnp.int32, (2 * TAPS, TAPS), 0)
    target = lax.broadcasted_iota(jnp.int32, (2 * TAPS, TAPS), 1)
    tap_offset = source - target
    inside = (tap_offset[None] >= 0) & (tap_offset[None] < widths[:, None, None])
    tap_scale = 1.0 / jnp.sqrt(widths.astype(jnp.float32))
    return jnp.where(inside, tap_scale[:, None, None], jnp.zeros((), jnp.float32))


def boxcar_max(dedispersed, widths):
    total_rows = dedispersed.shape[0]
    blocks_time = dedispersed.shape[1] // TAPS - 1
    window = dedispersed.reshape(total_rows, blocks_time + 1, TAPS)
    paired = jnp.concatenate([window[:, :-1], window[:, 1:]], axis=2).reshape(
        total_rows * blocks_time, 2 * TAPS
    )
    tables = template_tables(widths)
    joined = jnp.transpose(tables, (1, 0, 2)).reshape(2 * TAPS, TEMPLATES * TAPS)
    result = jnp.dot(
        paired,
        joined,
        precision=lax.Precision.HIGH,
        preferred_element_type=jnp.float32,
    )
    best_value = jnp.max(result.reshape(total_rows * blocks_time, TEMPLATES, TAPS), axis=1)
    return best_value.reshape(total_rows, blocks_time * TAPS)


def per_device(filterbank, offsets, widths):
    levels = offsets.shape[0]
    local_count = filterbank.shape[0].bit_length() - 1
    band_count = lax.axis_size("band")
    channels_all = filterbank.shape[0] * band_count

    def length_after(sections_done):
        needed = TS + TAPS + (levels - sections_done) * (SHIFT - 1)
        needed = -(-needed // 128) * 128
        return min(TIN, needed)

    partial_value = jnp.sum(filterbank[:, : length_after(0)], axis=0, keepdims=True)
    total_terms = butterfly_terms(partial_value, "band", jnp.add)
    widths_seq = [length_after(section) for section in range(local_count + 1)]
    head, tail = local_tree(filterbank, total_terms, offsets, widths_seq, channels_all, TAIL_WIDTH)
    band_index = lax.axis_index("band")
    bit_count = band_count.bit_length() - 1
    tail_width = TAIL_WIDTH

    def halves(own, partner, bit_index):
        upper_half = band_index // 2**bit_index % 2 == 1
        return jnp.where(upper_half, partner, own), jnp.where(upper_half, own, partner)

    def finish_tail(pending):
        own_tail, partner_tail, lower_edge, upper_edge, amounts, bit_index = pending
        lower_tail, upper_tail = halves(own_tail, partner_tail, bit_index)
        lower_window = jnp.concatenate([lower_edge, lower_tail], axis=1)
        upper_window = jnp.concatenate([upper_edge, upper_tail], axis=1)
        return lower_window[:, :tail_width] + shift_rows(upper_window, amounts, tail_width)

    partner_head = from_partner(head, "band", 0)
    tail, partner_head = lax.optimization_barrier((tail, partner_head))
    pending = None
    for bit_index in range(bit_count):
        amounts = offsets[local_count + bit_index]
        lower_head, upper_head = halves(head, partner_head, bit_index)
        head_width = head.shape[1] - SHIFT
        new_head = lower_head[:, :head_width] + shift_rows(upper_head, amounts, head_width)
        if bit_index + 1 < bit_count:
            next_partner_head = from_partner(new_head, "band", bit_index + 1)
        if pending is not None:
            waiting, ordered_head = lax.optimization_barrier((pending[1], new_head))
            tail = finish_tail(pending[:1] + (waiting,) + pending[2:])
        partner_tail = from_partner(tail, "band", bit_index)
        if bit_index + 1 < bit_count:
            partner_tail, next_partner_head = lax.optimization_barrier((partner_tail, next_partner_head))
            partner_head = next_partner_head
        pending = (tail, partner_tail, lower_head[:, head_width:], upper_head[:, head_width:], amounts, bit_index)
        head = new_head
    tail = finish_tail(pending)
    scale = 1.0 / math.sqrt(channels_all)
    head_scaled = head * scale
    head_detection = boxcar_max(head_scaled, widths)
    tail_scaled = jnp.concatenate([head_scaled[:, -TAPS:], tail * scale], axis=1)
    detection = jnp.concatenate([head_detection, boxcar_max(tail_scaled, widths)], axis=1)
    peak_series = butterfly(jnp.max(detection, axis=0), "band", jnp.maximum)
    return (detection, peak_series)


def solution(mesh):
    placed = (P(("beam", "band"), None), P(None, "band"), P())
    return jax.shard_map(
        per_device,
        mesh=mesh,
        in_specs=placed,
        out_specs=(P(("beam", "band"), None), P("beam")),
        check_vma=False,
    )
```

```python
import functools
import math

import jax
import jax.numpy as jnp
from jax import lax
from jax.experimental import pallas as pl
from jax.experimental.pallas import tpu as pltpu
from jax.sharding import PartitionSpec as P

TS = 2048
TIN = 6144
SHIFT = 256
TAPS = 128
TEMPLATES = 8
TAIL_WIDTH = 1152


def from_partner(value, axis, distance):
    mask = 2**distance
    pairs = [(source, source ^ mask) for source in range(lax.axis_size(axis))]
    return lax.ppermute(value, axis, pairs)


def from_xor(value, axis, mask):
    pairs = [(source, source ^ mask) for source in range(lax.axis_size(axis))]
    return lax.ppermute(value, axis, pairs)


def butterfly_terms(value, axis, combine):
    bit_count = lax.axis_size(axis).bit_length() - 1
    low_bit = 0
    received = [value]
    while low_bit < bit_count:
        while len(received) > 1:
            received = [combine(received[i], received[i + 1]) for i in range(0, len(received), 2)]
        value = received[0]
        width = min(2, bit_count - low_bit)
        received = [value] + [from_xor(value, axis, k << low_bit) for k in range(1, 2**width)]
        low_bit += width
    return received


def combine_terms(terms, combine):
    while len(terms) > 1:
        terms = [combine(terms[i], terms[i + 1]) for i in range(0, len(terms), 2)]
    return terms[0]


def butterfly(value, axis, combine):
    return combine_terms(butterfly_terms(value, axis, combine), combine)


def shift_rows(trial_rows, amounts, length):
    current = jnp.pad(trial_rows, ((0, 0), (0, 2 * SHIFT)))
    top_bit = (SHIFT - 1).bit_length()
    for bit_index in reversed(range(top_bit)):
        span = 2**bit_index
        keep_len = length + span - 1
        chosen = (amounts >> bit_index & 1)[:, None] == 1
        current = jnp.where(chosen, current[:, span : span + keep_len], current[:, :keep_len])
    return current


def local_tree_kernel(widths_seq, channels_all, term_count, x_ref, *refs):
    term_refs = refs[:term_count]
    offsets_ref, head_ref, tail_ref = refs[term_count:]
    rows = x_ref.shape[0]
    total = combine_terms([ref[:, : widths_seq[0]] for ref in term_refs], jnp.add)
    cur = x_ref[:, : widths_seq[0]] - total / channels_all
    row_id = lax.broadcasted_iota(jnp.int32, (rows, 1), 0)
    diagonal = lax.broadcasted_iota(jnp.int32, (rows, rows), 0) == lax.broadcasted_iota(
        jnp.int32, (rows, rows), 1
    )
    for section_index in range(len(widths_seq) - 1):
        mask = 2**section_index
        width = widths_seq[section_index]
        new_width = widths_seq[section_index + 1]
        is_upper = (row_id & mask) != 0
        from_below = pltpu.roll(cur, rows - mask, axis=0)
        from_above = pltpu.roll(cur, mask, axis=0)
        partner = jnp.where(is_upper, from_above, from_below)
        lower = jnp.where(is_upper, partner, cur)
        shifted = jnp.where(is_upper, cur, partner)
        amount_row = jnp.broadcast_to(offsets_ref[section_index : section_index + 1, :], (rows, rows))
        amount = jnp.sum(jnp.where(diagonal, amount_row, 0), axis=1, keepdims=True)
        for bit_index in range((SHIFT - 1).bit_length()):
            span = 2**bit_index
            chosen = (amount >> bit_index & 1) == 1
            shifted = jnp.where(chosen, pltpu.roll(shifted, width - span, axis=1), shifted)
        cur = lower[:, :new_width] + shifted[:, :new_width]
    head_width = head_ref.shape[1]
    head_ref[...] = cur[:, :head_width]
    tail_ref[...] = cur[:, head_width:]


def local_tree(filterbank, total_terms, offsets, widths_seq, channels_all, tail_width):
    rows = filterbank.shape[0]
    vmem = pl.BlockSpec(memory_space=pltpu.VMEM)
    work = rows * sum(widths_seq[:-1])
    head_width = widths_seq[-1] - tail_width
    return pl.pallas_call(
        functools.partial(local_tree_kernel, tuple(widths_seq), float(channels_all), len(total_terms)),
        out_shape=(
            pltpu.VMEM((rows, head_width), jnp.float32),
            pltpu.VMEM((rows, tail_width), jnp.float32),
        ),
        in_specs=[vmem] * (len(total_terms) + 2),
        out_specs=(vmem, vmem),
        cost_estimate=pl.CostEstimate(
            flops=40 * work, transcendentals=0, bytes_accessed=4 * (rows * widths_seq[0] + rows * widths_seq[-1])
        ),
    )(filterbank, *total_terms, offsets)


def merge_section(current, offsets_now, section_index, new_length):
    group_trials = 2**section_index
    total_rows = current.shape[0]
    groups = total_rows // (2 * group_trials)
    blocks = current.reshape(groups, 2, group_trials, current.shape[1])
    lower_part = blocks[:, 0, :, :new_length]
    upper_flat = blocks[:, 1].reshape(groups * group_trials, current.shape[1])
    amounts = offsets_now.reshape(groups, 2, group_trials)
    first_half = lower_part + shift_rows(upper_flat, amounts[:, 0].reshape(-1), new_length).reshape(
        groups, group_trials, new_length
    )
    second_half = lower_part + shift_rows(
        upper_flat, amounts[:, 1].reshape(-1), new_length
    ).reshape(groups, group_trials, new_length)
    return jnp.stack([first_half, second_half], axis=1).reshape(total_rows, new_length)


def template_tables(widths):
    source = lax.broadcasted_iota(jnp.int32, (2 * TAPS, TAPS), 0)
    target = lax.broadcasted_iota(jnp.int32, (2 * TAPS, TAPS), 1)
    tap_offset = source - target
    inside = (tap_offset[None] >= 0) & (tap_offset[None] < widths[:, None, None])
    tap_scale = 1.0 / jnp.sqrt(widths.astype(jnp.float32))
    return jnp.where(inside, tap_scale[:, None, None], jnp.zeros((), jnp.float32))


def boxcar_max(dedispersed, widths):
    total_rows = dedispersed.shape[0]
    blocks_time = TS // TAPS
    window = dedispersed.reshape(total_rows, blocks_time + 1, TAPS)
    paired = jnp.concatenate([window[:, :-1], window[:, 1:]], axis=2).reshape(
        total_rows * blocks_time, 2 * TAPS
    )
    tables = template_tables(widths)
    joined = jnp.transpose(tables, (1, 0, 2)).reshape(2 * TAPS, TEMPLATES * TAPS)
    result = jnp.dot(
        paired,
        joined,
        precision=lax.Precision.HIGH,
        preferred_element_type=jnp.float32,
    )
    best_value = jnp.max(result.reshape(total_rows * blocks_time, TEMPLATES, TAPS), axis=1)
    return best_value.reshape(total_rows, TS)


def per_device(filterbank, offsets, widths):
    levels = offsets.shape[0]
    local_count = filterbank.shape[0].bit_length() - 1
    band_count = lax.axis_size("band")
    channels_all = filterbank.shape[0] * band_count

    def length_after(sections_done):
        needed = TS + TAPS + (levels - sections_done) * (SHIFT - 1)
        needed = -(-needed // 128) * 128
        return min(TIN, needed)

    partial_value = jnp.sum(filterbank[:, : length_after(0)], axis=0, keepdims=True)
    total_terms = butterfly_terms(partial_value, "band", jnp.add)
    widths_seq = [length_after(section) for section in range(local_count + 1)]
    head, tail = local_tree(filterbank, total_terms, offsets, widths_seq, channels_all, TAIL_WIDTH)
    band_index = lax.axis_index("band")
    bit_count = band_count.bit_length() - 1
    tail_width = TAIL_WIDTH

    def halves(own, partner, bit_index):
        upper_half = band_index // 2**bit_index % 2 == 1
        return jnp.where(upper_half, partner, own), jnp.where(upper_half, own, partner)

    def finish_tail(pending):
        own_tail, partner_tail, lower_edge, upper_edge, amounts, bit_index = pending
        lower_tail, upper_tail = halves(own_tail, partner_tail, bit_index)
        lower_window = jnp.concatenate([lower_edge, lower_tail], axis=1)
        upper_window = jnp.concatenate([upper_edge, upper_tail], axis=1)
        return lower_window[:, :tail_width] + shift_rows(upper_window, amounts, tail_width)

    partner_head = from_partner(head, "band", 0)
    tail, partner_head = lax.optimization_barrier((tail, partner_head))
    pending = None
    for bit_index in range(bit_count):
        amounts = offsets[local_count + bit_index]
        lower_head, upper_head = halves(head, partner_head, bit_index)
        head_width = head.shape[1] - SHIFT
        new_head = lower_head[:, :head_width] + shift_rows(upper_head, amounts, head_width)
        if bit_index + 1 < bit_count:
            next_partner_head = from_partner(new_head, "band", bit_index + 1)
        if pending is not None:
            waiting, ordered_head = lax.optimization_barrier((pending[1], new_head))
            tail = finish_tail(pending[:1] + (waiting,) + pending[2:])
        partner_tail = from_partner(tail, "band", bit_index)
        if bit_index + 1 < bit_count:
            partner_tail, next_partner_head = lax.optimization_barrier((partner_tail, next_partner_head))
            partner_head = next_partner_head
        pending = (tail, partner_tail, lower_head[:, head_width:], upper_head[:, head_width:], amounts, bit_index)
        head = new_head
    tail = finish_tail(pending)
    current = jnp.concatenate([head, tail], axis=1)
    dedispersed = current * (1.0 / math.sqrt(channels_all))
    detection = boxcar_max(dedispersed, widths)
    peak_series = butterfly(jnp.max(detection, axis=0), "band", jnp.maximum)
    return (detection, peak_series)


def solution(mesh):
    placed = (P(("beam", "band"), None), P(None, "band"), P())
    return jax.shard_map(
        per_device,
        mesh=mesh,
        in_specs=placed,
        out_specs=(P(("beam", "band"), None), P("beam")),
        check_vma=False,
    )
```

```python
import functools
import math

import jax
import jax.numpy as jnp
from jax import lax
from jax.experimental import pallas as pl
from jax.experimental.pallas import tpu as pltpu
from jax.sharding import PartitionSpec as P

TS = 2048
TIN = 6144
SHIFT = 256
TAPS = 128
TEMPLATES = 8
TAIL_WIDTH = 1152


def from_partner(value, axis, distance):
    mask = 2**distance
    pairs = [(source, source ^ mask) for source in range(lax.axis_size(axis))]
    return lax.ppermute(value, axis, pairs)


def from_xor(value, axis, mask):
    pairs = [(source, source ^ mask) for source in range(lax.axis_size(axis))]
    return lax.ppermute(value, axis, pairs)


def butterfly(value, axis, combine):
    bit_count = lax.axis_size(axis).bit_length() - 1
    low_bit = 0
    while low_bit < bit_count:
        width = min(2, bit_count - low_bit)
        received = [value] + [from_xor(value, axis, k << low_bit) for k in range(1, 2**width)]
        while len(received) > 1:
            received = [combine(received[i], received[i + 1]) for i in range(0, len(received), 2)]
        value = received[0]
        low_bit += width
    return value


def shift_rows(trial_rows, amounts, length):
    current = jnp.pad(trial_rows, ((0, 0), (0, 2 * SHIFT)))
    top_bit = (SHIFT - 1).bit_length()
    for bit_index in reversed(range(top_bit)):
        span = 2**bit_index
        keep_len = length + span - 1
        chosen = (amounts >> bit_index & 1)[:, None] == 1
        current = jnp.where(chosen, current[:, span : span + keep_len], current[:, :keep_len])
    return current


def local_tree_kernel(widths_seq, channels_all, x_ref, total_ref, offsets_ref, head_ref, tail_ref):
    rows = x_ref.shape[0]
    cur = x_ref[:, : widths_seq[0]] - total_ref[:, : widths_seq[0]] / channels_all
    row_id = lax.broadcasted_iota(jnp.int32, (rows, 1), 0)
    diagonal = lax.broadcasted_iota(jnp.int32, (rows, rows), 0) == lax.broadcasted_iota(
        jnp.int32, (rows, rows), 1
    )
    for section_index in range(len(widths_seq) - 1):
        mask = 2**section_index
        width = widths_seq[section_index]
        new_width = widths_seq[section_index + 1]
        is_upper = (row_id & mask) != 0
        from_below = pltpu.roll(cur, rows - mask, axis=0)
        from_above = pltpu.roll(cur, mask, axis=0)
        partner = jnp.where(is_upper, from_above, from_below)
        lower = jnp.where(is_upper, partner, cur)
        shifted = jnp.where(is_upper, cur, partner)
        amount_row = jnp.broadcast_to(offsets_ref[section_index : section_index + 1, :], (rows, rows))
        amount = jnp.sum(jnp.where(diagonal, amount_row, 0), axis=1, keepdims=True)
        for bit_index in range((SHIFT - 1).bit_length()):
            span = 2**bit_index
            chosen = (amount >> bit_index & 1) == 1
            shifted = jnp.where(chosen, pltpu.roll(shifted, width - span, axis=1), shifted)
        cur = lower[:, :new_width] + shifted[:, :new_width]
    head_width = head_ref.shape[1]
    head_ref[...] = cur[:, :head_width]
    tail_ref[...] = cur[:, head_width:]


def local_tree(filterbank, channel_total, offsets, widths_seq, channels_all, tail_width):
    rows = filterbank.shape[0]
    vmem = pl.BlockSpec(memory_space=pltpu.VMEM)
    work = rows * sum(widths_seq[:-1])
    head_width = widths_seq[-1] - tail_width
    return pl.pallas_call(
        functools.partial(local_tree_kernel, tuple(widths_seq), float(channels_all)),
        out_shape=(
            pltpu.VMEM((rows, head_width), jnp.float32),
            pltpu.VMEM((rows, tail_width), jnp.float32),
        ),
        in_specs=[vmem, vmem, vmem],
        out_specs=(vmem, vmem),
        cost_estimate=pl.CostEstimate(
            flops=40 * work, transcendentals=0, bytes_accessed=4 * (rows * widths_seq[0] + rows * widths_seq[-1])
        ),
    )(filterbank, channel_total, offsets)


def merge_section(current, offsets_now, section_index, new_length):
    group_trials = 2**section_index
    total_rows = current.shape[0]
    groups = total_rows // (2 * group_trials)
    blocks = current.reshape(groups, 2, group_trials, current.shape[1])
    lower_part = blocks[:, 0, :, :new_length]
    upper_flat = blocks[:, 1].reshape(groups * group_trials, current.shape[1])
    amounts = offsets_now.reshape(groups, 2, group_trials)
    first_half = lower_part + shift_rows(upper_flat, amounts[:, 0].reshape(-1), new_length).reshape(
        groups, group_trials, new_length
    )
    second_half = lower_part + shift_rows(
        upper_flat, amounts[:, 1].reshape(-1), new_length
    ).reshape(groups, group_trials, new_length)
    return jnp.stack([first_half, second_half], axis=1).reshape(total_rows, new_length)


def template_tables(widths):
    source = lax.broadcasted_iota(jnp.int32, (2 * TAPS, TAPS), 0)
    target = lax.broadcasted_iota(jnp.int32, (2 * TAPS, TAPS), 1)
    tap_offset = source - target
    inside = (tap_offset[None] >= 0) & (tap_offset[None] < widths[:, None, None])
    tap_scale = 1.0 / jnp.sqrt(widths.astype(jnp.float32))
    return jnp.where(inside, tap_scale[:, None, None], jnp.zeros((), jnp.float32))


def boxcar_max(dedispersed, widths):
    total_rows = dedispersed.shape[0]
    blocks_time = TS // TAPS
    window = dedispersed.reshape(total_rows, blocks_time + 1, TAPS)
    paired = jnp.concatenate([window[:, :-1], window[:, 1:]], axis=2).reshape(
        total_rows * blocks_time, 2 * TAPS
    )
    tables = template_tables(widths)
    joined = jnp.transpose(tables, (1, 0, 2)).reshape(2 * TAPS, TEMPLATES * TAPS)
    result = jnp.dot(
        paired,
        joined,
        precision=lax.Precision.HIGH,
        preferred_element_type=jnp.float32,
    )
    best_value = jnp.max(result.reshape(total_rows * blocks_time, TEMPLATES, TAPS), axis=1)
    return best_value.reshape(total_rows, TS)


def per_device(filterbank, offsets, widths):
    levels = offsets.shape[0]
    local_count = filterbank.shape[0].bit_length() - 1
    band_count = lax.axis_size("band")
    channels_all = filterbank.shape[0] * band_count

    def length_after(sections_done):
        needed = TS + TAPS + (levels - sections_done) * (SHIFT - 1)
        needed = -(-needed // 128) * 128
        return min(TIN, needed)

    partial_value = jnp.sum(filterbank[:, : length_after(0)], axis=0, keepdims=True)
    channel_total = butterfly(partial_value, "band", jnp.add)
    widths_seq = [length_after(section) for section in range(local_count + 1)]
    head, tail = local_tree(filterbank, channel_total, offsets, widths_seq, channels_all, TAIL_WIDTH)
    band_index = lax.axis_index("band")
    bit_count = band_count.bit_length() - 1
    tail_width = TAIL_WIDTH

    def halves(own, partner, bit_index):
        upper_half = band_index // 2**bit_index % 2 == 1
        return jnp.where(upper_half, partner, own), jnp.where(upper_half, own, partner)

    def finish_tail(pending):
        own_tail, partner_tail, lower_edge, upper_edge, amounts, bit_index = pending
        lower_tail, upper_tail = halves(own_tail, partner_tail, bit_index)
        lower_window = jnp.concatenate([lower_edge, lower_tail], axis=1)
        upper_window = jnp.concatenate([upper_edge, upper_tail], axis=1)
        return lower_window[:, :tail_width] + shift_rows(upper_window, amounts, tail_width)

    partner_head = from_partner(head, "band", 0)
    tail, partner_head = lax.optimization_barrier((tail, partner_head))
    pending = None
    for bit_index in range(bit_count):
        amounts = offsets[local_count + bit_index]
        lower_head, upper_head = halves(head, partner_head, bit_index)
        head_width = head.shape[1] - SHIFT
        new_head = lower_head[:, :head_width] + shift_rows(upper_head, amounts, head_width)
        if bit_index + 1 < bit_count:
            next_partner_head = from_partner(new_head, "band", bit_index + 1)
        if pending is not None:
            waiting, ordered_head = lax.optimization_barrier((pending[1], new_head))
            tail = finish_tail(pending[:1] + (waiting,) + pending[2:])
        partner_tail = from_partner(tail, "band", bit_index)
        if bit_index + 1 < bit_count:
            partner_tail, next_partner_head = lax.optimization_barrier((partner_tail, next_partner_head))
            partner_head = next_partner_head
        pending = (tail, partner_tail, lower_head[:, head_width:], upper_head[:, head_width:], amounts, bit_index)
        head = new_head
    tail = finish_tail(pending)
    current = jnp.concatenate([head, tail], axis=1)
    dedispersed = current * (1.0 / math.sqrt(channels_all))
    detection = boxcar_max(dedispersed, widths)
    peak_series = butterfly(jnp.max(detection, axis=0), "band", jnp.maximum)
    return (detection, peak_series)


def solution(mesh):
    placed = (P(("beam", "band"), None), P(None, "band"), P())
    return jax.shard_map(
        per_device,
        mesh=mesh,
        in_specs=placed,
        out_specs=(P(("beam", "band"), None), P("beam")),
        check_vma=False,
    )
```

```python
import functools
import math

import jax
import jax.numpy as jnp
from jax import lax
from jax.experimental import pallas as pl
from jax.experimental.pallas import tpu as pltpu
from jax.sharding import PartitionSpec as P

TS = 2048
TIN = 6144
SHIFT = 256
TAPS = 128
TEMPLATES = 8
TAIL_WIDTH = 1152


def from_partner(value, axis, distance):
    mask = 2**distance
    pairs = [(source, source ^ mask) for source in range(lax.axis_size(axis))]
    return lax.ppermute(value, axis, pairs)


def from_xor(value, axis, mask):
    pairs = [(source, source ^ mask) for source in range(lax.axis_size(axis))]
    return lax.ppermute(value, axis, pairs)


def butterfly(value, axis, combine):
    bit_count = lax.axis_size(axis).bit_length() - 1
    low_bit = 0
    while low_bit < bit_count:
        width = min(2, bit_count - low_bit)
        received = [value] + [from_xor(value, axis, k << low_bit) for k in range(1, 2**width)]
        while len(received) > 1:
            received = [combine(received[i], received[i + 1]) for i in range(0, len(received), 2)]
        value = received[0]
        low_bit += width
    return value


def shift_rows(trial_rows, amounts, length):
    current = jnp.pad(trial_rows, ((0, 0), (0, 2 * SHIFT)))
    top_bit = (SHIFT - 1).bit_length()
    for bit_index in reversed(range(top_bit)):
        span = 2**bit_index
        keep_len = length + span - 1
        chosen = (amounts >> bit_index & 1)[:, None] == 1
        current = jnp.where(chosen, current[:, span : span + keep_len], current[:, :keep_len])
    return current


def local_tree_kernel(widths_seq, channels_all, x_ref, total_ref, offsets_ref, head_ref, tail_ref):
    rows = x_ref.shape[0]
    cur = x_ref[:, : widths_seq[0]] - total_ref[:, : widths_seq[0]] / channels_all
    row_id = lax.broadcasted_iota(jnp.int32, (rows, 1), 0)
    diagonal = lax.broadcasted_iota(jnp.int32, (rows, rows), 0) == lax.broadcasted_iota(
        jnp.int32, (rows, rows), 1
    )
    for section_index in range(len(widths_seq) - 1):
        mask = 2**section_index
        width = widths_seq[section_index]
        new_width = widths_seq[section_index + 1]
        is_upper = (row_id & mask) != 0
        from_below = pltpu.roll(cur, rows - mask, axis=0)
        from_above = pltpu.roll(cur, mask, axis=0)
        partner = jnp.where(is_upper, from_above, from_below)
        lower = jnp.where(is_upper, partner, cur)
        shifted = jnp.where(is_upper, cur, partner)
        amount_row = jnp.broadcast_to(offsets_ref[section_index : section_index + 1, :], (rows, rows))
        amount = jnp.sum(jnp.where(diagonal, amount_row, 0), axis=1, keepdims=True)
        for bit_index in range((SHIFT - 1).bit_length()):
            span = 2**bit_index
            chosen = (amount >> bit_index & 1) == 1
            shifted = jnp.where(chosen, pltpu.roll(shifted, width - span, axis=1), shifted)
        cur = lower[:, :new_width] + shifted[:, :new_width]
    head_width = head_ref.shape[1]
    head_ref[...] = cur[:, :head_width]
    tail_ref[...] = cur[:, head_width:]


def local_tree(filterbank, channel_total, offsets, widths_seq, channels_all, tail_width):
    rows = filterbank.shape[0]
    vmem = pl.BlockSpec(memory_space=pltpu.VMEM)
    work = rows * sum(widths_seq[:-1])
    head_width = widths_seq[-1] - tail_width
    return pl.pallas_call(
        functools.partial(local_tree_kernel, tuple(widths_seq), float(channels_all)),
        out_shape=(
            pltpu.VMEM((rows, head_width), jnp.float32),
            pltpu.VMEM((rows, tail_width), jnp.float32),
        ),
        in_specs=[vmem, vmem, vmem],
        out_specs=(vmem, vmem),
        cost_estimate=pl.CostEstimate(
            flops=40 * work, transcendentals=0, bytes_accessed=4 * (rows * widths_seq[0] + rows * widths_seq[-1])
        ),
    )(filterbank, channel_total, offsets)


def channel_sum_kernel(x_ref, out_ref):
    width = out_ref.shape[1]
    out_ref[...] = jnp.sum(x_ref[:, :width], axis=0, keepdims=True)


def channel_sum(filterbank, width):
    vmem = pl.BlockSpec(memory_space=pltpu.VMEM)
    return pl.pallas_call(
        channel_sum_kernel,
        out_shape=pltpu.VMEM((1, width), jnp.float32),
        in_specs=[vmem],
        out_specs=vmem,
        cost_estimate=pl.CostEstimate(
            flops=filterbank.shape[0] * width, transcendentals=0, bytes_accessed=4 * filterbank.shape[0] * width
        ),
    )(filterbank)


def merge_section(current, offsets_now, section_index, new_length):
    group_trials = 2**section_index
    total_rows = current.shape[0]
    groups = total_rows // (2 * group_trials)
    blocks = current.reshape(groups, 2, group_trials, current.shape[1])
    lower_part = blocks[:, 0, :, :new_length]
    upper_flat = blocks[:, 1].reshape(groups * group_trials, current.shape[1])
    amounts = offsets_now.reshape(groups, 2, group_trials)
    first_half = lower_part + shift_rows(upper_flat, amounts[:, 0].reshape(-1), new_length).reshape(
        groups, group_trials, new_length
    )
    second_half = lower_part + shift_rows(
        upper_flat, amounts[:, 1].reshape(-1), new_length
    ).reshape(groups, group_trials, new_length)
    return jnp.stack([first_half, second_half], axis=1).reshape(total_rows, new_length)


def template_tables(widths):
    source = lax.broadcasted_iota(jnp.int32, (2 * TAPS, TAPS), 0)
    target = lax.broadcasted_iota(jnp.int32, (2 * TAPS, TAPS), 1)
    tap_offset = source - target
    inside = (tap_offset[None] >= 0) & (tap_offset[None] < widths[:, None, None])
    tap_scale = 1.0 / jnp.sqrt(widths.astype(jnp.float32))
    return jnp.where(inside, tap_scale[:, None, None], jnp.zeros((), jnp.float32))


def boxcar_max(dedispersed, widths):
    total_rows = dedispersed.shape[0]
    blocks_time = TS // TAPS
    window = dedispersed.reshape(total_rows, blocks_time + 1, TAPS)
    paired = jnp.concatenate([window[:, :-1], window[:, 1:]], axis=2).reshape(
        total_rows * blocks_time, 2 * TAPS
    )
    tables = template_tables(widths)
    joined = jnp.transpose(tables, (1, 0, 2)).reshape(2 * TAPS, TEMPLATES * TAPS)
    result = jnp.dot(
        paired,
        joined,
        precision=lax.Precision.HIGH,
        preferred_element_type=jnp.float32,
    )
    best_value = jnp.max(result.reshape(total_rows * blocks_time, TEMPLATES, TAPS), axis=1)
    return best_value.reshape(total_rows, TS)


def per_device(filterbank, offsets, widths):
    levels = offsets.shape[0]
    local_count = filterbank.shape[0].bit_length() - 1
    band_count = lax.axis_size("band")
    channels_all = filterbank.shape[0] * band_count

    def length_after(sections_done):
        needed = TS + TAPS + (levels - sections_done) * (SHIFT - 1)
        needed = -(-needed // 128) * 128
        return min(TIN, needed)

    partial_value = channel_sum(filterbank, length_after(0))
    channel_total = butterfly(partial_value, "band", jnp.add)
    widths_seq = [length_after(section) for section in range(local_count + 1)]
    head, tail = local_tree(filterbank, channel_total, offsets, widths_seq, channels_all, TAIL_WIDTH)
    band_index = lax.axis_index("band")
    bit_count = band_count.bit_length() - 1
    tail_width = TAIL_WIDTH

    def halves(own, partner, bit_index):
        upper_half = band_index // 2**bit_index % 2 == 1
        return jnp.where(upper_half, partner, own), jnp.where(upper_half, own, partner)

    def finish_tail(pending):
        own_tail, partner_tail, lower_edge, upper_edge, amounts, bit_index = pending
        lower_tail, upper_tail = halves(own_tail, partner_tail, bit_index)
        lower_window = jnp.concatenate([lower_edge, lower_tail], axis=1)
        upper_window = jnp.concatenate([upper_edge, upper_tail], axis=1)
        return lower_window[:, :tail_width] + shift_rows(upper_window, amounts, tail_width)

    partner_head = from_partner(head, "band", 0)
    tail, partner_head = lax.optimization_barrier((tail, partner_head))
    pending = None
    for bit_index in range(bit_count):
        amounts = offsets[local_count + bit_index]
        lower_head, upper_head = halves(head, partner_head, bit_index)
        head_width = head.shape[1] - SHIFT
        new_head = lower_head[:, :head_width] + shift_rows(upper_head, amounts, head_width)
        if bit_index + 1 < bit_count:
            next_partner_head = from_partner(new_head, "band", bit_index + 1)
        if pending is not None:
            waiting, ordered_head = lax.optimization_barrier((pending[1], new_head))
            tail = finish_tail(pending[:1] + (waiting,) + pending[2:])
        partner_tail = from_partner(tail, "band", bit_index)
        if bit_index + 1 < bit_count:
            partner_tail, next_partner_head = lax.optimization_barrier((partner_tail, next_partner_head))
            partner_head = next_partner_head
        pending = (tail, partner_tail, lower_head[:, head_width:], upper_head[:, head_width:], amounts, bit_index)
        head = new_head
    tail = finish_tail(pending)
    current = jnp.concatenate([head, tail], axis=1)
    dedispersed = current * (1.0 / math.sqrt(channels_all))
    detection = boxcar_max(dedispersed, widths)
    peak_series = butterfly(jnp.max(detection, axis=0), "band", jnp.maximum)
    return (detection, peak_series)


def solution(mesh):
    placed = (P(("beam", "band"), None), P(None, "band"), P())
    return jax.shard_map(
        per_device,
        mesh=mesh,
        in_specs=placed,
        out_specs=(P(("beam", "band"), None), P("beam")),
        check_vma=False,
    )
```

```python
import functools
import math

import jax
import jax.numpy as jnp
from jax import lax
from jax.experimental import pallas as pl
from jax.experimental.pallas import tpu as pltpu
from jax.sharding import PartitionSpec as P

TS = 2048
TIN = 6144
SHIFT = 256
TAPS = 128
TEMPLATES = 8
TAIL_WIDTH = 1152


def from_partner(value, axis, distance):
    mask = 2**distance
    pairs = [(source, source ^ mask) for source in range(lax.axis_size(axis))]
    return lax.ppermute(value, axis, pairs)


def from_xor(value, axis, mask):
    pairs = [(source, source ^ mask) for source in range(lax.axis_size(axis))]
    return lax.ppermute(value, axis, pairs)


def butterfly(value, axis, combine):
    bit_count = lax.axis_size(axis).bit_length() - 1
    low_bit = 0
    while low_bit < bit_count:
        width = min(2, bit_count - low_bit)
        received = [value] + [from_xor(value, axis, k << low_bit) for k in range(1, 2**width)]
        while len(received) > 1:
            received = [combine(received[i], received[i + 1]) for i in range(0, len(received), 2)]
        value = received[0]
        low_bit += width
    return value


def shift_rows(trial_rows, amounts, length):
    current = jnp.pad(trial_rows, ((0, 0), (0, 2 * SHIFT)))
    top_bit = (SHIFT - 1).bit_length()
    for bit_index in reversed(range(top_bit)):
        span = 2**bit_index
        keep_len = length + span - 1
        chosen = (amounts >> bit_index & 1)[:, None] == 1
        current = jnp.where(chosen, current[:, span : span + keep_len], current[:, :keep_len])
    return current


def local_tree_kernel(widths_seq, channels_all, x_ref, total_ref, offsets_ref, head_ref, tail_ref):
    rows = x_ref.shape[0]
    cur = x_ref[:, : widths_seq[0]] - total_ref[:, : widths_seq[0]] / channels_all
    row_id = lax.broadcasted_iota(jnp.int32, (rows, 1), 0)
    diagonal = lax.broadcasted_iota(jnp.int32, (rows, rows), 0) == lax.broadcasted_iota(
        jnp.int32, (rows, rows), 1
    )
    for section_index in range(len(widths_seq) - 1):
        mask = 2**section_index
        width = widths_seq[section_index]
        new_width = widths_seq[section_index + 1]
        is_upper = (row_id & mask) != 0
        from_below = pltpu.roll(cur, rows - mask, axis=0)
        from_above = pltpu.roll(cur, mask, axis=0)
        partner = jnp.where(is_upper, from_above, from_below)
        lower = jnp.where(is_upper, partner, cur)
        shifted = jnp.where(is_upper, cur, partner)
        amount_row = jnp.broadcast_to(offsets_ref[section_index : section_index + 1, :], (rows, rows))
        amount = jnp.sum(jnp.where(diagonal, amount_row, 0), axis=1, keepdims=True)
        for bit_index in range((SHIFT - 1).bit_length()):
            span = 2**bit_index
            chosen = (amount >> bit_index & 1) == 1
            shifted = jnp.where(chosen, pltpu.roll(shifted, width - span, axis=1), shifted)
        cur = lower[:, :new_width] + shifted[:, :new_width]
    head_width = head_ref.shape[1]
    head_ref[...] = cur[:, :head_width]
    tail_ref[...] = cur[:, head_width:]


def local_tree(filterbank, channel_total, offsets, widths_seq, channels_all, tail_width):
    rows = filterbank.shape[0]
    vmem = pl.BlockSpec(memory_space=pltpu.VMEM)
    work = rows * sum(widths_seq[:-1])
    head_width = widths_seq[-1] - tail_width
    return pl.pallas_call(
        functools.partial(local_tree_kernel, tuple(widths_seq), float(channels_all)),
        out_shape=(
            pltpu.VMEM((rows, head_width), jnp.float32),
            pltpu.VMEM((rows, tail_width), jnp.float32),
        ),
        in_specs=[vmem, vmem, vmem],
        out_specs=(vmem, vmem),
        cost_estimate=pl.CostEstimate(
            flops=40 * work, transcendentals=0, bytes_accessed=4 * (rows * widths_seq[0] + rows * widths_seq[-1])
        ),
    )(filterbank, channel_total, offsets)


def merge_section(current, offsets_now, section_index, new_length):
    group_trials = 2**section_index
    total_rows = current.shape[0]
    groups = total_rows // (2 * group_trials)
    blocks = current.reshape(groups, 2, group_trials, current.shape[1])
    lower_part = blocks[:, 0, :, :new_length]
    upper_flat = blocks[:, 1].reshape(groups * group_trials, current.shape[1])
    amounts = offsets_now.reshape(groups, 2, group_trials)
    first_half = lower_part + shift_rows(upper_flat, amounts[:, 0].reshape(-1), new_length).reshape(
        groups, group_trials, new_length
    )
    second_half = lower_part + shift_rows(
        upper_flat, amounts[:, 1].reshape(-1), new_length
    ).reshape(groups, group_trials, new_length)
    return jnp.stack([first_half, second_half], axis=1).reshape(total_rows, new_length)


def template_tables(widths):
    source = lax.broadcasted_iota(jnp.int32, (2 * TAPS, TAPS), 0)
    target = lax.broadcasted_iota(jnp.int32, (2 * TAPS, TAPS), 1)
    tap_offset = source - target
    inside = (tap_offset[None] >= 0) & (tap_offset[None] < widths[:, None, None])
    tap_scale = 1.0 / jnp.sqrt(widths.astype(jnp.float32))
    return jnp.where(inside, tap_scale[:, None, None], jnp.zeros((), jnp.float32))


def boxcar_max(dedispersed, widths):
    total_rows = dedispersed.shape[0]
    blocks_time = dedispersed.shape[1] // TAPS - 1
    window = dedispersed.reshape(total_rows, blocks_time + 1, TAPS)
    paired = jnp.concatenate([window[:, :-1], window[:, 1:]], axis=2).reshape(
        total_rows * blocks_time, 2 * TAPS
    )
    tables = template_tables(widths)
    joined = jnp.transpose(tables, (1, 0, 2)).reshape(2 * TAPS, TEMPLATES * TAPS)
    result = jnp.dot(
        paired,
        joined,
        precision=lax.Precision.HIGH,
        preferred_element_type=jnp.float32,
    )
    best_value = jnp.max(result.reshape(total_rows * blocks_time, TEMPLATES, TAPS), axis=1)
    return best_value.reshape(total_rows, blocks_time * TAPS)


def per_device(filterbank, offsets, widths):
    levels = offsets.shape[0]
    local_count = filterbank.shape[0].bit_length() - 1
    band_count = lax.axis_size("band")
    channels_all = filterbank.shape[0] * band_count

    def length_after(sections_done):
        needed = TS + TAPS + (levels - sections_done) * (SHIFT - 1)
        needed = -(-needed // 128) * 128
        return min(TIN, needed)

    partial_value = jnp.sum(filterbank[:, : length_after(0)], axis=0, keepdims=True)
    channel_total = butterfly(partial_value, "band", jnp.add)
    widths_seq = [length_after(section) for section in range(local_count + 1)]
    head, tail = local_tree(filterbank, channel_total, offsets, widths_seq, channels_all, TAIL_WIDTH)
    band_index = lax.axis_index("band")
    bit_count = band_count.bit_length() - 1
    tail_width = TAIL_WIDTH

    def halves(own, partner, bit_index):
        upper_half = band_index // 2**bit_index % 2 == 1
        return jnp.where(upper_half, partner, own), jnp.where(upper_half, own, partner)

    def finish_tail(pending):
        own_tail, partner_tail, lower_edge, upper_edge, amounts, bit_index = pending
        lower_tail, upper_tail = halves(own_tail, partner_tail, bit_index)
        lower_window = jnp.concatenate([lower_edge, lower_tail], axis=1)
        upper_window = jnp.concatenate([upper_edge, upper_tail], axis=1)
        return lower_window[:, :tail_width] + shift_rows(upper_window, amounts, tail_width)

    partner_head = from_partner(head, "band", 0)
    tail, partner_head = lax.optimization_barrier((tail, partner_head))
    pending = None
    for bit_index in range(bit_count):
        amounts = offsets[local_count + bit_index]
        lower_head, upper_head = halves(head, partner_head, bit_index)
        head_width = head.shape[1] - SHIFT
        new_head = lower_head[:, :head_width] + shift_rows(upper_head, amounts, head_width)
        if bit_index + 1 < bit_count:
            next_partner_head = from_partner(new_head, "band", bit_index + 1)
        if pending is not None:
            waiting, ordered_head = lax.optimization_barrier((pending[1], new_head))
            tail = finish_tail(pending[:1] + (waiting,) + pending[2:])
        partner_tail = from_partner(tail, "band", bit_index)
        if bit_index + 1 < bit_count:
            partner_tail, next_partner_head = lax.optimization_barrier((partner_tail, next_partner_head))
            partner_head = next_partner_head
        pending = (tail, partner_tail, lower_head[:, head_width:], upper_head[:, head_width:], amounts, bit_index)
        head = new_head
    tail = finish_tail(pending)
    scale = 1.0 / math.sqrt(channels_all)
    head_scaled = head * scale
    head_detection = boxcar_max(head_scaled, widths)
    tail_scaled = jnp.concatenate([head_scaled[:, -TAPS:], tail * scale], axis=1)
    detection = jnp.concatenate([head_detection, boxcar_max(tail_scaled, widths)], axis=1)
    peak_series = butterfly(jnp.max(detection, axis=0), "band", jnp.maximum)
    return (detection, peak_series)


def solution(mesh):
    placed = (P(("beam", "band"), None), P(None, "band"), P())
    return jax.shard_map(
        per_device,
        mesh=mesh,
        in_specs=placed,
        out_specs=(P(("beam", "band"), None), P("beam")),
        check_vma=False,
    )
```

```python
import functools
import math

import jax
import jax.numpy as jnp
from jax import lax
from jax.experimental import pallas as pl
from jax.experimental.pallas import tpu as pltpu
from jax.sharding import PartitionSpec as P

TS = 2048
TIN = 6144
SHIFT = 256
TAPS = 128
TEMPLATES = 8
TAIL_WIDTH = 1152


def from_partner(value, axis, distance):
    mask = 2**distance
    pairs = [(source, source ^ mask) for source in range(lax.axis_size(axis))]
    return lax.ppermute(value, axis, pairs)


def from_xor(value, axis, mask):
    pairs = [(source, source ^ mask) for source in range(lax.axis_size(axis))]
    return lax.ppermute(value, axis, pairs)


def butterfly(value, axis, combine, late_pairwise=False):
    bit_count = lax.axis_size(axis).bit_length() - 1
    low_bit = 0
    while low_bit < bit_count:
        width = 1 if late_pairwise and low_bit >= 2 else min(2, bit_count - low_bit)
        received = [value] + [from_xor(value, axis, k << low_bit) for k in range(1, 2**width)]
        while len(received) > 1:
            received = [combine(received[i], received[i + 1]) for i in range(0, len(received), 2)]
        value = received[0]
        low_bit += width
    return value


def shift_rows(trial_rows, amounts, length):
    current = jnp.pad(trial_rows, ((0, 0), (0, 2 * SHIFT)))
    top_bit = (SHIFT - 1).bit_length()
    for bit_index in reversed(range(top_bit)):
        span = 2**bit_index
        keep_len = length + span - 1
        chosen = (amounts >> bit_index & 1)[:, None] == 1
        current = jnp.where(chosen, current[:, span : span + keep_len], current[:, :keep_len])
    return current


def local_tree_kernel(widths_seq, channels_all, x_ref, total_ref, offsets_ref, head_ref, tail_ref):
    rows = x_ref.shape[0]
    cur = x_ref[:, : widths_seq[0]] - total_ref[:, : widths_seq[0]] / channels_all
    row_id = lax.broadcasted_iota(jnp.int32, (rows, 1), 0)
    diagonal = lax.broadcasted_iota(jnp.int32, (rows, rows), 0) == lax.broadcasted_iota(
        jnp.int32, (rows, rows), 1
    )
    for section_index in range(len(widths_seq) - 1):
        mask = 2**section_index
        width = widths_seq[section_index]
        new_width = widths_seq[section_index + 1]
        is_upper = (row_id & mask) != 0
        from_below = pltpu.roll(cur, rows - mask, axis=0)
        from_above = pltpu.roll(cur, mask, axis=0)
        partner = jnp.where(is_upper, from_above, from_below)
        lower = jnp.where(is_upper, partner, cur)
        shifted = jnp.where(is_upper, cur, partner)
        amount_row = jnp.broadcast_to(offsets_ref[section_index : section_index + 1, :], (rows, rows))
        amount = jnp.sum(jnp.where(diagonal, amount_row, 0), axis=1, keepdims=True)
        for bit_index in range((SHIFT - 1).bit_length()):
            span = 2**bit_index
            chosen = (amount >> bit_index & 1) == 1
            shifted = jnp.where(chosen, pltpu.roll(shifted, width - span, axis=1), shifted)
        cur = lower[:, :new_width] + shifted[:, :new_width]
    head_width = head_ref.shape[1]
    head_ref[...] = cur[:, :head_width]
    tail_ref[...] = cur[:, head_width:]


def local_tree(filterbank, channel_total, offsets, widths_seq, channels_all, tail_width):
    rows = filterbank.shape[0]
    vmem = pl.BlockSpec(memory_space=pltpu.VMEM)
    work = rows * sum(widths_seq[:-1])
    head_width = widths_seq[-1] - tail_width
    return pl.pallas_call(
        functools.partial(local_tree_kernel, tuple(widths_seq), float(channels_all)),
        out_shape=(
            pltpu.VMEM((rows, head_width), jnp.float32),
            pltpu.VMEM((rows, tail_width), jnp.float32),
        ),
        in_specs=[vmem, vmem, vmem],
        out_specs=(vmem, vmem),
        cost_estimate=pl.CostEstimate(
            flops=40 * work, transcendentals=0, bytes_accessed=4 * (rows * widths_seq[0] + rows * widths_seq[-1])
        ),
    )(filterbank, channel_total, offsets)


def merge_section(current, offsets_now, section_index, new_length):
    group_trials = 2**section_index
    total_rows = current.shape[0]
    groups = total_rows // (2 * group_trials)
    blocks = current.reshape(groups, 2, group_trials, current.shape[1])
    lower_part = blocks[:, 0, :, :new_length]
    upper_flat = blocks[:, 1].reshape(groups * group_trials, current.shape[1])
    amounts = offsets_now.reshape(groups, 2, group_trials)
    first_half = lower_part + shift_rows(upper_flat, amounts[:, 0].reshape(-1), new_length).reshape(
        groups, group_trials, new_length
    )
    second_half = lower_part + shift_rows(
        upper_flat, amounts[:, 1].reshape(-1), new_length
    ).reshape(groups, group_trials, new_length)
    return jnp.stack([first_half, second_half], axis=1).reshape(total_rows, new_length)


def template_tables(widths):
    source = lax.broadcasted_iota(jnp.int32, (2 * TAPS, TAPS), 0)
    target = lax.broadcasted_iota(jnp.int32, (2 * TAPS, TAPS), 1)
    tap_offset = source - target
    inside = (tap_offset[None] >= 0) & (tap_offset[None] < widths[:, None, None])
    tap_scale = 1.0 / jnp.sqrt(widths.astype(jnp.float32))
    return jnp.where(inside, tap_scale[:, None, None], jnp.zeros((), jnp.float32))


def boxcar_max(dedispersed, widths):
    total_rows = dedispersed.shape[0]
    blocks_time = dedispersed.shape[1] // TAPS - 1
    window = dedispersed.reshape(total_rows, blocks_time + 1, TAPS)
    paired = jnp.concatenate([window[:, :-1], window[:, 1:]], axis=2).reshape(
        total_rows * blocks_time, 2 * TAPS
    )
    tables = template_tables(widths)
    joined = jnp.transpose(tables, (1, 0, 2)).reshape(2 * TAPS, TEMPLATES * TAPS)
    result = jnp.dot(
        paired,
        joined,
        precision=lax.Precision.HIGH,
        preferred_element_type=jnp.float32,
    )
    best_value = jnp.max(result.reshape(total_rows * blocks_time, TEMPLATES, TAPS), axis=1)
    return best_value.reshape(total_rows, blocks_time * TAPS)


def per_device(filterbank, offsets, widths):
    levels = offsets.shape[0]
    local_count = filterbank.shape[0].bit_length() - 1
    band_count = lax.axis_size("band")
    channels_all = filterbank.shape[0] * band_count

    def length_after(sections_done):
        needed = TS + TAPS + (levels - sections_done) * (SHIFT - 1)
        needed = -(-needed // 128) * 128
        return min(TIN, needed)

    partial_value = jnp.sum(filterbank[:, : length_after(0)], axis=0, keepdims=True)
    channel_total = butterfly(partial_value, "band", jnp.add)
    widths_seq = [length_after(section) for section in range(local_count + 1)]
    head, tail = local_tree(filterbank, channel_total, offsets, widths_seq, channels_all, TAIL_WIDTH)
    band_index = lax.axis_index("band")
    bit_count = band_count.bit_length() - 1
    tail_width = TAIL_WIDTH

    def halves(own, partner, bit_index):
        upper_half = band_index // 2**bit_index % 2 == 1
        return jnp.where(upper_half, partner, own), jnp.where(upper_half, own, partner)

    def finish_tail(pending):
        own_tail, partner_tail, lower_edge, upper_edge, amounts, bit_index = pending
        lower_tail, upper_tail = halves(own_tail, partner_tail, bit_index)
        lower_window = jnp.concatenate([lower_edge, lower_tail], axis=1)
        upper_window = jnp.concatenate([upper_edge, upper_tail], axis=1)
        return lower_window[:, :tail_width] + shift_rows(upper_window, amounts, tail_width)

    partner_head = from_partner(head, "band", 0)
    tail, partner_head = lax.optimization_barrier((tail, partner_head))
    pending = None
    for bit_index in range(bit_count):
        amounts = offsets[local_count + bit_index]
        lower_head, upper_head = halves(head, partner_head, bit_index)
        head_width = head.shape[1] - SHIFT
        new_head = lower_head[:, :head_width] + shift_rows(upper_head, amounts, head_width)
        if bit_index + 1 < bit_count:
            next_partner_head = from_partner(new_head, "band", bit_index + 1)
        if pending is not None:
            waiting, ordered_head = lax.optimization_barrier((pending[1], new_head))
            tail = finish_tail(pending[:1] + (waiting,) + pending[2:])
        partner_tail = from_partner(tail, "band", bit_index)
        if bit_index + 1 < bit_count:
            partner_tail, next_partner_head = lax.optimization_barrier((partner_tail, next_partner_head))
            partner_head = next_partner_head
        pending = (tail, partner_tail, lower_head[:, head_width:], upper_head[:, head_width:], amounts, bit_index)
        head = new_head
    tail = finish_tail(pending)
    scale = 1.0 / math.sqrt(channels_all)
    head_scaled = head * scale
    head_detection = boxcar_max(head_scaled, widths)
    tail_scaled = jnp.concatenate([head_scaled[:, -TAPS:], tail * scale], axis=1)
    detection = jnp.concatenate([head_detection, boxcar_max(tail_scaled, widths)], axis=1)
    peak_series = butterfly(jnp.max(detection, axis=0), "band", jnp.maximum, late_pairwise=True)
    return (detection, peak_series)


def solution(mesh):
    placed = (P(("beam", "band"), None), P(None, "band"), P())
    return jax.shard_map(
        per_device,
        mesh=mesh,
        in_specs=placed,
        out_specs=(P(("beam", "band"), None), P("beam")),
        check_vma=False,
    )
```
